128 devices in a mesh: seq: 32 (over y, z, core), tp: 4 (over x).
Axes of the slice: x: 4, y: 4, z: 4, core: 2. Of those that a mesh axis runs over, the one named last changes fastest.
Arguments:
- residual: bfloat16 [8192, 3584], P(('seq', 'tp')), may hold values from -6 to 6
- x_in: bfloat16 [8192, 3584], P('seq', 'tp'), may hold values from -6 to 6
- z_in: bfloat16 [8192, 3584], P('seq', 'tp'), may hold values from -6 to 6
- bc_in: bfloat16 [8192, 128], P('seq'), may hold values from -1.5 to 1.5
- dt_in: float32 [8192, 56], P('seq', 'tp'), may hold values from -6 to 6
- conv_x_weight: float32 [4, 3584], P(None, 'tp'), may hold values from -3 to 3
- conv_bc_weight: float32 [4, 128], replicated, may hold values from -3 to 3
- conv_x_cache: bfloat16 [16, 3, 3584], P(None, None, 'tp'), may hold values from -6 to 6
- conv_bc_cache: bfloat16 [16, 3, 128], replicated, may hold values from -1.5 to 1.5
- ssm_cache: float32 [16, 56, 64, 64], P(None, 'tp'), may hold values from -12 to 12
- dt_bias: float32 [56], P('tp'), may hold values from -1 to 1
- a_log: float32 [56], P('tp'), may hold values from -9 to -3.5
- d_skip: float32 [56], P('tp'), may hold values from 0.5 to 1.5
- norm_gain: float32 [3584], P('tp'), may hold values from 0.5 to 1.5
- out_weight: bfloat16 [3584, 3584], P('tp'), may hold values from -0.09375 to 0.09375
- attn_gain: float32 [3584], replicated, may hold values from 0.5 to 1.5
- q_weight: bfloat16 [3584, 3584], P(None, 'tp'), may hold values from -1 to 1
- q_down: bfloat16 [3584, 128], replicated, may hold values from -0.09375 to 0.09375
- q_up: bfloat16 [128, 3584], P(None, 'tp'), may hold values from -0.5 to 0.5
- cache_keys: bfloat16 [8192, 3584], P('seq', 'tp'), may hold values from -6 to 6
- cache_values: bfloat16 [8192, 3584], P('seq', 'tp'), may hold values from -6 to 6
- new_keys: bfloat16 [8192, 3584], P('seq', 'tp'), may hold values from -6 to 6
- new_values: bfloat16 [8192, 3584], P('seq', 'tp'), may hold values from -6 to 6
- lengths: int32 [16], replicated, may hold values from 1 to 2304, 8192 in all
Outputs:
- hidden: bfloat16 [8192, 3584], P(('seq', 'tp'))
- attended: bfloat16 [8192, 3584], P('seq', 'tp')
The draws below stay inside these ranges and needn't reach their ends.
Inputs may be any that keep to these rules, and one draw needn't show every extreme that they name: lengths of the prompts' second halves sum to 8192; the largest is 2304.
All inputs are finite; a program needn't handle non-finite values.
Results may differ from the reference program's by a relative error of at most 0.014.
Values may be sent and summed in bfloat16 or wider, within the bound.
No kernel may reach another device: no remote copies, remote signals or barrier semaphores. Data moves between devices by JAX's collectives and lax.ppermute only.
A program may use at most 192 MiB of HBM per device.

```python
import math
import jax
import jax.numpy as jnp
import numpy as np
from jax import lax

D = 3584
MH = 56
HD = 64
N = 64
KW = 4
INNER = 3584
AH = 16
HA = 224
QW = 3584
RANK = 128
TOK_DEV = 256
REACH = 9
HALF_MAX = 2304
TOKENS = 8192
PROMPTS = 16


def draw_residual(key, part):
    noise = jax.random.normal(jax.random.fold_in(key, 7002), (TOKENS, D), jnp.float32)
    values = noise
    return jnp.clip(values, -6.0, 6.0).astype(jnp.bfloat16)


def draw_q_weight(key, part):
    noise = jnp.clip(jax.random.normal(jax.random.fold_in(key, 7003), (D, QW), jnp.float32), -6.0, 6.0) / D ** 0.5
    values = noise
    return jnp.clip(values, -1.0, 1.0).astype(jnp.bfloat16)


def draw_cache_keys(key, part):
    noise = jnp.clip(jax.random.normal(jax.random.fold_in(key, 7004), (TOKENS, QW), jnp.float32), -6.0, 6.0)
    values = noise
    return values.astype(jnp.bfloat16)


def shard_levels(key, shape, cuts, least, high):
    level = 1.0
    for dim, shards_of in cuts:
        heights = jax.random.uniform(jax.random.fold_in(jax.random.fold_in(key, 6), dim), (shards_of,), jnp.float32, least / len(cuts), high / len(cuts))
        level = level * jnp.repeat(jnp.exp(heights), shape[dim] // shards_of).reshape((-1,) + (1,) * (len(shape) - 1 - dim))
    return level


def split_up(amount, total, most, skew):
    weights = [(1 << 20) // math.isqrt(standing ** skew) + 1 for standing in range(2, amount + 1)]
    surplus, holding = total - most - (amount - 1), [1] * (amount - 1)
    while surplus > 0:
        free = [i for i in range(amount - 1) if holding[i] < most]
        mass, left = sum([weights[i] for i in free]), surplus
        for i in free:
            extra = min(most - holding[i], max(1, left * weights[i] // mass), surplus)
            holding[i] = holding[i] + extra
            surplus = surplus - extra
    return np.array([most] + holding)


def ragged_sizes(key, amount, total, bound, skew):
    if amount == 2:
        one = jax.random.randint(key, (), max(1, total - bound), min(bound, total - 1) + 1)
        return jnp.stack([one, total - one])
    sizes = jnp.asarray(split_up(amount, total, bound, skew), jnp.int32)
    twos = (amount - 1) // 2
    source_of, taker = sizes[1:1 + 2 * twos:2], sizes[2:2 + 2 * twos:2]
    slack = jnp.minimum(source_of - 1, bound - taker)
    moved = jax.random.randint(jax.random.fold_in(key, 1), (twos,), 0, 1 << 20) % (slack + 1)
    sizes = sizes.at[1:1 + 2 * twos:2].set(source_of - moved).at[2:2 + 2 * twos:2].set(taker + moved)
    return sizes[jax.random.permutation(jax.random.fold_in(key, 2), amount)]


def bell_draw(key, dims, scale, most, cuts=(), held_as=jnp.bfloat16):
    loudness = shard_levels(key, dims, cuts, -0.22, 0.18) if cuts else 1.0
    drawn = jax.random.normal(key, dims, jnp.float32) * scale * loudness
    return jnp.minimum(jnp.maximum(drawn, -most), most).astype(held_as)


def setup_inputs(seed: int = 0) -> dict:
    key_of = jax.random.split(jax.random.key(seed), 25)
    residual = draw_residual(jax.random.fold_in(key_of[24], 71), 0)
    x_in = bell_draw(key_of[1], (TOKENS, INNER), 1.0, 6.0, ((0, 32), (1, 4)))
    z_in = bell_draw(key_of[2], (TOKENS, INNER), 1.0, 6.0, ((0, 32), (1, 4)))
    bc_in = bell_draw(key_of[3], (TOKENS, 2 * N), 0.25, 1.5, ((0, 32),))
    dt_in = bell_draw(key_of[4], (TOKENS, MH), 1.0, 6.0, ((0, 32), (1, 4)), jnp.float32)
    conv_x_weight = bell_draw(key_of[5], (KW, INNER), 0.5, 3.0, ((1, 4),), jnp.float32)
    conv_bc_weight = bell_draw(key_of[6], (KW, 2 * N), 0.5, 3.0, (), jnp.float32)
    conv_x_cache = bell_draw(key_of[7], (PROMPTS, KW - 1, INNER), 1.0, 6.0, ((2, 4),))
    conv_bc_cache = bell_draw(key_of[8], (PROMPTS, KW - 1, 2 * N), 0.25, 1.5)
    ssm_cache = bell_draw(key_of[9], (PROMPTS, MH, HD, N), 2.0, 12.0, ((1, 4),), jnp.float32)
    dt_bias = jnp.clip(jax.random.uniform(key_of[10], (MH,), jnp.float32, -1.0, 1.0) * shard_levels(key_of[10], (MH,), ((0, 4),), -0.4, 0.0), -1.0, 1.0)
    a_log = jnp.clip(-9.0 + 5.5 * jax.random.uniform(key_of[11], (MH,), jnp.float32) ** shard_levels(key_of[11], (MH,), ((0, 4),), -0.2, 0.2), -9.0, -3.5)
    d_skip = jnp.clip(0.5 + 1.0 * jax.random.uniform(key_of[12], (MH,), jnp.float32) ** shard_levels(key_of[12], (MH,), ((0, 4),), -0.2, 0.2), 0.5, 1.5)
    norm_gain = jnp.clip(1.0 + 0.1 * jax.random.normal(key_of[13], (INNER,), jnp.float32), 0.5, 1.5)
    out_weight = bell_draw(key_of[14], (INNER, D), INNER ** -0.5, 0.09375, ((0, 4),))
    attn_gain = jnp.clip(1.0 + 0.1 * jax.random.normal(key_of[15], (D,), jnp.float32), 0.5, 1.5)
    q_weight = draw_q_weight(jax.random.fold_in(key_of[24], 71), 0)
    q_down = bell_draw(key_of[17], (D, RANK), D ** -0.5, 0.09375)
    q_up = bell_draw(key_of[18], (RANK, QW), RANK ** -0.5, 0.5, ((1, 4),))
    cache_keys = draw_cache_keys(jax.random.fold_in(key_of[24], 71), 0)
    cache_values = bell_draw(key_of[20], (TOKENS, QW), 1.0, 6.0, ((0, 32), (1, 4)))
    new_keys = bell_draw(key_of[21], (TOKENS, QW), 1.0, 6.0, ((0, 32), (1, 4)))
    new_values = bell_draw(key_of[22], (TOKENS, QW), 1.0, 6.0, ((0, 32), (1, 4)))
    lengths = ragged_sizes(key_of[23], PROMPTS, TOKENS, HALF_MAX, 2).astype(jnp.int32)
    return {"residual": residual, "x_in": x_in, "z_in": z_in, "bc_in": bc_in, "dt_in": dt_in, "conv_x_weight": conv_x_weight, "conv_bc_weight": conv_bc_weight, "conv_x_cache": conv_x_cache, "conv_bc_cache": conv_bc_cache, "ssm_cache": ssm_cache, "dt_bias": dt_bias, "a_log": a_log, "d_skip": d_skip, "norm_gain": norm_gain, "out_weight": out_weight, "attn_gain": attn_gain, "q_weight": q_weight, "q_down": q_down, "q_up": q_up, "cache_keys": cache_keys, "cache_values": cache_values, "new_keys": new_keys, "new_values": new_values, "lengths": lengths}


EPS = 1e-05
NEG = -1e+30

def locate(lengths, index):
    ends = jnp.cumsum(lengths).astype(jnp.int32)
    starts = (ends - lengths).astype(jnp.int32)
    count = lengths.shape[0]
    segment = lax.optimization_barrier(jnp.sum((index[:, None] >= ends[None, :]).astype(jnp.int32), axis=1)).astype(jnp.int32)
    segment = jnp.minimum(segment, count - 1)
    onehot = segment[:, None] == jnp.arange(count, dtype=jnp.int32)[None, :]
    begin = lax.optimization_barrier(jnp.sum(jnp.where(onehot, starts[None, :], 0), axis=1)).astype(jnp.int32)
    valid = (index >= 0) & (index < ends[count - 1])
    return (segment, begin, valid, onehot)

def convolve(inputs, cache, weight, position, onehot):
    taps = weight.shape[0]
    length = inputs.shape[0]
    padded = jnp.concatenate([jnp.zeros((taps - 1, inputs.shape[1]), inputs.dtype), inputs], axis=0)
    picks = onehot.astype(jnp.float32)
    cached_rows = [jnp.dot(picks, cache[:, slot, :].astype(jnp.float32), precision=lax.Precision.HIGHEST) for slot in range(taps - 1)]
    result = weight[0][None, :] * inputs.astype(jnp.float32)
    for lag in range(1, taps):
        shifted = padded[taps - 1 - lag:taps - 1 - lag + length].astype(jnp.float32)
        slot_index = taps - 1 + position - lag
        fallback = jnp.zeros_like(shifted)
        for slot in range(taps - 1):
            fallback = jnp.where((slot_index == slot)[:, None], cached_rows[slot], fallback)
        shifted = jnp.where((position >= lag)[:, None], shifted, fallback)
        result = result + weight[lag][None, :] * shifted
    return jax.nn.silu(result).astype(jnp.bfloat16)

def reference(residual, x_in, z_in, bc_in, dt_in, conv_x_weight, conv_bc_weight, conv_x_cache, conv_bc_cache, ssm_cache, dt_bias, a_log, d_skip, norm_gain, out_weight, attn_gain, q_weight, q_down, q_up, cache_keys, cache_values, new_keys, new_values, lengths):
    index = jnp.arange(TOKENS, dtype=jnp.int32)
    segment, begin, valid, onehot = locate(lengths, index)
    position = (index - begin).astype(jnp.int32)
    x_conv = convolve(x_in, conv_x_cache, conv_x_weight, position, onehot)
    bc_conv = convolve(bc_in, conv_bc_cache, conv_bc_weight, position, onehot)
    values = x_conv.astype(jnp.float32).reshape(TOKENS, MH, HD)
    inputs_b = bc_conv[:, :N].astype(jnp.float32)
    inputs_c = bc_conv[:, N:].astype(jnp.float32)
    step = jax.nn.softplus(dt_in + dt_bias[None, :])
    decay = jnp.exp(-step * jnp.exp(a_log)[None, :])

    def advance(state, inputs):
        x_row, b_row, c_row, decay_row, step_row, start_row, segment_row = inputs
        cached = lax.dynamic_index_in_dim(ssm_cache, segment_row, 0, keepdims=False)
        state = jnp.where(start_row, cached, state)
        state = decay_row[:, None, None] * state + (step_row[:, None] * x_row)[:, :, None] * b_row[None, None, :]
        return (state, lax.optimization_barrier(jnp.sum(state * c_row[None, None, :], axis=2)))
    initial = jnp.zeros((MH, HD, N), jnp.float32)
    _, outputs = lax.scan(advance, initial, (values, inputs_b, inputs_c, decay, step, position == 0, segment))
    mixed = outputs + d_skip[None, :, None] * values
    gated = (mixed * jax.nn.silu(z_in.astype(jnp.float32).reshape(TOKENS, MH, HD))).reshape(TOKENS, INNER)
    normed = (gated * lax.rsqrt(lax.optimization_barrier(jnp.mean(gated * gated, axis=1, keepdims=True)) + EPS) * norm_gain[None, :]).astype(jnp.bfloat16)
    hidden = (residual.astype(jnp.float32) + jnp.dot(normed, out_weight, preferred_element_type=jnp.float32)).astype(jnp.bfloat16)
    level = hidden.astype(jnp.float32)
    attn_in = (level * lax.rsqrt(lax.optimization_barrier(jnp.mean(level * level, axis=1, keepdims=True)) + EPS) * attn_gain[None, :]).astype(jnp.bfloat16)
    low = jnp.dot(attn_in, q_down, preferred_element_type=jnp.float32).astype(jnp.bfloat16)
    query = (jnp.dot(attn_in, q_weight, preferred_element_type=jnp.float32) + jnp.dot(low, q_up, preferred_element_type=jnp.float32)).astype(jnp.bfloat16)
    span = REACH * TOK_DEV
    padding = ((span, span), (0, 0))
    padded_ck = jnp.pad(cache_keys, padding)
    padded_cv = jnp.pad(cache_values, padding)
    padded_nk = jnp.pad(new_keys, padding)
    padded_nv = jnp.pad(new_values, padding)
    cache_span = (2 * REACH + 1) * TOK_DEV
    new_span = (REACH + 1) * TOK_DEV
    scale = 1.0 / HA ** 0.5

    def block_out(block_index):
        start = (block_index * TOK_DEV).astype(jnp.int32)
        query_index = start + jnp.arange(TOK_DEV, dtype=jnp.int32)
        query_segment = lax.dynamic_slice_in_dim(segment, start, TOK_DEV, 0)
        rows = lax.dynamic_slice_in_dim(query, start, TOK_DEV, 0).astype(jnp.float32).reshape(TOK_DEV, AH, HA)
        cache_index = (start - span + jnp.arange(cache_span, dtype=jnp.int32)).astype(jnp.int32)
        new_index = (start - span + jnp.arange(new_span, dtype=jnp.int32)).astype(jnp.int32)
        cache_segment, _, cache_valid, _ = locate(lengths, cache_index)
        new_segment, _, new_valid, _ = locate(lengths, new_index)
        cache_mask = cache_valid[None, :] & (cache_segment[None, :] == query_segment[:, None])
        new_mask = new_valid[None, :] & (new_segment[None, :] == query_segment[:, None]) & (new_index[None, :] <= query_index[:, None])
        mask = jnp.concatenate([cache_mask, new_mask], axis=1)
        keys = jnp.concatenate([lax.dynamic_slice_in_dim(padded_ck, start, cache_span, 0), lax.dynamic_slice_in_dim(padded_nk, start, new_span, 0)], axis=0)
        vals = jnp.concatenate([lax.dynamic_slice_in_dim(padded_cv, start, cache_span, 0), lax.dynamic_slice_in_dim(padded_nv, start, new_span, 0)], axis=0)
        keys = keys.astype(jnp.float32).reshape(-1, AH, HA)
        vals = vals.astype(jnp.float32).reshape(-1, AH, HA)
        scores = jnp.einsum('qhd,khd->hqk', rows, keys) * scale
        scores = jnp.where(mask[None], scores, NEG)
        top = lax.optimization_barrier(jnp.max(scores, axis=2, keepdims=True))
        weights = jnp.exp(scores - top)
        probs = (weights / lax.optimization_barrier(jnp.sum(weights, axis=2, keepdims=True))).astype(jnp.bfloat16)
        result = jnp.einsum('hqk,khd->qhd', probs.astype(jnp.float32), vals)
        return result.reshape(TOK_DEV, QW).astype(jnp.bfloat16)
    blocks = lax.map(block_out, jnp.arange(TOKENS // TOK_DEV, dtype=jnp.int32))
    attended = blocks.reshape(TOKENS, QW)
    return (hidden, attended)
```

```python
import jax
import jax.numpy as jnp
from jax import lax
from jax.sharding import PartitionSpec as P

HA = 224


EPS = 1e-05
NEG = -1e30


def shifted_2(value, axis, steps):
    count = lax.axis_size(axis)
    initial, last = (max(0, -steps), min(count, count - steps))
    return lax.ppermute(value, axis, [(source, source + steps) for source in range(initial, last)])


def locate(lengths, index):
    ends = jnp.cumsum(lengths)
    starts = ends - lengths
    count = lengths.shape[0]
    segment = jnp.sum((index[:, None] >= ends[None, :]).astype(jnp.int32), axis=1)
    segment = jnp.minimum(segment, count - 1)
    onehot = segment[:, None] == jnp.arange(count, dtype=jnp.int32)[None, :]
    begin = jnp.sum(jnp.where(onehot, starts[None, :], 0), axis=1)
    valid = (index >= 0) & (index < ends[count - 1])
    return (segment, begin, valid, onehot)


def convolve(inputs, border, cache, weight, position, onehot):
    taps = weight.shape[0]
    length = inputs.shape[0]
    extended = jnp.concatenate([border, inputs], axis=0)
    picks = onehot.astype(jnp.bfloat16)
    cached_rows = [
        jnp.dot(picks, cache[:, slot, :], preferred_element_type=jnp.float32)
        for slot in range(taps - 1)
    ]
    result = weight[0][None, :] * inputs.astype(jnp.float32)
    for lag in range(1, taps):
        shifted = extended[taps - 1 - lag : taps - 1 - lag + length].astype(jnp.float32)
        slot_index = taps - 1 + position - lag
        fallback = jnp.zeros_like(shifted)
        for slot in range(taps - 1):
            fallback = jnp.where((slot_index == slot)[:, None], cached_rows[slot], fallback)
        shifted = jnp.where((position >= lag)[:, None], shifted, fallback)
        result = result + weight[lag][None, :] * shifted
    return jax.nn.silu(result).astype(jnp.bfloat16)


def per_device(
    residual,
    x_in,
    z_in,
    bc_in,
    dt_in,
    conv_x_weight,
    conv_bc_weight,
    conv_x_cache,
    conv_bc_cache,
    ssm_cache,
    dt_bias,
    a_log,
    d_skip,
    norm_gain,
    out_weight,
    attn_gain,
    q_weight,
    q_down,
    q_up,
    cache_keys,
    cache_values,
    new_keys,
    new_values,
    lengths,
):
    high_precision = lax.Precision.HIGH
    length = x_in.shape[0]
    taps = conv_x_weight.shape[0]
    seq_index = lax.axis_index("seq")
    seq_count = lax.axis_size("seq")
    reach = seq_count // 4 + 1
    first = seq_index * length
    local_index = first + jnp.arange(length, dtype=jnp.int32)
    segment, begin, valid, onehot = locate(lengths, local_index)
    position = local_index - begin
    x_border, bc_border = shifted_2(
        (x_in[length - taps + 1 :], bc_in[length - taps + 1 :]), "seq", 1
    )
    x_conv = convolve(x_in, x_border, conv_x_cache, conv_x_weight, position, onehot)
    bc_conv = convolve(bc_in, bc_border, conv_bc_cache, conv_bc_weight, position, onehot)
    heads = dt_bias.shape[0]
    state_size = bc_in.shape[1] // 2
    head_size = x_in.shape[1] // heads
    prompts = lengths.shape[0]
    values_bf = x_conv.reshape(length, heads, head_size)
    values = x_conv.astype(jnp.float32).reshape(length, heads, head_size)
    inputs_b = bc_conv[:, :state_size]
    inputs_c = bc_conv[:, state_size:]
    step = jax.nn.softplus(dt_in + dt_bias[None, :])
    log_decay = -step * jnp.exp(a_log)[None, :]
    cumulative = jnp.cumsum(log_decay, axis=0)
    local_begin = jnp.maximum(begin - first, 0)
    before = jnp.take(cumulative - log_decay, local_begin, axis=0)
    from_begin = jnp.exp(cumulative - before)
    block = min(length, 512)
    pair_scores = jnp.dot(inputs_c, inputs_b.T, preferred_element_type=jnp.float32)
    cumulative_t = cumulative.T
    step_t = step.T
    order = jnp.arange(length, dtype=jnp.int32)

    def intra(block_start):
        query_rows = block_start + jnp.arange(block, dtype=jnp.int32)
        same = (segment[:, None] == segment[None, :]) & (query_rows[:, None] >= order[None, :])
        gap = cumulative_t[:, :, None] - cumulative_t[:, None, :]
        factor = jnp.where(same[None], jnp.exp(jnp.where(same[None], gap, 0.0)), 0.0)
        weights = factor * step_t[:, None, :] * pair_scores[None, :, :]
        return jnp.einsum(
            "hqs,shd->qhd",
            weights,
            values_bf,
            precision=high_precision,
            preferred_element_type=jnp.float32,
        )

    intra_out = lax.map(intra, jnp.arange(length // block, dtype=jnp.int32) * block).reshape(
        length, heads, head_size
    )
    last_segment = segment[length - 1]
    in_last = segment == last_segment
    tail_weight = (
        jnp.where(in_last[:, None], jnp.exp(cumulative[length - 1][None, :] - cumulative), 0.0)
        * step
    )
    weighted = tail_weight[:, :, None] * values
    local_state = jnp.einsum(
        "thd,tn->hdn",
        weighted,
        inputs_b,
        precision=high_precision,
        preferred_element_type=jnp.float32,
    )
    whole_decay = jnp.exp(cumulative[length - 1] - before[length - 1])
    starts_here = begin[length - 1] >= first
    cached_last = lax.dynamic_index_in_dim(ssm_cache, last_segment, 0, keepdims=False)
    chain_state = local_state + jnp.where(
        starts_here, whole_decay[:, None, None] * cached_last, 0.0
    )
    chain_decay = jnp.where(starts_here, jnp.zeros_like(whole_decay), whole_decay)

    scan_decay, scan_state = chain_decay, chain_state
    distance = 1
    while distance <= reach and distance < seq_count:
        prior_decay, prior_state = shifted_2((scan_decay, scan_state), "seq", distance)
        scan_state = scan_decay[:, None, None] * prior_state + scan_state
        scan_decay = scan_decay * prior_decay
        distance *= 2
    carried = shifted_2(scan_state, "seq", 1)
    continuing = position[0] > 0
    replace = (jnp.arange(prompts, dtype=jnp.int32) == segment[0]) & continuing
    initial = jnp.where(replace[:, None, None, None], carried[None], ssm_cache)
    selected = (onehot[:, :, None].astype(jnp.bfloat16) * inputs_c[:, None, :]).reshape(
        length, prompts * state_size
    )
    table = jnp.transpose(initial, (0, 3, 1, 2)).reshape(prompts * state_size, heads * head_size)
    init_out = (
        jnp.dot(
            selected, table, precision=high_precision, preferred_element_type=jnp.float32
        ).reshape(length, heads, head_size)
        * from_begin[:, :, None]
    )
    mixed = intra_out + init_out + d_skip[None, :, None] * values
    gated = (
        mixed * jax.nn.silu(z_in.astype(jnp.float32).reshape(length, heads, head_size))
    ).reshape(length, heads * head_size)
    squares = lax.psum(jnp.sum(gated * gated, axis=1), "tp")
    width = gated.shape[1] * lax.axis_size("tp")
    normed = (gated * lax.rsqrt(squares / width + EPS)[:, None] * norm_gain[None, :]).astype(
        jnp.bfloat16
    )
    summed = lax.psum_scatter(
        jnp.dot(normed, out_weight, preferred_element_type=jnp.float32),
        "tp",
        scatter_dimension=0,
        tiled=True,
    )
    hidden = (residual.astype(jnp.float32) + summed).astype(jnp.bfloat16)
    level = hidden.astype(jnp.float32)
    attn_in = (
        level * lax.rsqrt(jnp.mean(level * level, axis=1, keepdims=True) + EPS) * attn_gain[None, :]
    ).astype(jnp.bfloat16)
    piece = lax.all_gather(attn_in, "tp", axis=0, tiled=True)
    low = jnp.dot(piece, q_down, preferred_element_type=jnp.float32).astype(jnp.bfloat16)
    query = (
        jnp.dot(piece, q_weight, preferred_element_type=jnp.float32)
        + jnp.dot(low, q_up, preferred_element_type=jnp.float32)
    ).astype(jnp.bfloat16)
    count_heads = query.shape[1] // HA

    def piece_mask(query_index, query_segment, offset, causal):
        key_index = (seq_index + offset) * length + jnp.arange(length, dtype=jnp.int32)
        key_segment, _, key_valid, _ = locate(lengths, key_index)
        allowed = key_valid[None, :] & (key_segment[None, :] == query_segment[:, None])
        if causal:
            allowed = allowed & (key_index[None, :] <= query_index[:, None])
        return allowed

    cache_pieces = [(cache_keys, cache_values, 0)]
    new_pieces = [(new_keys, new_values, 0)]
    for distance in range(1, reach + 1):
        behind = shifted_2((cache_keys, cache_values, new_keys, new_values), "seq", distance)
        cache_pieces.append((behind[0], behind[1], -distance))
        new_pieces.append((behind[2], behind[3], -distance))
        forward = shifted_2((cache_keys, cache_values), "seq", -distance)
        cache_pieces.append((forward[0], forward[1], distance))
    all_keys = jnp.concatenate(
        [entry[0] for entry in cache_pieces] + [entry[0] for entry in new_pieces], axis=0
    )
    all_values = jnp.concatenate(
        [entry[1] for entry in cache_pieces] + [entry[1] for entry in new_pieces], axis=0
    )
    mask = jnp.concatenate(
        [piece_mask(local_index, segment, entry[2], False) for entry in cache_pieces]
        + [piece_mask(local_index, segment, entry[2], True) for entry in new_pieces],
        axis=1,
    )
    scale = 1.0 / HA**0.5

    def attend(head):
        column = head * HA
        query_head = lax.dynamic_slice_in_dim(query, column, HA, 1)
        key_head = lax.dynamic_slice_in_dim(all_keys, column, HA, 1)
        value_head = lax.dynamic_slice_in_dim(all_values, column, HA, 1)
        scores = (
            lax.dot_general(
                query_head, key_head, (((1,), (1,)), ((), ())), preferred_element_type=jnp.float32
            )
            * scale
        )
        scores = jnp.where(mask, scores, NEG)
        top = jnp.max(scores, axis=1, keepdims=True)
        weights = jnp.exp(scores - top)
        probs = (weights / jnp.sum(weights, axis=1, keepdims=True)).astype(jnp.bfloat16)
        return jnp.dot(probs, value_head, preferred_element_type=jnp.float32).astype(jnp.bfloat16)

    per_head = lax.map(attend, jnp.arange(count_heads, dtype=jnp.int32))
    attended = jnp.transpose(per_head, (1, 0, 2)).reshape(length, count_heads * HA)
    return (hidden, attended)


def solution(mesh):
    in_specs = (
        P(("seq", "tp"), None),
        P("seq", "tp"),
        P("seq", "tp"),
        P("seq", None),
        P("seq", "tp"),
        P(None, "tp"),
        P(),
        P(None, None, "tp"),
        P(),
        P(None, "tp", None, None),
        P("tp"),
        P("tp"),
        P("tp"),
        P("tp"),
        P("tp", None),
        P(),
        P(None, "tp"),
        P(),
        P(None, "tp"),
        P("seq", "tp"),
        P("seq", "tp"),
        P("seq", "tp"),
        P("seq", "tp"),
        P(),
    )
    out_specs = (P(("seq", "tp"), None), P("seq", "tp"))
    return jax.shard_map(
        per_device, mesh=mesh, in_specs=in_specs, out_specs=out_specs, check_vma=False
    )
```

```python
import jax
import jax.numpy as jnp
from jax import lax
from jax.sharding import PartitionSpec as P

HA = 224


EPS = 1e-05
NEG = -1e30


def shifted_2(value, axis, steps):
    count = lax.axis_size(axis)
    initial, last = (max(0, -steps), min(count, count - steps))
    return lax.ppermute(value, axis, [(source, source + steps) for source in range(initial, last)])


def locate(lengths, index):
    ends = jnp.cumsum(lengths)
    starts = ends - lengths
    count = lengths.shape[0]
    segment = jnp.sum((index[:, None] >= ends[None, :]).astype(jnp.int32), axis=1)
    segment = jnp.minimum(segment, count - 1)
    onehot = segment[:, None] == jnp.arange(count, dtype=jnp.int32)[None, :]
    begin = jnp.sum(jnp.where(onehot, starts[None, :], 0), axis=1)
    valid = (index >= 0) & (index < ends[count - 1])
    return (segment, begin, valid, onehot)


def convolve(inputs, border, cache, weight, position, onehot):
    taps = weight.shape[0]
    length = inputs.shape[0]
    extended = jnp.concatenate([border, inputs], axis=0)
    picks = onehot.astype(jnp.bfloat16)
    cached_rows = [
        jnp.dot(picks, cache[:, slot, :], preferred_element_type=jnp.float32)
        for slot in range(taps - 1)
    ]
    result = weight[0][None, :] * inputs.astype(jnp.float32)
    for lag in range(1, taps):
        shifted = extended[taps - 1 - lag : taps - 1 - lag + length].astype(jnp.float32)
        slot_index = taps - 1 + position - lag
        fallback = jnp.zeros_like(shifted)
        for slot in range(taps - 1):
            fallback = jnp.where((slot_index == slot)[:, None], cached_rows[slot], fallback)
        shifted = jnp.where((position >= lag)[:, None], shifted, fallback)
        result = result + weight[lag][None, :] * shifted
    return jax.nn.silu(result).astype(jnp.bfloat16)


def per_device(
    residual,
    x_in,
    z_in,
    bc_in,
    dt_in,
    conv_x_weight,
    conv_bc_weight,
    conv_x_cache,
    conv_bc_cache,
    ssm_cache,
    dt_bias,
    a_log,
    d_skip,
    norm_gain,
    out_weight,
    attn_gain,
    q_weight,
    q_down,
    q_up,
    cache_keys,
    cache_values,
    new_keys,
    new_values,
    lengths,
):
    high_precision = lax.Precision.HIGH
    length = x_in.shape[0]
    taps = conv_x_weight.shape[0]
    seq_index = lax.axis_index("seq")
    seq_count = lax.axis_size("seq")
    reach = seq_count // 4 + 1
    first = seq_index * length
    local_index = first + jnp.arange(length, dtype=jnp.int32)
    segment, begin, valid, onehot = locate(lengths, local_index)
    position = local_index - begin
    x_border, bc_border = shifted_2(
        (x_in[length - taps + 1 :], bc_in[length - taps + 1 :]), "seq", 1
    )
    x_conv = convolve(x_in, x_border, conv_x_cache, conv_x_weight, position, onehot)
    bc_conv = convolve(bc_in, bc_border, conv_bc_cache, conv_bc_weight, position, onehot)
    heads = dt_bias.shape[0]
    state_size = bc_in.shape[1] // 2
    head_size = x_in.shape[1] // heads
    prompts = lengths.shape[0]
    values_bf = x_conv.reshape(length, heads, head_size)
    values = x_conv.astype(jnp.float32).reshape(length, heads, head_size)
    inputs_b = bc_conv[:, :state_size]
    inputs_c = bc_conv[:, state_size:]
    step = jax.nn.softplus(dt_in + dt_bias[None, :])
    log_decay = -step * jnp.exp(a_log)[None, :]
    cumulative = jnp.cumsum(log_decay, axis=0)
    local_begin = jnp.maximum(begin - first, 0)
    before = jnp.take(cumulative - log_decay, local_begin, axis=0)
    from_begin = jnp.exp(cumulative - before)
    block = min(length, 512)
    pair_scores = jnp.dot(inputs_c, inputs_b.T, preferred_element_type=jnp.float32)
    cumulative_t = cumulative.T
    step_t = step.T
    order = jnp.arange(length, dtype=jnp.int32)

    def intra(block_start):
        query_rows = block_start + jnp.arange(block, dtype=jnp.int32)
        same = (segment[:, None] == segment[None, :]) & (query_rows[:, None] >= order[None, :])
        gap = cumulative_t[:, :, None] - cumulative_t[:, None, :]
        factor = jnp.where(same[None], jnp.exp(jnp.where(same[None], gap, 0.0)), 0.0)
        weights = factor * step_t[:, None, :] * pair_scores[None, :, :]
        return jnp.einsum(
            "hqs,shd->qhd",
            weights,
            values_bf,
            precision=high_precision,
            preferred_element_type=jnp.float32,
        )

    intra_out = lax.map(intra, jnp.arange(length // block, dtype=jnp.int32) * block).reshape(
        length, heads, head_size
    )
    last_segment = segment[length - 1]
    in_last = segment == last_segment
    tail_weight = (
        jnp.where(in_last[:, None], jnp.exp(cumulative[length - 1][None, :] - cumulative), 0.0)
        * step
    )
    weighted = tail_weight[:, :, None] * values
    local_state = jnp.einsum(
        "thd,tn->hdn",
        weighted,
        inputs_b,
        precision=high_precision,
        preferred_element_type=jnp.float32,
    )
    whole_decay = jnp.exp(cumulative[length - 1] - before[length - 1])
    starts_here = begin[length - 1] >= first
    cached_last = lax.dynamic_index_in_dim(ssm_cache, last_segment, 0, keepdims=False)
    chain_state = local_state + jnp.where(
        starts_here, whole_decay[:, None, None] * cached_last, 0.0
    )
    chain_decay = jnp.where(starts_here, jnp.zeros_like(whole_decay), whole_decay)

    scan_decay, scan_state = chain_decay, chain_state
    distance = 1
    while distance <= reach and distance < seq_count:
        prior_decay, prior_state = shifted_2((scan_decay, scan_state), "seq", distance)
        scan_state = scan_decay[:, None, None] * prior_state + scan_state
        scan_decay = scan_decay * prior_decay
        distance *= 2
    carried = shifted_2(scan_state, "seq", 1)
    continuing = position[0] > 0
    replace = (jnp.arange(prompts, dtype=jnp.int32) == segment[0]) & continuing
    initial = jnp.where(replace[:, None, None, None], carried[None], ssm_cache)
    selected = (onehot[:, :, None].astype(jnp.bfloat16) * inputs_c[:, None, :]).reshape(
        length, prompts * state_size
    )
    table = jnp.transpose(initial, (0, 3, 1, 2)).reshape(prompts * state_size, heads * head_size)
    init_out = (
        jnp.dot(
            selected, table, precision=high_precision, preferred_element_type=jnp.float32
        ).reshape(length, heads, head_size)
        * from_begin[:, :, None]
    )
    mixed = intra_out + init_out + d_skip[None, :, None] * values
    gated = (
        mixed * jax.nn.silu(z_in.astype(jnp.float32).reshape(length, heads, head_size))
    ).reshape(length, heads * head_size)
    squares = lax.psum(jnp.sum(gated * gated, axis=1), "tp")
    width = gated.shape[1] * lax.axis_size("tp")
    normed = (gated * lax.rsqrt(squares / width + EPS)[:, None] * norm_gain[None, :]).astype(
        jnp.bfloat16
    )
    summed = lax.psum_scatter(
        jnp.dot(normed, out_weight, preferred_element_type=jnp.float32),
        "tp",
        scatter_dimension=0,
        tiled=True,
    )
    hidden = (residual.astype(jnp.float32) + summed).astype(jnp.bfloat16)
    level = hidden.astype(jnp.float32)
    attn_in = (
        level * lax.rsqrt(jnp.mean(level * level, axis=1, keepdims=True) + EPS) * attn_gain[None, :]
    ).astype(jnp.bfloat16)
    piece = lax.all_gather(attn_in, "tp", axis=0, tiled=True)
    low = jnp.dot(piece, q_down, preferred_element_type=jnp.float32).astype(jnp.bfloat16)
    query = (
        jnp.dot(piece, q_weight, preferred_element_type=jnp.float32)
        + jnp.dot(low, q_up, preferred_element_type=jnp.float32)
    ).astype(jnp.bfloat16)
    count_heads = query.shape[1] // HA

    def piece_mask(query_index, query_segment, offset, causal):
        key_index = (seq_index + offset) * length + jnp.arange(length, dtype=jnp.int32)
        key_segment, _, key_valid, _ = locate(lengths, key_index)
        allowed = key_valid[None, :] & (key_segment[None, :] == query_segment[:, None])
        if causal:
            allowed = allowed & (key_index[None, :] <= query_index[:, None])
        return allowed

    cache_pieces = [(cache_keys, cache_values, 0)]
    new_pieces = [(new_keys, new_values, 0)]
    earlier = jnp.stack([cache_keys, cache_values, new_keys, new_values])
    later = jnp.stack([cache_keys, cache_values])
    for distance in range(1, reach + 1):
        behind = shifted_2(earlier, "seq", distance)
        cache_pieces.append((behind[0], behind[1], -distance))
        new_pieces.append((behind[2], behind[3], -distance))
        forward = shifted_2(later, "seq", -distance)
        cache_pieces.append((forward[0], forward[1], distance))
    all_keys = jnp.concatenate(
        [entry[0] for entry in cache_pieces] + [entry[0] for entry in new_pieces], axis=0
    )
    all_values = jnp.concatenate(
        [entry[1] for entry in cache_pieces] + [entry[1] for entry in new_pieces], axis=0
    )
    mask = jnp.concatenate(
        [piece_mask(local_index, segment, entry[2], False) for entry in cache_pieces]
        + [piece_mask(local_index, segment, entry[2], True) for entry in new_pieces],
        axis=1,
    )
    scale = 1.0 / HA**0.5

    def attend(head):
        column = head * HA
        query_head = lax.dynamic_slice_in_dim(query, column, HA, 1)
        key_head = lax.dynamic_slice_in_dim(all_keys, column, HA, 1)
        value_head = lax.dynamic_slice_in_dim(all_values, column, HA, 1)
        scores = (
            lax.dot_general(
                query_head, key_head, (((1,), (1,)), ((), ())), preferred_element_type=jnp.float32
            )
            * scale
        )
        scores = jnp.where(mask, scores, NEG)
        top = jnp.max(scores, axis=1, keepdims=True)
        weights = jnp.exp(scores - top)
        probs = (weights / jnp.sum(weights, axis=1, keepdims=True)).astype(jnp.bfloat16)
        return jnp.dot(probs, value_head, preferred_element_type=jnp.float32).astype(jnp.bfloat16)

    per_head = lax.map(attend, jnp.arange(count_heads, dtype=jnp.int32))
    attended = jnp.transpose(per_head, (1, 0, 2)).reshape(length, count_heads * HA)
    return (hidden, attended)


def solution(mesh):
    in_specs = (
        P(("seq", "tp"), None),
        P("seq", "tp"),
        P("seq", "tp"),
        P("seq", None),
        P("seq", "tp"),
        P(None, "tp"),
        P(),
        P(None, None, "tp"),
        P(),
        P(None, "tp", None, None),
        P("tp"),
        P("tp"),
        P("tp"),
        P("tp"),
        P("tp", None),
        P(),
        P(None, "tp"),
        P(),
        P(None, "tp"),
        P("seq", "tp"),
        P("seq", "tp"),
        P("seq", "tp"),
        P("seq", "tp"),
        P(),
    )
    out_specs = (P(("seq", "tp"), None), P("seq", "tp"))
    return jax.shard_map(
        per_device, mesh=mesh, in_specs=in_specs, out_specs=out_specs, check_vma=False
    )
```

```python
import jax
import jax.numpy as jnp
from jax import lax
from jax.sharding import PartitionSpec as P

HA = 224


EPS = 1e-05
NEG = -1e30


def shifted_2(value, axis, steps):
    count = lax.axis_size(axis)
    initial, last = (max(0, -steps), min(count, count - steps))
    return lax.ppermute(value, axis, [(source, source + steps) for source in range(initial, last)])


def locate(lengths, index):
    ends = jnp.cumsum(lengths)
    starts = ends - lengths
    count = lengths.shape[0]
    segment = jnp.sum((index[:, None] >= ends[None, :]).astype(jnp.int32), axis=1)
    segment = jnp.minimum(segment, count - 1)
    onehot = segment[:, None] == jnp.arange(count, dtype=jnp.int32)[None, :]
    begin = jnp.sum(jnp.where(onehot, starts[None, :], 0), axis=1)
    valid = (index >= 0) & (index < ends[count - 1])
    return (segment, begin, valid, onehot)


def convolve(inputs, border, cache, weight, position, onehot):
    taps = weight.shape[0]
    length = inputs.shape[0]
    extended = jnp.concatenate([border, inputs], axis=0)
    picks = onehot.astype(jnp.bfloat16)
    cached_rows = [
        jnp.dot(picks, cache[:, slot, :], preferred_element_type=jnp.float32)
        for slot in range(taps - 1)
    ]
    result = weight[0][None, :] * inputs.astype(jnp.float32)
    for lag in range(1, taps):
        shifted = extended[taps - 1 - lag : taps - 1 - lag + length].astype(jnp.float32)
        slot_index = taps - 1 + position - lag
        fallback = jnp.zeros_like(shifted)
        for slot in range(taps - 1):
            fallback = jnp.where((slot_index == slot)[:, None], cached_rows[slot], fallback)
        shifted = jnp.where((position >= lag)[:, None], shifted, fallback)
        result = result + weight[lag][None, :] * shifted
    return jax.nn.silu(result).astype(jnp.bfloat16)


def per_device(
    residual,
    x_in,
    z_in,
    bc_in,
    dt_in,
    conv_x_weight,
    conv_bc_weight,
    conv_x_cache,
    conv_bc_cache,
    ssm_cache,
    dt_bias,
    a_log,
    d_skip,
    norm_gain,
    out_weight,
    attn_gain,
    q_weight,
    q_down,
    q_up,
    cache_keys,
    cache_values,
    new_keys,
    new_values,
    lengths,
):
    high_precision = lax.Precision.HIGH
    length = x_in.shape[0]
    taps = conv_x_weight.shape[0]
    seq_index = lax.axis_index("seq")
    seq_count = lax.axis_size("seq")
    reach = seq_count // 4 + 1
    first = seq_index * length
    behind = jnp.stack([cache_keys, cache_values, new_keys, new_values])
    forward = jnp.stack([cache_keys, cache_values])
    behind_pieces, forward_pieces = [], []
    for _ in range(reach):
        behind = shifted_2(behind, "seq", 1)
        forward = shifted_2(forward, "seq", -1)
        behind_pieces.append(behind)
        forward_pieces.append(forward)
    local_index = first + jnp.arange(length, dtype=jnp.int32)
    segment, begin, valid, onehot = locate(lengths, local_index)
    position = local_index - begin
    x_border, bc_border = shifted_2(
        (x_in[length - taps + 1 :], bc_in[length - taps + 1 :]), "seq", 1
    )
    x_conv = convolve(x_in, x_border, conv_x_cache, conv_x_weight, position, onehot)
    bc_conv = convolve(bc_in, bc_border, conv_bc_cache, conv_bc_weight, position, onehot)
    heads = dt_bias.shape[0]
    state_size = bc_in.shape[1] // 2
    head_size = x_in.shape[1] // heads
    prompts = lengths.shape[0]
    values_bf = x_conv.reshape(length, heads, head_size)
    values = x_conv.astype(jnp.float32).reshape(length, heads, head_size)
    inputs_b = bc_conv[:, :state_size]
    inputs_c = bc_conv[:, state_size:]
    step = jax.nn.softplus(dt_in + dt_bias[None, :])
    log_decay = -step * jnp.exp(a_log)[None, :]
    cumulative = jnp.cumsum(log_decay, axis=0)
    local_begin = jnp.maximum(begin - first, 0)
    before = jnp.take(cumulative - log_decay, local_begin, axis=0)
    from_begin = jnp.exp(cumulative - before)
    block = min(length, 512)
    pair_scores = jnp.dot(inputs_c, inputs_b.T, preferred_element_type=jnp.float32)
    cumulative_t = cumulative.T
    step_t = step.T
    order = jnp.arange(length, dtype=jnp.int32)

    def intra(block_start):
        query_rows = block_start + jnp.arange(block, dtype=jnp.int32)
        same = (segment[:, None] == segment[None, :]) & (query_rows[:, None] >= order[None, :])
        gap = cumulative_t[:, :, None] - cumulative_t[:, None, :]
        factor = jnp.where(same[None], jnp.exp(jnp.where(same[None], gap, 0.0)), 0.0)
        weights = factor * step_t[:, None, :] * pair_scores[None, :, :]
        return jnp.einsum(
            "hqs,shd->qhd",
            weights,
            values_bf,
            precision=high_precision,
            preferred_element_type=jnp.float32,
        )

    intra_out = lax.map(intra, jnp.arange(length // block, dtype=jnp.int32) * block).reshape(
        length, heads, head_size
    )
    last_segment = segment[length - 1]
    in_last = segment == last_segment
    tail_weight = (
        jnp.where(in_last[:, None], jnp.exp(cumulative[length - 1][None, :] - cumulative), 0.0)
        * step
    )
    weighted = tail_weight[:, :, None] * values
    local_state = jnp.einsum(
        "thd,tn->hdn",
        weighted,
        inputs_b,
        precision=high_precision,
        preferred_element_type=jnp.float32,
    )
    whole_decay = jnp.exp(cumulative[length - 1] - before[length - 1])
    starts_here = begin[length - 1] >= first
    cached_last = lax.dynamic_index_in_dim(ssm_cache, last_segment, 0, keepdims=False)
    chain_state = local_state + jnp.where(
        starts_here, whole_decay[:, None, None] * cached_last, 0.0
    )
    chain_decay = jnp.where(starts_here, jnp.zeros_like(whole_decay), whole_decay)

    scan_decay, scan_state = chain_decay, chain_state
    distance = 1
    while distance <= reach and distance < seq_count:
        prior_decay, prior_state = shifted_2((scan_decay, scan_state), "seq", distance)
        scan_state = scan_decay[:, None, None] * prior_state + scan_state
        scan_decay = scan_decay * prior_decay
        distance *= 2
    carried = shifted_2(scan_state, "seq", 1)
    continuing = position[0] > 0
    replace = (jnp.arange(prompts, dtype=jnp.int32) == segment[0]) & continuing
    initial = jnp.where(replace[:, None, None, None], carried[None], ssm_cache)
    selected = (onehot[:, :, None].astype(jnp.bfloat16) * inputs_c[:, None, :]).reshape(
        length, prompts * state_size
    )
    table = jnp.transpose(initial, (0, 3, 1, 2)).reshape(prompts * state_size, heads * head_size)
    init_out = (
        jnp.dot(
            selected, table, precision=high_precision, preferred_element_type=jnp.float32
        ).reshape(length, heads, head_size)
        * from_begin[:, :, None]
    )
    mixed = intra_out + init_out + d_skip[None, :, None] * values
    gated = (
        mixed * jax.nn.silu(z_in.astype(jnp.float32).reshape(length, heads, head_size))
    ).reshape(length, heads * head_size)
    squares = lax.psum(jnp.sum(gated * gated, axis=1), "tp")
    width = gated.shape[1] * lax.axis_size("tp")
    normed = (gated * lax.rsqrt(squares / width + EPS)[:, None] * norm_gain[None, :]).astype(
        jnp.bfloat16
    )
    summed = lax.psum_scatter(
        jnp.dot(normed, out_weight, preferred_element_type=jnp.float32),
        "tp",
        scatter_dimension=0,
        tiled=True,
    )
    hidden = (residual.astype(jnp.float32) + summed).astype(jnp.bfloat16)
    level = hidden.astype(jnp.float32)
    attn_in = (
        level * lax.rsqrt(jnp.mean(level * level, axis=1, keepdims=True) + EPS) * attn_gain[None, :]
    ).astype(jnp.bfloat16)
    piece = lax.all_gather(attn_in, "tp", axis=0, tiled=True)
    low = jnp.dot(piece, q_down, preferred_element_type=jnp.float32).astype(jnp.bfloat16)
    query = (
        jnp.dot(piece, q_weight, preferred_element_type=jnp.float32)
        + jnp.dot(low, q_up, preferred_element_type=jnp.float32)
    ).astype(jnp.bfloat16)
    count_heads = query.shape[1] // HA

    def piece_mask(query_index, query_segment, offset, causal):
        key_index = (seq_index + offset) * length + jnp.arange(length, dtype=jnp.int32)
        key_segment, _, key_valid, _ = locate(lengths, key_index)
        allowed = key_valid[None, :] & (key_segment[None, :] == query_segment[:, None])
        if causal:
            allowed = allowed & (key_index[None, :] <= query_index[:, None])
        return allowed

    cache_pieces = [(cache_keys, cache_values, 0)]
    new_pieces = [(new_keys, new_values, 0)]
    for distance in range(1, reach + 1):
        behind = behind_pieces[distance - 1]
        cache_pieces.append((behind[0], behind[1], -distance))
        new_pieces.append((behind[2], behind[3], -distance))
        forward = forward_pieces[distance - 1]
        cache_pieces.append((forward[0], forward[1], distance))
    all_keys = jnp.concatenate(
        [entry[0] for entry in cache_pieces] + [entry[0] for entry in new_pieces], axis=0
    )
    all_values = jnp.concatenate(
        [entry[1] for entry in cache_pieces] + [entry[1] for entry in new_pieces], axis=0
    )
    mask = jnp.concatenate(
        [piece_mask(local_index, segment, entry[2], False) for entry in cache_pieces]
        + [piece_mask(local_index, segment, entry[2], True) for entry in new_pieces],
        axis=1,
    )
    scale = 1.0 / HA**0.5

    def attend(head):
        column = head * HA
        query_head = lax.dynamic_slice_in_dim(query, column, HA, 1)
        key_head = lax.dynamic_slice_in_dim(all_keys, column, HA, 1)
        value_head = lax.dynamic_slice_in_dim(all_values, column, HA, 1)
        scores = (
            lax.dot_general(
                query_head, key_head, (((1,), (1,)), ((), ())), preferred_element_type=jnp.float32
            )
            * scale
        )
        scores = jnp.where(mask, scores, NEG)
        top = jnp.max(scores, axis=1, keepdims=True)
        weights = jnp.exp(scores - top)
        probs = (weights / jnp.sum(weights, axis=1, keepdims=True)).astype(jnp.bfloat16)
        return jnp.dot(probs, value_head, preferred_element_type=jnp.float32).astype(jnp.bfloat16)

    per_head = lax.map(attend, jnp.arange(count_heads, dtype=jnp.int32))
    attended = jnp.transpose(per_head, (1, 0, 2)).reshape(length, count_heads * HA)
    return (hidden, attended)


def solution(mesh):
    in_specs = (
        P(("seq", "tp"), None),
        P("seq", "tp"),
        P("seq", "tp"),
        P("seq", None),
        P("seq", "tp"),
        P(None, "tp"),
        P(),
        P(None, None, "tp"),
        P(),
        P(None, "tp", None, None),
        P("tp"),
        P("tp"),
        P("tp"),
        P("tp"),
        P("tp", None),
        P(),
        P(None, "tp"),
        P(),
        P(None, "tp"),
        P("seq", "tp"),
        P("seq", "tp"),
        P("seq", "tp"),
        P("seq", "tp"),
        P(),
    )
    out_specs = (P(("seq", "tp"), None), P("seq", "tp"))
    return jax.shard_map(
        per_device, mesh=mesh, in_specs=in_specs, out_specs=out_specs, check_vma=False
    )
```

```python
import jax
import jax.numpy as jnp
from jax import lax
from jax.sharding import PartitionSpec as P

HA = 224


EPS = 1e-05
NEG = -1e30


def shifted_2(value, axis, steps):
    count = lax.axis_size(axis)
    initial, last = (max(0, -steps), min(count, count - steps))
    return lax.ppermute(value, axis, [(source, source + steps) for source in range(initial, last)])


def locate(lengths, index):
    ends = jnp.cumsum(lengths)
    starts = ends - lengths
    count = lengths.shape[0]
    segment = jnp.sum((index[:, None] >= ends[None, :]).astype(jnp.int32), axis=1)
    segment = jnp.minimum(segment, count - 1)
    onehot = segment[:, None] == jnp.arange(count, dtype=jnp.int32)[None, :]
    begin = jnp.sum(jnp.where(onehot, starts[None, :], 0), axis=1)
    valid = (index >= 0) & (index < ends[count - 1])
    return (segment, begin, valid, onehot)


def convolve(inputs, border, cache, weight, position, onehot):
    taps = weight.shape[0]
    length = inputs.shape[0]
    extended = jnp.concatenate([border, inputs], axis=0)
    picks = onehot.astype(jnp.bfloat16)
    cached_rows = [
        jnp.dot(picks, cache[:, slot, :], preferred_element_type=jnp.float32)
        for slot in range(taps - 1)
    ]
    result = weight[0][None, :] * inputs.astype(jnp.float32)
    for lag in range(1, taps):
        shifted = extended[taps - 1 - lag : taps - 1 - lag + length].astype(jnp.float32)
        slot_index = taps - 1 + position - lag
        fallback = jnp.zeros_like(shifted)
        for slot in range(taps - 1):
            fallback = jnp.where((slot_index == slot)[:, None], cached_rows[slot], fallback)
        shifted = jnp.where((position >= lag)[:, None], shifted, fallback)
        result = result + weight[lag][None, :] * shifted
    return jax.nn.silu(result).astype(jnp.bfloat16)


def per_device(
    residual,
    x_in,
    z_in,
    bc_in,
    dt_in,
    conv_x_weight,
    conv_bc_weight,
    conv_x_cache,
    conv_bc_cache,
    ssm_cache,
    dt_bias,
    a_log,
    d_skip,
    norm_gain,
    out_weight,
    attn_gain,
    q_weight,
    q_down,
    q_up,
    cache_keys,
    cache_values,
    new_keys,
    new_values,
    lengths,
):
    high_precision = lax.Precision.HIGH
    length = x_in.shape[0]
    taps = conv_x_weight.shape[0]
    seq_index = lax.axis_index("seq")
    seq_count = lax.axis_size("seq")
    reach = seq_count // 4 + 1
    first = seq_index * length
    long_hop = seq_count // 4
    behind_pieces = [jnp.stack([cache_keys, cache_values, new_keys, new_values])] * (reach + 1)
    forward_pieces = [jnp.stack([cache_keys, cache_values])] * (reach + 1)
    relay_steps = []
    for distance in range(1, long_hop):
        relay_steps.append([(distance, distance - 1, 1)])
    for distance in range(long_hop, reach + 1):
        relay_steps[distance - long_hop].append((distance, distance - long_hop, long_hop))

    def advance(values):
        if not relay_steps:
            return values
        moves = relay_steps.pop(0)
        sent = []
        for distance, source, steps in moves:
            sent.append(
                (
                    shifted_2(behind_pieces[source], "seq", steps),
                    shifted_2(forward_pieces[source], "seq", -steps),
                )
            )
        sent, values = lax.optimization_barrier((sent, values))
        for (distance, _, _), (behind, forward) in zip(moves, sent):
            behind_pieces[distance] = behind
            forward_pieces[distance] = forward
        return values

    local_index = first + jnp.arange(length, dtype=jnp.int32)
    segment, begin, valid, onehot = locate(lengths, local_index)
    position = local_index - begin
    x_border, bc_border = shifted_2(
        (x_in[length - taps + 1 :], bc_in[length - taps + 1 :]), "seq", 1
    )
    x_conv = convolve(x_in, x_border, conv_x_cache, conv_x_weight, position, onehot)
    bc_conv = convolve(bc_in, bc_border, conv_bc_cache, conv_bc_weight, position, onehot)
    x_conv, bc_conv = advance((x_conv, bc_conv))
    heads = dt_bias.shape[0]
    state_size = bc_in.shape[1] // 2
    head_size = x_in.shape[1] // heads
    prompts = lengths.shape[0]
    values_bf = x_conv.reshape(length, heads, head_size)
    values = x_conv.astype(jnp.float32).reshape(length, heads, head_size)
    inputs_b = bc_conv[:, :state_size]
    inputs_c = bc_conv[:, state_size:]
    step = jax.nn.softplus(dt_in + dt_bias[None, :])
    log_decay = -step * jnp.exp(a_log)[None, :]
    cumulative = jnp.cumsum(log_decay, axis=0)
    local_begin = jnp.maximum(begin - first, 0)
    before = jnp.take(cumulative - log_decay, local_begin, axis=0)
    from_begin = jnp.exp(cumulative - before)
    block = min(length, 512)
    pair_scores = jnp.dot(inputs_c, inputs_b.T, preferred_element_type=jnp.float32)
    cumulative_t = cumulative.T
    step_t = step.T
    order = jnp.arange(length, dtype=jnp.int32)

    def intra(block_start):
        query_rows = block_start + jnp.arange(block, dtype=jnp.int32)
        same = (segment[:, None] == segment[None, :]) & (query_rows[:, None] >= order[None, :])
        gap = cumulative_t[:, :, None] - cumulative_t[:, None, :]
        factor = jnp.where(same[None], jnp.exp(jnp.where(same[None], gap, 0.0)), 0.0)
        weights = factor * step_t[:, None, :] * pair_scores[None, :, :]
        return jnp.einsum(
            "hqs,shd->qhd",
            weights,
            values_bf,
            precision=high_precision,
            preferred_element_type=jnp.float32,
        )

    intra_out = lax.map(intra, jnp.arange(length // block, dtype=jnp.int32) * block).reshape(
        length, heads, head_size
    )
    last_segment = segment[length - 1]
    in_last = segment == last_segment
    tail_weight = (
        jnp.where(in_last[:, None], jnp.exp(cumulative[length - 1][None, :] - cumulative), 0.0)
        * step
    )
    weighted = tail_weight[:, :, None] * values
    local_state = jnp.einsum(
        "thd,tn->hdn",
        weighted,
        inputs_b,
        precision=high_precision,
        preferred_element_type=jnp.float32,
    )
    whole_decay = jnp.exp(cumulative[length - 1] - before[length - 1])
    starts_here = begin[length - 1] >= first
    cached_last = lax.dynamic_index_in_dim(ssm_cache, last_segment, 0, keepdims=False)
    chain_state = local_state + jnp.where(
        starts_here, whole_decay[:, None, None] * cached_last, 0.0
    )
    chain_decay = jnp.where(starts_here, jnp.zeros_like(whole_decay), whole_decay)

    scan_decay, scan_state = advance((chain_decay, chain_state))
    distance = 1
    while distance <= reach and distance < seq_count:
        prior_decay, prior_state = shifted_2((scan_decay, scan_state), "seq", distance)
        scan_state = scan_decay[:, None, None] * prior_state + scan_state
        scan_decay = scan_decay * prior_decay
        scan_decay, scan_state = advance((scan_decay, scan_state))
        distance *= 2
    carried = advance(shifted_2(scan_state, "seq", 1))
    continuing = position[0] > 0
    replace = (jnp.arange(prompts, dtype=jnp.int32) == segment[0]) & continuing
    initial = jnp.where(replace[:, None, None, None], carried[None], ssm_cache)
    selected = (onehot[:, :, None].astype(jnp.bfloat16) * inputs_c[:, None, :]).reshape(
        length, prompts * state_size
    )
    table = jnp.transpose(initial, (0, 3, 1, 2)).reshape(prompts * state_size, heads * head_size)
    init_out = (
        jnp.dot(
            selected, table, precision=high_precision, preferred_element_type=jnp.float32
        ).reshape(length, heads, head_size)
        * from_begin[:, :, None]
    )
    mixed = intra_out + init_out + d_skip[None, :, None] * values
    gated = (
        mixed * jax.nn.silu(z_in.astype(jnp.float32).reshape(length, heads, head_size))
    ).reshape(length, heads * head_size)
    squares = lax.psum(jnp.sum(gated * gated, axis=1), "tp")
    width = gated.shape[1] * lax.axis_size("tp")
    normed = (gated * lax.rsqrt(squares / width + EPS)[:, None] * norm_gain[None, :]).astype(
        jnp.bfloat16
    )
    normed = advance(normed)
    summed = lax.psum_scatter(
        jnp.dot(normed, out_weight, preferred_element_type=jnp.float32),
        "tp",
        scatter_dimension=0,
        tiled=True,
    )
    hidden = (residual.astype(jnp.float32) + summed).astype(jnp.bfloat16)
    level = hidden.astype(jnp.float32)
    attn_in = (
        level * lax.rsqrt(jnp.mean(level * level, axis=1, keepdims=True) + EPS) * attn_gain[None, :]
    ).astype(jnp.bfloat16)
    piece = lax.all_gather(attn_in, "tp", axis=0, tiled=True)
    low = jnp.dot(piece, q_down, preferred_element_type=jnp.float32).astype(jnp.bfloat16)
    query = (
        jnp.dot(piece, q_weight, preferred_element_type=jnp.float32)
        + jnp.dot(low, q_up, preferred_element_type=jnp.float32)
    ).astype(jnp.bfloat16)
    count_heads = query.shape[1] // HA

    def piece_mask(query_index, query_segment, offset, causal):
        key_index = (seq_index + offset) * length + jnp.arange(length, dtype=jnp.int32)
        key_segment, _, key_valid, _ = locate(lengths, key_index)
        allowed = key_valid[None, :] & (key_segment[None, :] == query_segment[:, None])
        if causal:
            allowed = allowed & (key_index[None, :] <= query_index[:, None])
        return allowed

    cache_pieces = [(cache_keys, cache_values, 0)]
    new_pieces = [(new_keys, new_values, 0)]
    while relay_steps:
        advance(())
    for distance in range(1, reach + 1):
        behind = behind_pieces[distance]
        cache_pieces.append((behind[0], behind[1], -distance))
        new_pieces.append((behind[2], behind[3], -distance))
        forward = forward_pieces[distance]
        cache_pieces.append((forward[0], forward[1], distance))
    all_keys = jnp.concatenate(
        [entry[0] for entry in cache_pieces] + [entry[0] for entry in new_pieces], axis=0
    )
    all_values = jnp.concatenate(
        [entry[1] for entry in cache_pieces] + [entry[1] for entry in new_pieces], axis=0
    )
    mask = jnp.concatenate(
        [piece_mask(local_index, segment, entry[2], False) for entry in cache_pieces]
        + [piece_mask(local_index, segment, entry[2], True) for entry in new_pieces],
        axis=1,
    )
    scale = 1.0 / HA**0.5

    def attend(head):
        column = head * HA
        query_head = lax.dynamic_slice_in_dim(query, column, HA, 1)
        key_head = lax.dynamic_slice_in_dim(all_keys, column, HA, 1)
        value_head = lax.dynamic_slice_in_dim(all_values, column, HA, 1)
        scores = (
            lax.dot_general(
                query_head, key_head, (((1,), (1,)), ((), ())), preferred_element_type=jnp.float32
            )
            * scale
        )
        scores = jnp.where(mask, scores, NEG)
        top = jnp.max(scores, axis=1, keepdims=True)
        weights = jnp.exp(scores - top)
        probs = (weights / jnp.sum(weights, axis=1, keepdims=True)).astype(jnp.bfloat16)
        return jnp.dot(probs, value_head, preferred_element_type=jnp.float32).astype(jnp.bfloat16)

    per_head = lax.map(attend, jnp.arange(count_heads, dtype=jnp.int32))
    attended = jnp.transpose(per_head, (1, 0, 2)).reshape(length, count_heads * HA)
    return (hidden, attended)


def solution(mesh):
    in_specs = (
        P(("seq", "tp"), None),
        P("seq", "tp"),
        P("seq", "tp"),
        P("seq", None),
        P("seq", "tp"),
        P(None, "tp"),
        P(),
        P(None, None, "tp"),
        P(),
        P(None, "tp", None, None),
        P("tp"),
        P("tp"),
        P("tp"),
        P("tp"),
        P("tp", None),
        P(),
        P(None, "tp"),
        P(),
        P(None, "tp"),
        P("seq", "tp"),
        P("seq", "tp"),
        P("seq", "tp"),
        P("seq", "tp"),
        P(),
    )
    out_specs = (P(("seq", "tp"), None), P("seq", "tp"))
    return jax.shard_map(
        per_device, mesh=mesh, in_specs=in_specs, out_specs=out_specs, check_vma=False
    )
```

```python
import jax
import jax.numpy as jnp
from jax import lax
from jax.sharding import PartitionSpec as P

HA = 224


EPS = 1e-05
NEG = -1e30


def shifted_2(value, axis, steps):
    count = lax.axis_size(axis)
    initial, last = (max(0, -steps), min(count, count - steps))
    return lax.ppermute(value, axis, [(source, source + steps) for source in range(initial, last)])


def locate(lengths, index):
    ends = jnp.cumsum(lengths)
    starts = ends - lengths
    count = lengths.shape[0]
    segment = jnp.sum((index[:, None] >= ends[None, :]).astype(jnp.int32), axis=1)
    segment = jnp.minimum(segment, count - 1)
    onehot = segment[:, None] == jnp.arange(count, dtype=jnp.int32)[None, :]
    begin = jnp.sum(jnp.where(onehot, starts[None, :], 0), axis=1)
    valid = (index >= 0) & (index < ends[count - 1])
    return (segment, begin, valid, onehot)


def convolve(inputs, border, cache, weight, position, onehot):
    taps = weight.shape[0]
    length = inputs.shape[0]
    extended = jnp.concatenate([border, inputs], axis=0)
    picks = onehot.astype(jnp.bfloat16)
    cached_rows = [
        jnp.dot(picks, cache[:, slot, :], preferred_element_type=jnp.float32)
        for slot in range(taps - 1)
    ]
    result = weight[0][None, :] * inputs.astype(jnp.float32)
    for lag in range(1, taps):
        shifted = extended[taps - 1 - lag : taps - 1 - lag + length].astype(jnp.float32)
        slot_index = taps - 1 + position - lag
        fallback = jnp.zeros_like(shifted)
        for slot in range(taps - 1):
            fallback = jnp.where((slot_index == slot)[:, None], cached_rows[slot], fallback)
        shifted = jnp.where((position >= lag)[:, None], shifted, fallback)
        result = result + weight[lag][None, :] * shifted
    return jax.nn.silu(result).astype(jnp.bfloat16)


def per_device(
    residual,
    x_in,
    z_in,
    bc_in,
    dt_in,
    conv_x_weight,
    conv_bc_weight,
    conv_x_cache,
    conv_bc_cache,
    ssm_cache,
    dt_bias,
    a_log,
    d_skip,
    norm_gain,
    out_weight,
    attn_gain,
    q_weight,
    q_down,
    q_up,
    cache_keys,
    cache_values,
    new_keys,
    new_values,
    lengths,
):
    high_precision = lax.Precision.HIGH
    length = x_in.shape[0]
    taps = conv_x_weight.shape[0]
    seq_index = lax.axis_index("seq")
    seq_count = lax.axis_size("seq")
    reach = seq_count // 4 + 1
    first = seq_index * length
    long_hop = reach + 1
    behind_pieces = [jnp.stack([cache_keys, cache_values, new_keys, new_values])] * (reach + 1)
    forward_pieces = [jnp.stack([cache_keys, cache_values])] * (reach + 1)
    relay_steps = []
    for distance in range(1, long_hop):
        relay_steps.append([(distance, distance - 1, 1)])
    for distance in range(long_hop, reach + 1):
        relay_steps[distance - long_hop].append((distance, distance - long_hop, long_hop))

    def advance(values):
        if not relay_steps:
            return values
        moves = relay_steps.pop(0)
        sent = []
        for distance, source, steps in moves:
            sent.append(
                (
                    shifted_2(behind_pieces[source], "seq", steps),
                    shifted_2(forward_pieces[source], "seq", -steps),
                )
            )
        sent, values = lax.optimization_barrier((sent, values))
        for (distance, _, _), (behind, forward) in zip(moves, sent):
            behind_pieces[distance] = behind
            forward_pieces[distance] = forward
        return values

    local_index = first + jnp.arange(length, dtype=jnp.int32)
    segment, begin, valid, onehot = locate(lengths, local_index)
    position = local_index - begin
    x_border, bc_border = shifted_2(
        (x_in[length - taps + 1 :], bc_in[length - taps + 1 :]), "seq", 1
    )
    x_conv = convolve(x_in, x_border, conv_x_cache, conv_x_weight, position, onehot)
    bc_conv = convolve(bc_in, bc_border, conv_bc_cache, conv_bc_weight, position, onehot)
    x_conv, bc_conv = advance((x_conv, bc_conv))
    heads = dt_bias.shape[0]
    state_size = bc_in.shape[1] // 2
    head_size = x_in.shape[1] // heads
    prompts = lengths.shape[0]
    values_bf = x_conv.reshape(length, heads, head_size)
    values = x_conv.astype(jnp.float32).reshape(length, heads, head_size)
    inputs_b = bc_conv[:, :state_size]
    inputs_c = bc_conv[:, state_size:]
    step = jax.nn.softplus(dt_in + dt_bias[None, :])
    log_decay = -step * jnp.exp(a_log)[None, :]
    cumulative = jnp.cumsum(log_decay, axis=0)
    local_begin = jnp.maximum(begin - first, 0)
    before = jnp.take(cumulative - log_decay, local_begin, axis=0)
    from_begin = jnp.exp(cumulative - before)
    block = min(length, 512)
    pair_scores = jnp.dot(inputs_c, inputs_b.T, preferred_element_type=jnp.float32)
    cumulative_t = cumulative.T
    step_t = step.T
    order = jnp.arange(length, dtype=jnp.int32)

    def intra(block_start):
        query_rows = block_start + jnp.arange(block, dtype=jnp.int32)
        same = (segment[:, None] == segment[None, :]) & (query_rows[:, None] >= order[None, :])
        gap = cumulative_t[:, :, None] - cumulative_t[:, None, :]
        factor = jnp.where(same[None], jnp.exp(jnp.where(same[None], gap, 0.0)), 0.0)
        weights = factor * step_t[:, None, :] * pair_scores[None, :, :]
        return jnp.einsum(
            "hqs,shd->qhd",
            weights,
            values_bf,
            precision=high_precision,
            preferred_element_type=jnp.float32,
        )

    intra_out = lax.map(intra, jnp.arange(length // block, dtype=jnp.int32) * block).reshape(
        length, heads, head_size
    )
    last_segment = segment[length - 1]
    in_last = segment == last_segment
    tail_weight = (
        jnp.where(in_last[:, None], jnp.exp(cumulative[length - 1][None, :] - cumulative), 0.0)
        * step
    )
    weighted = tail_weight[:, :, None] * values
    local_state = jnp.einsum(
        "thd,tn->hdn",
        weighted,
        inputs_b,
        precision=high_precision,
        preferred_element_type=jnp.float32,
    )
    whole_decay = jnp.exp(cumulative[length - 1] - before[length - 1])
    starts_here = begin[length - 1] >= first
    cached_last = lax.dynamic_index_in_dim(ssm_cache, last_segment, 0, keepdims=False)
    chain_state = local_state + jnp.where(
        starts_here, whole_decay[:, None, None] * cached_last, 0.0
    )
    chain_decay = jnp.where(starts_here, jnp.zeros_like(whole_decay), whole_decay)

    scan_decay, scan_state = advance((chain_decay, chain_state))
    distance = 1
    while distance <= reach and distance < seq_count:
        prior_decay, prior_state = shifted_2((scan_decay, scan_state), "seq", distance)
        scan_state = scan_decay[:, None, None] * prior_state + scan_state
        scan_decay = scan_decay * prior_decay
        scan_decay, scan_state = advance((scan_decay, scan_state))
        distance *= 2
    carried = advance(shifted_2(scan_state, "seq", 1))
    continuing = position[0] > 0
    replace = (jnp.arange(prompts, dtype=jnp.int32) == segment[0]) & continuing
    initial = jnp.where(replace[:, None, None, None], carried[None], ssm_cache)
    selected = (onehot[:, :, None].astype(jnp.bfloat16) * inputs_c[:, None, :]).reshape(
        length, prompts * state_size
    )
    table = jnp.transpose(initial, (0, 3, 1, 2)).reshape(prompts * state_size, heads * head_size)
    init_out = (
        jnp.dot(
            selected, table, precision=high_precision, preferred_element_type=jnp.float32
        ).reshape(length, heads, head_size)
        * from_begin[:, :, None]
    )
    mixed = intra_out + init_out + d_skip[None, :, None] * values
    gated = (
        mixed * jax.nn.silu(z_in.astype(jnp.float32).reshape(length, heads, head_size))
    ).reshape(length, heads * head_size)
    gated = advance(gated)
    squares = lax.psum(jnp.sum(gated * gated, axis=1), "tp")
    width = gated.shape[1] * lax.axis_size("tp")
    normed = (gated * lax.rsqrt(squares / width + EPS)[:, None] * norm_gain[None, :]).astype(
        jnp.bfloat16
    )
    normed = advance(normed)
    summed = lax.psum_scatter(
        jnp.dot(normed, out_weight, preferred_element_type=jnp.float32),
        "tp",
        scatter_dimension=0,
        tiled=True,
    )
    hidden = (residual.astype(jnp.float32) + summed).astype(jnp.bfloat16)
    level = hidden.astype(jnp.float32)
    attn_in = (
        level * lax.rsqrt(jnp.mean(level * level, axis=1, keepdims=True) + EPS) * attn_gain[None, :]
    ).astype(jnp.bfloat16)
    piece = lax.all_gather(attn_in, "tp", axis=0, tiled=True)
    low = jnp.dot(piece, q_down, preferred_element_type=jnp.float32).astype(jnp.bfloat16)
    query = (
        jnp.dot(piece, q_weight, preferred_element_type=jnp.float32)
        + jnp.dot(low, q_up, preferred_element_type=jnp.float32)
    ).astype(jnp.bfloat16)
    count_heads = query.shape[1] // HA

    def piece_mask(query_index, query_segment, offset, causal):
        key_index = (seq_index + offset) * length + jnp.arange(length, dtype=jnp.int32)
        key_segment, _, key_valid, _ = locate(lengths, key_index)
        allowed = key_valid[None, :] & (key_segment[None, :] == query_segment[:, None])
        if causal:
            allowed = allowed & (key_index[None, :] <= query_index[:, None])
        return allowed

    cache_pieces = [(cache_keys, cache_values, 0)]
    new_pieces = [(new_keys, new_values, 0)]
    while relay_steps:
        advance(())
    for distance in range(1, reach + 1):
        behind = behind_pieces[distance]
        cache_pieces.append((behind[0], behind[1], -distance))
        new_pieces.append((behind[2], behind[3], -distance))
        forward = forward_pieces[distance]
        cache_pieces.append((forward[0], forward[1], distance))
    all_keys = jnp.concatenate(
        [entry[0] for entry in cache_pieces] + [entry[0] for entry in new_pieces], axis=0
    )
    all_values = jnp.concatenate(
        [entry[1] for entry in cache_pieces] + [entry[1] for entry in new_pieces], axis=0
    )
    mask = jnp.concatenate(
        [piece_mask(local_index, segment, entry[2], False) for entry in cache_pieces]
        + [piece_mask(local_index, segment, entry[2], True) for entry in new_pieces],
        axis=1,
    )
    scale = 1.0 / HA**0.5

    def attend(head):
        column = head * HA
        query_head = lax.dynamic_slice_in_dim(query, column, HA, 1)
        key_head = lax.dynamic_slice_in_dim(all_keys, column, HA, 1)
        value_head = lax.dynamic_slice_in_dim(all_values, column, HA, 1)
        scores = (
            lax.dot_general(
                query_head, key_head, (((1,), (1,)), ((), ())), preferred_element_type=jnp.float32
            )
            * scale
        )
        scores = jnp.where(mask, scores, NEG)
        top = jnp.max(scores, axis=1, keepdims=True)
        weights = jnp.exp(scores - top)
        probs = (weights / jnp.sum(weights, axis=1, keepdims=True)).astype(jnp.bfloat16)
        return jnp.dot(probs, value_head, preferred_element_type=jnp.float32).astype(jnp.bfloat16)

    per_head = lax.map(attend, jnp.arange(count_heads, dtype=jnp.int32))
    attended = jnp.transpose(per_head, (1, 0, 2)).reshape(length, count_heads * HA)
    return (hidden, attended)


def solution(mesh):
    in_specs = (
        P(("seq", "tp"), None),
        P("seq", "tp"),
        P("seq", "tp"),
        P("seq", None),
        P("seq", "tp"),
        P(None, "tp"),
        P(),
        P(None, None, "tp"),
        P(),
        P(None, "tp", None, None),
        P("tp"),
        P("tp"),
        P("tp"),
        P("tp"),
        P("tp", None),
        P(),
        P(None, "tp"),
        P(),
        P(None, "tp"),
        P("seq", "tp"),
        P("seq", "tp"),
        P("seq", "tp"),
        P("seq", "tp"),
        P(),
    )
    out_specs = (P(("seq", "tp"), None), P("seq", "tp"))
    return jax.shard_map(
        per_device, mesh=mesh, in_specs=in_specs, out_specs=out_specs, check_vma=False
    )
```

```python
import jax
import jax.numpy as jnp
from jax import lax
from jax.sharding import PartitionSpec as P

HA = 224


EPS = 1e-05
NEG = -1e30


def shifted_2(value, axis, steps):
    count = lax.axis_size(axis)
    initial, last = (max(0, -steps), min(count, count - steps))
    return lax.ppermute(value, axis, [(source, source + steps) for source in range(initial, last)])


def locate(lengths, index):
    ends = jnp.cumsum(lengths)
    starts = ends - lengths
    count = lengths.shape[0]
    segment = jnp.sum((index[:, None] >= ends[None, :]).astype(jnp.int32), axis=1)
    segment = jnp.minimum(segment, count - 1)
    onehot = segment[:, None] == jnp.arange(count, dtype=jnp.int32)[None, :]
    begin = jnp.sum(jnp.where(onehot, starts[None, :], 0), axis=1)
    valid = (index >= 0) & (index < ends[count - 1])
    return (segment, begin, valid, onehot)


def convolve(inputs, border, cache, weight, position, onehot):
    taps = weight.shape[0]
    length = inputs.shape[0]
    extended = jnp.concatenate([border, inputs], axis=0)
    picks = onehot.astype(jnp.bfloat16)
    cached_rows = [
        jnp.dot(picks, cache[:, slot, :], preferred_element_type=jnp.float32)
        for slot in range(taps - 1)
    ]
    result = weight[0][None, :] * inputs.astype(jnp.float32)
    for lag in range(1, taps):
        shifted = extended[taps - 1 - lag : taps - 1 - lag + length].astype(jnp.float32)
        slot_index = taps - 1 + position - lag
        fallback = jnp.zeros_like(shifted)
        for slot in range(taps - 1):
            fallback = jnp.where((slot_index == slot)[:, None], cached_rows[slot], fallback)
        shifted = jnp.where((position >= lag)[:, None], shifted, fallback)
        result = result + weight[lag][None, :] * shifted
    return jax.nn.silu(result).astype(jnp.bfloat16)


def per_device(
    residual,
    x_in,
    z_in,
    bc_in,
    dt_in,
    conv_x_weight,
    conv_bc_weight,
    conv_x_cache,
    conv_bc_cache,
    ssm_cache,
    dt_bias,
    a_log,
    d_skip,
    norm_gain,
    out_weight,
    attn_gain,
    q_weight,
    q_down,
    q_up,
    cache_keys,
    cache_values,
    new_keys,
    new_values,
    lengths,
):
    high_precision = lax.Precision.HIGH
    length = x_in.shape[0]
    taps = conv_x_weight.shape[0]
    seq_index = lax.axis_index("seq")
    seq_count = lax.axis_size("seq")
    reach = seq_count // 4 + 1
    first = seq_index * length
    long_hop = reach + 1
    tied_steps = 5
    behind_pieces = [jnp.stack([cache_keys, cache_values, new_keys, new_values])] * (reach + 1)
    forward_pieces = [jnp.stack([cache_keys, cache_values])] * (reach + 1)
    relay_steps = []
    for distance in range(1, long_hop):
        relay_steps.append([(distance, distance - 1, 1)])
    for distance in range(long_hop, reach + 1):
        relay_steps[distance - long_hop].append((distance, distance - long_hop, long_hop))

    def advance(values, tied=True):
        if not relay_steps or (tied and len(relay_steps) <= reach - tied_steps):
            return values
        moves = relay_steps.pop(0)
        sent = []
        for distance, source, steps in moves:
            sent.append(
                (
                    shifted_2(behind_pieces[source], "seq", steps),
                    shifted_2(forward_pieces[source], "seq", -steps),
                )
            )
        sent, values = lax.optimization_barrier((sent, values))
        for (distance, _, _), (behind, forward) in zip(moves, sent):
            behind_pieces[distance] = behind
            forward_pieces[distance] = forward
        return values

    local_index = first + jnp.arange(length, dtype=jnp.int32)
    segment, begin, valid, onehot = locate(lengths, local_index)
    position = local_index - begin
    x_border, bc_border = shifted_2(
        (x_in[length - taps + 1 :], bc_in[length - taps + 1 :]), "seq", 1
    )
    x_conv = convolve(x_in, x_border, conv_x_cache, conv_x_weight, position, onehot)
    bc_conv = convolve(bc_in, bc_border, conv_bc_cache, conv_bc_weight, position, onehot)
    x_conv, bc_conv = advance((x_conv, bc_conv))
    heads = dt_bias.shape[0]
    state_size = bc_in.shape[1] // 2
    head_size = x_in.shape[1] // heads
    prompts = lengths.shape[0]
    values_bf = x_conv.reshape(length, heads, head_size)
    values = x_conv.astype(jnp.float32).reshape(length, heads, head_size)
    inputs_b = bc_conv[:, :state_size]
    inputs_c = bc_conv[:, state_size:]
    step = jax.nn.softplus(dt_in + dt_bias[None, :])
    log_decay = -step * jnp.exp(a_log)[None, :]
    cumulative = jnp.cumsum(log_decay, axis=0)
    local_begin = jnp.maximum(begin - first, 0)
    before = jnp.take(cumulative - log_decay, local_begin, axis=0)
    from_begin = jnp.exp(cumulative - before)
    block = min(length, 512)
    pair_scores = jnp.dot(inputs_c, inputs_b.T, preferred_element_type=jnp.float32)
    cumulative_t = cumulative.T
    step_t = step.T
    order = jnp.arange(length, dtype=jnp.int32)

    def intra(block_start):
        query_rows = block_start + jnp.arange(block, dtype=jnp.int32)
        same = (segment[:, None] == segment[None, :]) & (query_rows[:, None] >= order[None, :])
        gap = cumulative_t[:, :, None] - cumulative_t[:, None, :]
        factor = jnp.where(same[None], jnp.exp(jnp.where(same[None], gap, 0.0)), 0.0)
        weights = factor * step_t[:, None, :] * pair_scores[None, :, :]
        return jnp.einsum(
            "hqs,shd->qhd",
            weights,
            values_bf,
            precision=high_precision,
            preferred_element_type=jnp.float32,
        )

    intra_out = lax.map(intra, jnp.arange(length // block, dtype=jnp.int32) * block).reshape(
        length, heads, head_size
    )
    last_segment = segment[length - 1]
    in_last = segment == last_segment
    tail_weight = (
        jnp.where(in_last[:, None], jnp.exp(cumulative[length - 1][None, :] - cumulative), 0.0)
        * step
    )
    weighted = tail_weight[:, :, None] * values
    local_state = jnp.einsum(
        "thd,tn->hdn",
        weighted,
        inputs_b,
        precision=high_precision,
        preferred_element_type=jnp.float32,
    )
    whole_decay = jnp.exp(cumulative[length - 1] - before[length - 1])
    starts_here = begin[length - 1] >= first
    cached_last = lax.dynamic_index_in_dim(ssm_cache, last_segment, 0, keepdims=False)
    chain_state = local_state + jnp.where(
        starts_here, whole_decay[:, None, None] * cached_last, 0.0
    )
    chain_decay = jnp.where(starts_here, jnp.zeros_like(whole_decay), whole_decay)

    scan_decay, scan_state = advance((chain_decay, chain_state))
    distance = 1
    while distance <= reach and distance < seq_count:
        prior_decay, prior_state = shifted_2((scan_decay, scan_state), "seq", distance)
        scan_state = scan_decay[:, None, None] * prior_state + scan_state
        scan_decay = scan_decay * prior_decay
        scan_decay, scan_state = advance((scan_decay, scan_state))
        distance *= 2
    carried = advance(shifted_2(scan_state, "seq", 1))
    continuing = position[0] > 0
    replace = (jnp.arange(prompts, dtype=jnp.int32) == segment[0]) & continuing
    initial = jnp.where(replace[:, None, None, None], carried[None], ssm_cache)
    selected = (onehot[:, :, None].astype(jnp.bfloat16) * inputs_c[:, None, :]).reshape(
        length, prompts * state_size
    )
    table = jnp.transpose(initial, (0, 3, 1, 2)).reshape(prompts * state_size, heads * head_size)
    init_out = (
        jnp.dot(
            selected, table, precision=high_precision, preferred_element_type=jnp.float32
        ).reshape(length, heads, head_size)
        * from_begin[:, :, None]
    )
    mixed = intra_out + init_out + d_skip[None, :, None] * values
    gated = (
        mixed * jax.nn.silu(z_in.astype(jnp.float32).reshape(length, heads, head_size))
    ).reshape(length, heads * head_size)
    gated = advance(gated)
    squares = lax.psum(jnp.sum(gated * gated, axis=1), "tp")
    width = gated.shape[1] * lax.axis_size("tp")
    normed = (gated * lax.rsqrt(squares / width + EPS)[:, None] * norm_gain[None, :]).astype(
        jnp.bfloat16
    )
    normed = advance(normed)
    summed = lax.psum_scatter(
        jnp.dot(normed, out_weight, preferred_element_type=jnp.float32),
        "tp",
        scatter_dimension=0,
        tiled=True,
    )
    hidden = (residual.astype(jnp.float32) + summed).astype(jnp.bfloat16)
    level = hidden.astype(jnp.float32)
    attn_in = (
        level * lax.rsqrt(jnp.mean(level * level, axis=1, keepdims=True) + EPS) * attn_gain[None, :]
    ).astype(jnp.bfloat16)
    piece = lax.all_gather(attn_in, "tp", axis=0, tiled=True)
    low = jnp.dot(piece, q_down, preferred_element_type=jnp.float32).astype(jnp.bfloat16)
    query = (
        jnp.dot(piece, q_weight, preferred_element_type=jnp.float32)
        + jnp.dot(low, q_up, preferred_element_type=jnp.float32)
    ).astype(jnp.bfloat16)
    count_heads = query.shape[1] // HA

    def piece_mask(query_index, query_segment, offset, causal):
        key_index = (seq_index + offset) * length + jnp.arange(length, dtype=jnp.int32)
        key_segment, _, key_valid, _ = locate(lengths, key_index)
        allowed = key_valid[None, :] & (key_segment[None, :] == query_segment[:, None])
        if causal:
            allowed = allowed & (key_index[None, :] <= query_index[:, None])
        return allowed

    cache_pieces = [(cache_keys, cache_values, 0)]
    new_pieces = [(new_keys, new_values, 0)]
    while relay_steps:
        advance((), tied=False)
    for distance in range(1, reach + 1):
        behind = behind_pieces[distance]
        cache_pieces.append((behind[0], behind[1], -distance))
        new_pieces.append((behind[2], behind[3], -distance))
        forward = forward_pieces[distance]
        cache_pieces.append((forward[0], forward[1], distance))
    all_keys = jnp.concatenate(
        [entry[0] for entry in cache_pieces] + [entry[0] for entry in new_pieces], axis=0
    )
    all_values = jnp.concatenate(
        [entry[1] for entry in cache_pieces] + [entry[1] for entry in new_pieces], axis=0
    )
    mask = jnp.concatenate(
        [piece_mask(local_index, segment, entry[2], False) for entry in cache_pieces]
        + [piece_mask(local_index, segment, entry[2], True) for entry in new_pieces],
        axis=1,
    )
    scale = 1.0 / HA**0.5

    def attend(head):
        column = head * HA
        query_head = lax.dynamic_slice_in_dim(query, column, HA, 1)
        key_head = lax.dynamic_slice_in_dim(all_keys, column, HA, 1)
        value_head = lax.dynamic_slice_in_dim(all_values, column, HA, 1)
        scores = (
            lax.dot_general(
                query_head, key_head, (((1,), (1,)), ((), ())), preferred_element_type=jnp.float32
            )
            * scale
        )
        scores = jnp.where(mask, scores, NEG)
        top = jnp.max(scores, axis=1, keepdims=True)
        weights = jnp.exp(scores - top)
        probs = (weights / jnp.sum(weights, axis=1, keepdims=True)).astype(jnp.bfloat16)
        return jnp.dot(probs, value_head, preferred_element_type=jnp.float32).astype(jnp.bfloat16)

    per_head = lax.map(attend, jnp.arange(count_heads, dtype=jnp.int32))
    attended = jnp.transpose(per_head, (1, 0, 2)).reshape(length, count_heads * HA)
    return (hidden, attended)


def solution(mesh):
    in_specs = (
        P(("seq", "tp"), None),
        P("seq", "tp"),
        P("seq", "tp"),
        P("seq", None),
        P("seq", "tp"),
        P(None, "tp"),
        P(),
        P(None, None, "tp"),
        P(),
        P(None, "tp", None, None),
        P("tp"),
        P("tp"),
        P("tp"),
        P("tp"),
        P("tp", None),
        P(),
        P(None, "tp"),
        P(),
        P(None, "tp"),
        P("seq", "tp"),
        P("seq", "tp"),
        P("seq", "tp"),
        P("seq", "tp"),
        P(),
    )
    out_specs = (P(("seq", "tp"), None), P("seq", "tp"))
    return jax.shard_map(
        per_device, mesh=mesh, in_specs=in_specs, out_specs=out_specs, check_vma=False
    )
```

```python
import jax
import jax.numpy as jnp
from jax import lax
from jax.sharding import PartitionSpec as P

HA = 224


EPS = 1e-05
NEG = -1e30


def shifted_2(value, axis, steps):
    count = lax.axis_size(axis)
    initial, last = (max(0, -steps), min(count, count - steps))
    return lax.ppermute(value, axis, [(source, source + steps) for source in range(initial, last)])


def locate(lengths, index):
    ends = jnp.cumsum(lengths)
    starts = ends - lengths
    count = lengths.shape[0]
    segment = jnp.sum((index[:, None] >= ends[None, :]).astype(jnp.int32), axis=1)
    segment = jnp.minimum(segment, count - 1)
    onehot = segment[:, None] == jnp.arange(count, dtype=jnp.int32)[None, :]
    begin = jnp.sum(jnp.where(onehot, starts[None, :], 0), axis=1)
    valid = (index >= 0) & (index < ends[count - 1])
    return (segment, begin, valid, onehot)


def convolve(inputs, border, cache, weight, position, onehot):
    taps = weight.shape[0]
    length = inputs.shape[0]
    extended = jnp.concatenate([border, inputs], axis=0)
    picks = onehot.astype(jnp.bfloat16)
    cached_rows = [
        jnp.dot(picks, cache[:, slot, :], preferred_element_type=jnp.float32)
        for slot in range(taps - 1)
    ]
    result = weight[0][None, :] * inputs.astype(jnp.float32)
    for lag in range(1, taps):
        shifted = extended[taps - 1 - lag : taps - 1 - lag + length].astype(jnp.float32)
        slot_index = taps - 1 + position - lag
        fallback = jnp.zeros_like(shifted)
        for slot in range(taps - 1):
            fallback = jnp.where((slot_index == slot)[:, None], cached_rows[slot], fallback)
        shifted = jnp.where((position >= lag)[:, None], shifted, fallback)
        result = result + weight[lag][None, :] * shifted
    return jax.nn.silu(result).astype(jnp.bfloat16)


def per_device(
    residual,
    x_in,
    z_in,
    bc_in,
    dt_in,
    conv_x_weight,
    conv_bc_weight,
    conv_x_cache,
    conv_bc_cache,
    ssm_cache,
    dt_bias,
    a_log,
    d_skip,
    norm_gain,
    out_weight,
    attn_gain,
    q_weight,
    q_down,
    q_up,
    cache_keys,
    cache_values,
    new_keys,
    new_values,
    lengths,
):
    high_precision = lax.Precision.HIGH
    length = x_in.shape[0]
    taps = conv_x_weight.shape[0]
    seq_index = lax.axis_index("seq")
    seq_count = lax.axis_size("seq")
    reach = seq_count // 4 + 1
    first = seq_index * length
    long_hop = reach + 1
    tied_steps = 5
    behind_pieces = [jnp.stack([cache_keys, cache_values, new_keys, new_values])] * (reach + 1)
    forward_pieces = [jnp.stack([cache_keys, cache_values])] * (reach + 1)
    relay_steps = []
    for distance in range(1, long_hop):
        relay_steps.append([(distance, distance - 1, 1)])
    for distance in range(long_hop, reach + 1):
        relay_steps[distance - long_hop].append((distance, distance - long_hop, long_hop))

    def advance(values, tied=True, after=None):
        if not relay_steps or (tied and len(relay_steps) <= reach - tied_steps):
            return values
        moves = relay_steps.pop(0)
        sent = []
        for distance, source, steps in moves:
            behind, forward = behind_pieces[source], forward_pieces[source]
            if after is not None:
                behind, forward, _ = lax.optimization_barrier((behind, forward, after))
            sent.append((shifted_2(behind, "seq", steps), shifted_2(forward, "seq", -steps)))
        sent, values = lax.optimization_barrier((sent, values))
        for (distance, _, _), (behind, forward) in zip(moves, sent):
            behind_pieces[distance] = behind
            forward_pieces[distance] = forward
        return values

    local_index = first + jnp.arange(length, dtype=jnp.int32)
    segment, begin, valid, onehot = locate(lengths, local_index)
    position = local_index - begin
    x_border, bc_border = shifted_2(
        (x_in[length - taps + 1 :], bc_in[length - taps + 1 :]), "seq", 1
    )
    x_conv = convolve(x_in, x_border, conv_x_cache, conv_x_weight, position, onehot)
    bc_conv = convolve(bc_in, bc_border, conv_bc_cache, conv_bc_weight, position, onehot)
    x_conv, bc_conv = advance((x_conv, bc_conv))
    heads = dt_bias.shape[0]
    state_size = bc_in.shape[1] // 2
    head_size = x_in.shape[1] // heads
    prompts = lengths.shape[0]
    values_bf = x_conv.reshape(length, heads, head_size)
    values = x_conv.astype(jnp.float32).reshape(length, heads, head_size)
    inputs_b = bc_conv[:, :state_size]
    inputs_c = bc_conv[:, state_size:]
    step = jax.nn.softplus(dt_in + dt_bias[None, :])
    log_decay = -step * jnp.exp(a_log)[None, :]
    cumulative = jnp.cumsum(log_decay, axis=0)
    local_begin = jnp.maximum(begin - first, 0)
    before = jnp.take(cumulative - log_decay, local_begin, axis=0)
    from_begin = jnp.exp(cumulative - before)
    block = min(length, 512)
    pair_scores = jnp.dot(inputs_c, inputs_b.T, preferred_element_type=jnp.float32)
    cumulative_t = cumulative.T
    step_t = step.T
    order = jnp.arange(length, dtype=jnp.int32)

    def intra(block_start):
        query_rows = block_start + jnp.arange(block, dtype=jnp.int32)
        same = (segment[:, None] == segment[None, :]) & (query_rows[:, None] >= order[None, :])
        gap = cumulative_t[:, :, None] - cumulative_t[:, None, :]
        factor = jnp.where(same[None], jnp.exp(jnp.where(same[None], gap, 0.0)), 0.0)
        weights = factor * step_t[:, None, :] * pair_scores[None, :, :]
        return jnp.einsum(
            "hqs,shd->qhd",
            weights,
            values_bf,
            precision=high_precision,
            preferred_element_type=jnp.float32,
        )

    intra_out = lax.map(intra, jnp.arange(length // block, dtype=jnp.int32) * block).reshape(
        length, heads, head_size
    )
    last_segment = segment[length - 1]
    in_last = segment == last_segment
    tail_weight = (
        jnp.where(in_last[:, None], jnp.exp(cumulative[length - 1][None, :] - cumulative), 0.0)
        * step
    )
    weighted = tail_weight[:, :, None] * values
    local_state = jnp.einsum(
        "thd,tn->hdn",
        weighted,
        inputs_b,
        precision=high_precision,
        preferred_element_type=jnp.float32,
    )
    whole_decay = jnp.exp(cumulative[length - 1] - before[length - 1])
    starts_here = begin[length - 1] >= first
    cached_last = lax.dynamic_index_in_dim(ssm_cache, last_segment, 0, keepdims=False)
    chain_state = local_state + jnp.where(
        starts_here, whole_decay[:, None, None] * cached_last, 0.0
    )
    chain_decay = jnp.where(starts_here, jnp.zeros_like(whole_decay), whole_decay)

    scan_decay, scan_state = advance((chain_decay, chain_state))
    distance = 1
    while distance <= reach and distance < seq_count:
        prior_decay, prior_state = shifted_2((scan_decay, scan_state), "seq", distance)
        scan_state = scan_decay[:, None, None] * prior_state + scan_state
        scan_decay = scan_decay * prior_decay
        scan_decay, scan_state = advance((scan_decay, scan_state))
        distance *= 2
    carried = advance(shifted_2(scan_state, "seq", 1))
    continuing = position[0] > 0
    first_rows = (segment == segment[0]) & continuing
    cached_rows = onehot & ~first_rows[:, None]
    selected = (cached_rows[:, :, None].astype(jnp.bfloat16) * inputs_c[:, None, :]).reshape(
        length, prompts * state_size
    )
    table = jnp.transpose(ssm_cache, (0, 3, 1, 2)).reshape(prompts * state_size, heads * head_size)
    carried_table = jnp.transpose(carried, (2, 0, 1)).reshape(state_size, heads * head_size)
    from_cache = jnp.dot(selected, table, precision=high_precision, preferred_element_type=jnp.float32)
    from_carried = jnp.dot(
        inputs_c, carried_table, precision=high_precision, preferred_element_type=jnp.float32
    )
    init_out = (
        jnp.where(first_rows[:, None], from_carried, from_cache).reshape(length, heads, head_size)
        * from_begin[:, :, None]
    )
    mixed = intra_out + init_out + d_skip[None, :, None] * values
    gated = (
        mixed * jax.nn.silu(z_in.astype(jnp.float32).reshape(length, heads, head_size))
    ).reshape(length, heads * head_size)
    gated = advance(gated)
    squares = lax.psum(jnp.sum(gated * gated, axis=1), "tp")
    width = gated.shape[1] * lax.axis_size("tp")
    normed = (gated * lax.rsqrt(squares / width + EPS)[:, None] * norm_gain[None, :]).astype(
        jnp.bfloat16
    )
    normed = advance(normed)
    summed = lax.psum_scatter(
        jnp.dot(normed, out_weight, preferred_element_type=jnp.float32),
        "tp",
        scatter_dimension=0,
        tiled=True,
    )
    hidden = (residual.astype(jnp.float32) + summed).astype(jnp.bfloat16)
    level = hidden.astype(jnp.float32)
    attn_in = (
        level * lax.rsqrt(jnp.mean(level * level, axis=1, keepdims=True) + EPS) * attn_gain[None, :]
    ).astype(jnp.bfloat16)
    piece = lax.all_gather(attn_in, "tp", axis=0, tiled=True)
    low = jnp.dot(piece, q_down, preferred_element_type=jnp.float32).astype(jnp.bfloat16)
    query = (
        jnp.dot(piece, q_weight, preferred_element_type=jnp.float32)
        + jnp.dot(low, q_up, preferred_element_type=jnp.float32)
    ).astype(jnp.bfloat16)
    count_heads = query.shape[1] // HA

    def piece_mask(query_index, query_segment, offset, causal):
        key_index = (seq_index + offset) * length + jnp.arange(length, dtype=jnp.int32)
        key_segment, _, key_valid, _ = locate(lengths, key_index)
        allowed = key_valid[None, :] & (key_segment[None, :] == query_segment[:, None])
        if causal:
            allowed = allowed & (key_index[None, :] <= query_index[:, None])
        return allowed

    cache_pieces = [(cache_keys, cache_values, 0)]
    new_pieces = [(new_keys, new_values, 0)]
    while relay_steps:
        advance((), tied=False, after=attn_in)
    for distance in range(1, reach + 1):
        behind = behind_pieces[distance]
        cache_pieces.append((behind[0], behind[1], -distance))
        new_pieces.append((behind[2], behind[3], -distance))
        forward = forward_pieces[distance]
        cache_pieces.append((forward[0], forward[1], distance))
    all_keys = jnp.concatenate(
        [entry[0] for entry in cache_pieces] + [entry[0] for entry in new_pieces], axis=0
    )
    all_values = jnp.concatenate(
        [entry[1] for entry in cache_pieces] + [entry[1] for entry in new_pieces], axis=0
    )
    mask = jnp.concatenate(
        [piece_mask(local_index, segment, entry[2], False) for entry in cache_pieces]
        + [piece_mask(local_index, segment, entry[2], True) for entry in new_pieces],
        axis=1,
    )
    scale = 1.0 / HA**0.5

    def attend(head):
        column = head * HA
        query_head = lax.dynamic_slice_in_dim(query, column, HA, 1)
        key_head = lax.dynamic_slice_in_dim(all_keys, column, HA, 1)
        value_head = lax.dynamic_slice_in_dim(all_values, column, HA, 1)
        scores = (
            lax.dot_general(
                query_head, key_head, (((1,), (1,)), ((), ())), preferred_element_type=jnp.float32
            )
            * scale
        )
        scores = jnp.where(mask, scores, NEG)
        top = jnp.max(scores, axis=1, keepdims=True)
        weights = jnp.exp(scores - top)
        probs = (weights / jnp.sum(weights, axis=1, keepdims=True)).astype(jnp.bfloat16)
        return jnp.dot(probs, value_head, preferred_element_type=jnp.float32).astype(jnp.bfloat16)

    per_head = lax.map(attend, jnp.arange(count_heads, dtype=jnp.int32))
    attended = jnp.transpose(per_head, (1, 0, 2)).reshape(length, count_heads * HA)
    return (hidden, attended)


def solution(mesh):
    in_specs = (
        P(("seq", "tp"), None),
        P("seq", "tp"),
        P("seq", "tp"),
        P("seq", None),
        P("seq", "tp"),
        P(None, "tp"),
        P(),
        P(None, None, "tp"),
        P(),
        P(None, "tp", None, None),
        P("tp"),
        P("tp"),
        P("tp"),
        P("tp"),
        P("tp", None),
        P(),
        P(None, "tp"),
        P(),
        P(None, "tp"),
        P("seq", "tp"),
        P("seq", "tp"),
        P("seq", "tp"),
        P("seq", "tp"),
        P(),
    )
    out_specs = (P(("seq", "tp"), None), P("seq", "tp"))
    return jax.shard_map(
        per_device, mesh=mesh, in_specs=in_specs, out_specs=out_specs, check_vma=False
    )
```

```python
import jax
import jax.numpy as jnp
from jax import lax
from jax.sharding import PartitionSpec as P

HA = 224


EPS = 1e-05
NEG = -1e30


def shifted_2(value, axis, steps):
    count = lax.axis_size(axis)
    initial, last = (max(0, -steps), min(count, count - steps))
    return lax.ppermute(value, axis, [(source, source + steps) for source in range(initial, last)])


def locate(lengths, index):
    ends = jnp.cumsum(lengths)
    starts = ends - lengths
    count = lengths.shape[0]
    segment = jnp.sum((index[:, None] >= ends[None, :]).astype(jnp.int32), axis=1)
    segment = jnp.minimum(segment, count - 1)
    onehot = segment[:, None] == jnp.arange(count, dtype=jnp.int32)[None, :]
    begin = jnp.sum(jnp.where(onehot, starts[None, :], 0), axis=1)
    valid = (index >= 0) & (index < ends[count - 1])
    return (segment, begin, valid, onehot)


def convolve(inputs, border, cache, weight, position, onehot):
    taps = weight.shape[0]
    length = inputs.shape[0]
    extended = jnp.concatenate([border, inputs], axis=0)
    picks = onehot.astype(jnp.bfloat16)
    cached_rows = [
        jnp.dot(picks, cache[:, slot, :], preferred_element_type=jnp.float32)
        for slot in range(taps - 1)
    ]
    result = weight[0][None, :] * inputs.astype(jnp.float32)
    for lag in range(1, taps):
        shifted = extended[taps - 1 - lag : taps - 1 - lag + length].astype(jnp.float32)
        slot_index = taps - 1 + position - lag
        fallback = jnp.zeros_like(shifted)
        for slot in range(taps - 1):
            fallback = jnp.where((slot_index == slot)[:, None], cached_rows[slot], fallback)
        shifted = jnp.where((position >= lag)[:, None], shifted, fallback)
        result = result + weight[lag][None, :] * shifted
    return jax.nn.silu(result).astype(jnp.bfloat16)


def per_device(
    residual,
    x_in,
    z_in,
    bc_in,
    dt_in,
    conv_x_weight,
    conv_bc_weight,
    conv_x_cache,
    conv_bc_cache,
    ssm_cache,
    dt_bias,
    a_log,
    d_skip,
    norm_gain,
    out_weight,
    attn_gain,
    q_weight,
    q_down,
    q_up,
    cache_keys,
    cache_values,
    new_keys,
    new_values,
    lengths,
):
    high_precision = lax.Precision.HIGH
    length = x_in.shape[0]
    taps = conv_x_weight.shape[0]
    seq_index = lax.axis_index("seq")
    seq_count = lax.axis_size("seq")
    reach = seq_count // 4 + 1
    first = seq_index * length
    residual_rows = lax.all_gather(residual, "tp", axis=0, tiled=True)
    long_hop = reach + 1
    tied_steps = 5
    behind_pieces = [jnp.stack([cache_keys, cache_values, new_keys, new_values])] * (reach + 1)
    forward_pieces = [jnp.stack([cache_keys, cache_values])] * (reach + 1)
    relay_steps = []
    for distance in range(1, long_hop):
        relay_steps.append([(distance, distance - 1, 1)])
    for distance in range(long_hop, reach + 1):
        relay_steps[distance - long_hop].append((distance, distance - long_hop, long_hop))

    def advance(values, tied=True):
        if not relay_steps or (tied and len(relay_steps) <= reach - tied_steps):
            return values
        moves = relay_steps.pop(0)
        sent = []
        for distance, source, steps in moves:
            sent.append(
                (
                    shifted_2(behind_pieces[source], "seq", steps),
                    shifted_2(forward_pieces[source], "seq", -steps),
                )
            )
        sent, values = lax.optimization_barrier((sent, values))
        for (distance, _, _), (behind, forward) in zip(moves, sent):
            behind_pieces[distance] = behind
            forward_pieces[distance] = forward
        return values

    local_index = first + jnp.arange(length, dtype=jnp.int32)
    segment, begin, valid, onehot = locate(lengths, local_index)
    position = local_index - begin
    x_border, bc_border = shifted_2(
        (x_in[length - taps + 1 :], bc_in[length - taps + 1 :]), "seq", 1
    )
    x_conv = convolve(x_in, x_border, conv_x_cache, conv_x_weight, position, onehot)
    bc_conv = convolve(bc_in, bc_border, conv_bc_cache, conv_bc_weight, position, onehot)
    x_conv, bc_conv = advance((x_conv, bc_conv))
    heads = dt_bias.shape[0]
    state_size = bc_in.shape[1] // 2
    head_size = x_in.shape[1] // heads
    prompts = lengths.shape[0]
    values_bf = x_conv.reshape(length, heads, head_size)
    values = x_conv.astype(jnp.float32).reshape(length, heads, head_size)
    inputs_b = bc_conv[:, :state_size]
    inputs_c = bc_conv[:, state_size:]
    step = jax.nn.softplus(dt_in + dt_bias[None, :])
    log_decay = -step * jnp.exp(a_log)[None, :]
    cumulative = jnp.cumsum(log_decay, axis=0)
    local_begin = jnp.maximum(begin - first, 0)
    before = jnp.take(cumulative - log_decay, local_begin, axis=0)
    from_begin = jnp.exp(cumulative - before)
    block = min(length, 512)
    pair_scores = jnp.dot(inputs_c, inputs_b.T, preferred_element_type=jnp.float32)
    cumulative_t = cumulative.T
    step_t = step.T
    order = jnp.arange(length, dtype=jnp.int32)

    def intra(block_start):
        query_rows = block_start + jnp.arange(block, dtype=jnp.int32)
        same = (segment[:, None] == segment[None, :]) & (query_rows[:, None] >= order[None, :])
        gap = cumulative_t[:, :, None] - cumulative_t[:, None, :]
        factor = jnp.where(same[None], jnp.exp(jnp.where(same[None], gap, 0.0)), 0.0)
        weights = factor * step_t[:, None, :] * pair_scores[None, :, :]
        return jnp.einsum(
            "hqs,shd->qhd",
            weights,
            values_bf,
            precision=high_precision,
            preferred_element_type=jnp.float32,
        )

    intra_out = lax.map(intra, jnp.arange(length // block, dtype=jnp.int32) * block).reshape(
        length, heads, head_size
    )
    last_segment = segment[length - 1]
    in_last = segment == last_segment
    tail_weight = (
        jnp.where(in_last[:, None], jnp.exp(cumulative[length - 1][None, :] - cumulative), 0.0)
        * step
    )
    weighted = tail_weight[:, :, None] * values
    local_state = jnp.einsum(
        "thd,tn->hdn",
        weighted,
        inputs_b,
        precision=high_precision,
        preferred_element_type=jnp.float32,
    )
    whole_decay = jnp.exp(cumulative[length - 1] - before[length - 1])
    starts_here = begin[length - 1] >= first
    cached_last = lax.dynamic_index_in_dim(ssm_cache, last_segment, 0, keepdims=False)
    chain_state = local_state + jnp.where(
        starts_here, whole_decay[:, None, None] * cached_last, 0.0
    )
    chain_decay = jnp.where(starts_here, jnp.zeros_like(whole_decay), whole_decay)

    scan_decay, scan_state = advance((chain_decay, chain_state))
    distance = 1
    while distance <= reach and distance < seq_count:
        prior_decay, prior_state = shifted_2((scan_decay, scan_state), "seq", distance)
        scan_state = scan_decay[:, None, None] * prior_state + scan_state
        scan_decay = scan_decay * prior_decay
        scan_decay, scan_state = advance((scan_decay, scan_state))
        distance *= 2
    carried = advance(shifted_2(scan_state, "seq", 1))
    continuing = position[0] > 0
    replace = (jnp.arange(prompts, dtype=jnp.int32) == segment[0]) & continuing
    initial = jnp.where(replace[:, None, None, None], carried[None], ssm_cache)
    selected = (onehot[:, :, None].astype(jnp.bfloat16) * inputs_c[:, None, :]).reshape(
        length, prompts * state_size
    )
    table = jnp.transpose(initial, (0, 3, 1, 2)).reshape(prompts * state_size, heads * head_size)
    init_out = (
        jnp.dot(
            selected, table, precision=high_precision, preferred_element_type=jnp.float32
        ).reshape(length, heads, head_size)
        * from_begin[:, :, None]
    )
    mixed = intra_out + init_out + d_skip[None, :, None] * values
    gated = (
        mixed * jax.nn.silu(z_in.astype(jnp.float32).reshape(length, heads, head_size))
    ).reshape(length, heads * head_size)
    gated = advance(gated)
    squares = lax.psum(jnp.sum(gated * gated, axis=1), "tp")
    width = gated.shape[1] * lax.axis_size("tp")
    normed = (gated * lax.rsqrt(squares / width + EPS)[:, None] * norm_gain[None, :]).astype(
        jnp.bfloat16
    )
    normed = advance(normed)
    summed = lax.psum(
        jnp.dot(normed, out_weight, preferred_element_type=jnp.float32).astype(jnp.bfloat16), "tp"
    )
    hidden_rows = (residual_rows.astype(jnp.float32) + summed.astype(jnp.float32)).astype(
        jnp.bfloat16
    )
    rows = residual.shape[0]
    hidden = lax.dynamic_slice_in_dim(hidden_rows, lax.axis_index("tp") * rows, rows, 0)
    level = hidden_rows.astype(jnp.float32)
    attn_in = (
        level * lax.rsqrt(jnp.mean(level * level, axis=1, keepdims=True) + EPS) * attn_gain[None, :]
    ).astype(jnp.bfloat16)
    piece = attn_in
    low = jnp.dot(piece, q_down, preferred_element_type=jnp.float32).astype(jnp.bfloat16)
    query = (
        jnp.dot(piece, q_weight, preferred_element_type=jnp.float32)
        + jnp.dot(low, q_up, preferred_element_type=jnp.float32)
    ).astype(jnp.bfloat16)
    count_heads = query.shape[1] // HA

    def piece_mask(query_index, query_segment, offset, causal):
        key_index = (seq_index + offset) * length + jnp.arange(length, dtype=jnp.int32)
        key_segment, _, key_valid, _ = locate(lengths, key_index)
        allowed = key_valid[None, :] & (key_segment[None, :] == query_segment[:, None])
        if causal:
            allowed = allowed & (key_index[None, :] <= query_index[:, None])
        return allowed

    cache_pieces = [(cache_keys, cache_values, 0)]
    new_pieces = [(new_keys, new_values, 0)]
    while relay_steps:
        advance((), tied=False)
    for distance in range(1, reach + 1):
        behind = behind_pieces[distance]
        cache_pieces.append((behind[0], behind[1], -distance))
        new_pieces.append((behind[2], behind[3], -distance))
        forward = forward_pieces[distance]
        cache_pieces.append((forward[0], forward[1], distance))
    all_keys = jnp.concatenate(
        [entry[0] for entry in cache_pieces] + [entry[0] for entry in new_pieces], axis=0
    )
    all_values = jnp.concatenate(
        [entry[1] for entry in cache_pieces] + [entry[1] for entry in new_pieces], axis=0
    )
    mask = jnp.concatenate(
        [piece_mask(local_index, segment, entry[2], False) for entry in cache_pieces]
        + [piece_mask(local_index, segment, entry[2], True) for entry in new_pieces],
        axis=1,
    )
    scale = 1.0 / HA**0.5

    def attend(head):
        column = head * HA
        query_head = lax.dynamic_slice_in_dim(query, column, HA, 1)
        key_head = lax.dynamic_slice_in_dim(all_keys, column, HA, 1)
        value_head = lax.dynamic_slice_in_dim(all_values, column, HA, 1)
        scores = (
            lax.dot_general(
                query_head, key_head, (((1,), (1,)), ((), ())), preferred_element_type=jnp.float32
            )
            * scale
        )
        scores = jnp.where(mask, scores, NEG)
        top = jnp.max(scores, axis=1, keepdims=True)
        weights = jnp.exp(scores - top)
        probs = (weights / jnp.sum(weights, axis=1, keepdims=True)).astype(jnp.bfloat16)
        return jnp.dot(probs, value_head, preferred_element_type=jnp.float32).astype(jnp.bfloat16)

    per_head = lax.map(attend, jnp.arange(count_heads, dtype=jnp.int32))
    attended = jnp.transpose(per_head, (1, 0, 2)).reshape(length, count_heads * HA)
    return (hidden, attended)


def solution(mesh):
    in_specs = (
        P(("seq", "tp"), None),
        P("seq", "tp"),
        P("seq", "tp"),
        P("seq", None),
        P("seq", "tp"),
        P(None, "tp"),
        P(),
        P(None, None, "tp"),
        P(),
        P(None, "tp", None, None),
        P("tp"),
        P("tp"),
        P("tp"),
        P("tp"),
        P("tp", None),
        P(),
        P(None, "tp"),
        P(),
        P(None, "tp"),
        P("seq", "tp"),
        P("seq", "tp"),
        P("seq", "tp"),
        P("seq", "tp"),
        P(),
    )
    out_specs = (P(("seq", "tp"), None), P("seq", "tp"))
    return jax.shard_map(
        per_device, mesh=mesh, in_specs=in_specs, out_specs=out_specs, check_vma=False
    )
```

```python
import jax
import jax.numpy as jnp
from jax import lax
from jax.sharding import PartitionSpec as P

HA = 224


EPS = 1e-05
NEG = -1e30


def shifted_2(value, axis, steps):
    count = lax.axis_size(axis)
    initial, last = (max(0, -steps), min(count, count - steps))
    return lax.ppermute(value, axis, [(source, source + steps) for source in range(initial, last)])


def locate(lengths, index):
    ends = jnp.cumsum(lengths)
    starts = ends - lengths
    count = lengths.shape[0]
    segment = jnp.sum((index[:, None] >= ends[None, :]).astype(jnp.int32), axis=1)
    segment = jnp.minimum(segment, count - 1)
    onehot = segment[:, None] == jnp.arange(count, dtype=jnp.int32)[None, :]
    begin = jnp.sum(jnp.where(onehot, starts[None, :], 0), axis=1)
    valid = (index >= 0) & (index < ends[count - 1])
    return (segment, begin, valid, onehot)


def convolve(inputs, border, cache, weight, position, onehot):
    taps = weight.shape[0]
    length = inputs.shape[0]
    extended = jnp.concatenate([border, inputs], axis=0)
    picks = onehot.astype(jnp.bfloat16)
    cached_rows = [
        jnp.dot(picks, cache[:, slot, :], preferred_element_type=jnp.float32)
        for slot in range(taps - 1)
    ]
    result = weight[0][None, :] * inputs.astype(jnp.float32)
    for lag in range(1, taps):
        shifted = extended[taps - 1 - lag : taps - 1 - lag + length].astype(jnp.float32)
        slot_index = taps - 1 + position - lag
        fallback = jnp.zeros_like(shifted)
        for slot in range(taps - 1):
            fallback = jnp.where((slot_index == slot)[:, None], cached_rows[slot], fallback)
        shifted = jnp.where((position >= lag)[:, None], shifted, fallback)
        result = result + weight[lag][None, :] * shifted
    return jax.nn.silu(result).astype(jnp.bfloat16)


def per_device(
    residual,
    x_in,
    z_in,
    bc_in,
    dt_in,
    conv_x_weight,
    conv_bc_weight,
    conv_x_cache,
    conv_bc_cache,
    ssm_cache,
    dt_bias,
    a_log,
    d_skip,
    norm_gain,
    out_weight,
    attn_gain,
    q_weight,
    q_down,
    q_up,
    cache_keys,
    cache_values,
    new_keys,
    new_values,
    lengths,
):
    high_precision = lax.Precision.HIGH
    length = x_in.shape[0]
    taps = conv_x_weight.shape[0]
    seq_index = lax.axis_index("seq")
    seq_count = lax.axis_size("seq")
    reach = seq_count // 4 + 1
    first = seq_index * length
    residual_rows = lax.all_gather(residual, "tp", axis=0, tiled=True)
    long_hop = reach + 1
    tied_steps = 9
    behind_pieces = [jnp.stack([cache_keys, cache_values, new_keys, new_values])] * (reach + 1)
    forward_pieces = [jnp.stack([cache_keys, cache_values])] * (reach + 1)
    relay_steps = []
    for distance in range(1, long_hop):
        relay_steps.append([(distance, distance - 1, 1)])
    for distance in range(long_hop, reach + 1):
        relay_steps[distance - long_hop].append((distance, distance - long_hop, long_hop))

    def advance(values, tied=True):
        if not relay_steps or (tied and len(relay_steps) <= reach - tied_steps):
            return values
        moves = relay_steps.pop(0)
        sent = []
        for distance, source, steps in moves:
            sent.append(
                (
                    shifted_2(behind_pieces[source], "seq", steps),
                    shifted_2(forward_pieces[source], "seq", -steps),
                )
            )
        sent, values = lax.optimization_barrier((sent, values))
        for (distance, _, _), (behind, forward) in zip(moves, sent):
            behind_pieces[distance] = behind
            forward_pieces[distance] = forward
        return values

    local_index = first + jnp.arange(length, dtype=jnp.int32)
    segment, begin, valid, onehot = locate(lengths, local_index)
    position = local_index - begin
    x_border, bc_border = shifted_2(
        (x_in[length - taps + 1 :], bc_in[length - taps + 1 :]), "seq", 1
    )
    x_conv = convolve(x_in, x_border, conv_x_cache, conv_x_weight, position, onehot)
    bc_conv = convolve(bc_in, bc_border, conv_bc_cache, conv_bc_weight, position, onehot)
    x_conv, bc_conv = advance((x_conv, bc_conv))
    heads = dt_bias.shape[0]
    state_size = bc_in.shape[1] // 2
    head_size = x_in.shape[1] // heads
    prompts = lengths.shape[0]
    values_bf = x_conv.reshape(length, heads, head_size)
    values = x_conv.astype(jnp.float32).reshape(length, heads, head_size)
    inputs_b = bc_conv[:, :state_size]
    inputs_c = bc_conv[:, state_size:]
    step = jax.nn.softplus(dt_in + dt_bias[None, :])
    log_decay = -step * jnp.exp(a_log)[None, :]
    cumulative = jnp.cumsum(log_decay, axis=0)
    local_begin = jnp.maximum(begin - first, 0)
    before = jnp.take(cumulative - log_decay, local_begin, axis=0)
    from_begin = jnp.exp(cumulative - before)
    block = min(length, 512)
    pair_scores = jnp.dot(inputs_c, inputs_b.T, preferred_element_type=jnp.float32)
    cumulative_t = cumulative.T
    step_t = step.T
    order = jnp.arange(length, dtype=jnp.int32)

    def intra(block_start):
        query_rows = block_start + jnp.arange(block, dtype=jnp.int32)
        same = (segment[:, None] == segment[None, :]) & (query_rows[:, None] >= order[None, :])
        gap = cumulative_t[:, :, None] - cumulative_t[:, None, :]
        factor = jnp.where(same[None], jnp.exp(jnp.where(same[None], gap, 0.0)), 0.0)
        weights = factor * step_t[:, None, :] * pair_scores[None, :, :]
        return jnp.einsum(
            "hqs,shd->qhd",
            weights,
            values_bf,
            precision=high_precision,
            preferred_element_type=jnp.float32,
        )

    intra_out = lax.map(intra, jnp.arange(length // block, dtype=jnp.int32) * block).reshape(
        length, heads, head_size
    )
    last_segment = segment[length - 1]
    in_last = segment == last_segment
    tail_weight = (
        jnp.where(in_last[:, None], jnp.exp(cumulative[length - 1][None, :] - cumulative), 0.0)
        * step
    )
    weighted = tail_weight[:, :, None] * values
    local_state = jnp.einsum(
        "thd,tn->hdn",
        weighted,
        inputs_b,
        precision=high_precision,
        preferred_element_type=jnp.float32,
    )
    whole_decay = jnp.exp(cumulative[length - 1] - before[length - 1])
    starts_here = begin[length - 1] >= first
    cached_last = lax.dynamic_index_in_dim(ssm_cache, last_segment, 0, keepdims=False)
    chain_state = local_state + jnp.where(
        starts_here, whole_decay[:, None, None] * cached_last, 0.0
    )
    chain_decay = jnp.where(starts_here, jnp.zeros_like(whole_decay), whole_decay)

    scan_decay, scan_state = advance((chain_decay, chain_state))
    distance = 1
    while distance <= reach and distance < seq_count:
        prior_decay, prior_state = shifted_2((scan_decay, scan_state), "seq", distance)
        scan_state = scan_decay[:, None, None] * prior_state + scan_state
        scan_decay = scan_decay * prior_decay
        scan_decay, scan_state = advance((scan_decay, scan_state))
        distance *= 2
    carried = advance(shifted_2(scan_state, "seq", 1))
    continuing = position[0] > 0
    replace = (jnp.arange(prompts, dtype=jnp.int32) == segment[0]) & continuing
    initial = jnp.where(replace[:, None, None, None], carried[None], ssm_cache)
    selected = (onehot[:, :, None].astype(jnp.bfloat16) * inputs_c[:, None, :]).reshape(
        length, prompts * state_size
    )
    table = jnp.transpose(initial, (0, 3, 1, 2)).reshape(prompts * state_size, heads * head_size)
    init_out = (
        jnp.dot(
            selected, table, precision=high_precision, preferred_element_type=jnp.float32
        ).reshape(length, heads, head_size)
        * from_begin[:, :, None]
    )
    mixed = intra_out + init_out + d_skip[None, :, None] * values
    gated = (
        mixed * jax.nn.silu(z_in.astype(jnp.float32).reshape(length, heads, head_size))
    ).reshape(length, heads * head_size)
    gated = advance(gated)
    squares = lax.psum(jnp.sum(gated * gated, axis=1), "tp")
    width = gated.shape[1] * lax.axis_size("tp")
    normed = (gated * lax.rsqrt(squares / width + EPS)[:, None] * norm_gain[None, :]).astype(
        jnp.bfloat16
    )
    normed = advance(normed)
    summed = lax.psum(
        jnp.dot(normed, out_weight, preferred_element_type=jnp.float32).astype(jnp.bfloat16), "tp"
    )
    hidden_rows = (residual_rows.astype(jnp.float32) + summed.astype(jnp.float32)).astype(
        jnp.bfloat16
    )
    rows = residual.shape[0]
    hidden = lax.dynamic_slice_in_dim(hidden_rows, lax.axis_index("tp") * rows, rows, 0)
    level = hidden_rows.astype(jnp.float32)
    attn_in = (
        level * lax.rsqrt(jnp.mean(level * level, axis=1, keepdims=True) + EPS) * attn_gain[None, :]
    ).astype(jnp.bfloat16)
    piece = attn_in
    low = jnp.dot(piece, q_down, preferred_element_type=jnp.float32).astype(jnp.bfloat16)
    query = (
        jnp.dot(piece, q_weight, preferred_element_type=jnp.float32)
        + jnp.dot(low, q_up, preferred_element_type=jnp.float32)
    ).astype(jnp.bfloat16)
    count_heads = query.shape[1] // HA

    def piece_mask(query_index, query_segment, offset, causal):
        key_index = (seq_index + offset) * length + jnp.arange(length, dtype=jnp.int32)
        key_segment, _, key_valid, _ = locate(lengths, key_index)
        allowed = key_valid[None, :] & (key_segment[None, :] == query_segment[:, None])
        if causal:
            allowed = allowed & (key_index[None, :] <= query_index[:, None])
        return allowed

    cache_pieces = [(cache_keys, cache_values, 0)]
    new_pieces = [(new_keys, new_values, 0)]
    while relay_steps:
        advance((), tied=False)
    for distance in range(1, reach + 1):
        behind = behind_pieces[distance]
        cache_pieces.append((behind[0], behind[1], -distance))
        new_pieces.append((behind[2], behind[3], -distance))
        forward = forward_pieces[distance]
        cache_pieces.append((forward[0], forward[1], distance))
    all_keys = jnp.concatenate(
        [entry[0] for entry in cache_pieces] + [entry[0] for entry in new_pieces], axis=0
    )
    all_values = jnp.concatenate(
        [entry[1] for entry in cache_pieces] + [entry[1] for entry in new_pieces], axis=0
    )
    mask = jnp.concatenate(
        [piece_mask(local_index, segment, entry[2], False) for entry in cache_pieces]
        + [piece_mask(local_index, segment, entry[2], True) for entry in new_pieces],
        axis=1,
    )
    scale = 1.0 / HA**0.5

    def attend(head):
        column = head * HA
        query_head = lax.dynamic_slice_in_dim(query, column, HA, 1)
        key_head = lax.dynamic_slice_in_dim(all_keys, column, HA, 1)
        value_head = lax.dynamic_slice_in_dim(all_values, column, HA, 1)
        scores = (
            lax.dot_general(
                query_head, key_head, (((1,), (1,)), ((), ())), preferred_element_type=jnp.float32
            )
            * scale
        )
        scores = jnp.where(mask, scores, NEG)
        top = jnp.max(scores, axis=1, keepdims=True)
        weights = jnp.exp(scores - top)
        probs = (weights / jnp.sum(weights, axis=1, keepdims=True)).astype(jnp.bfloat16)
        return jnp.dot(probs, value_head, preferred_element_type=jnp.float32).astype(jnp.bfloat16)

    per_head = lax.map(attend, jnp.arange(count_heads, dtype=jnp.int32))
    attended = jnp.transpose(per_head, (1, 0, 2)).reshape(length, count_heads * HA)
    return (hidden, attended)


def solution(mesh):
    in_specs = (
        P(("seq", "tp"), None),
        P("seq", "tp"),
        P("seq", "tp"),
        P("seq", None),
        P("seq", "tp"),
        P(None, "tp"),
        P(),
        P(None, None, "tp"),
        P(),
        P(None, "tp", None, None),
        P("tp"),
        P("tp"),
        P("tp"),
        P("tp"),
        P("tp", None),
        P(),
        P(None, "tp"),
        P(),
        P(None, "tp"),
        P("seq", "tp"),
        P("seq", "tp"),
        P("seq", "tp"),
        P("seq", "tp"),
        P(),
    )
    out_specs = (P(("seq", "tp"), None), P("seq", "tp"))
    return jax.shard_map(
        per_device, mesh=mesh, in_specs=in_specs, out_specs=out_specs, check_vma=False
    )
```

```python
import jax
import jax.numpy as jnp
from jax import lax
from jax.sharding import PartitionSpec as P

HA = 224


EPS = 1e-05
NEG = -1e30


def shifted_2(value, axis, steps):
    count = lax.axis_size(axis)
    initial, last = (max(0, -steps), min(count, count - steps))
    return lax.ppermute(value, axis, [(source, source + steps) for source in range(initial, last)])


def locate(lengths, index):
    ends = jnp.cumsum(lengths)
    starts = ends - lengths
    count = lengths.shape[0]
    segment = jnp.sum((index[:, None] >= ends[None, :]).astype(jnp.int32), axis=1)
    segment = jnp.minimum(segment, count - 1)
    onehot = segment[:, None] == jnp.arange(count, dtype=jnp.int32)[None, :]
    begin = jnp.sum(jnp.where(onehot, starts[None, :], 0), axis=1)
    valid = (index >= 0) & (index < ends[count - 1])
    return (segment, begin, valid, onehot)


def convolve(inputs, border, cache, weight, position, onehot):
    taps = weight.shape[0]
    length = inputs.shape[0]
    extended = jnp.concatenate([border, inputs], axis=0)
    picks = onehot.astype(jnp.bfloat16)
    cached_rows = [
        jnp.dot(picks, cache[:, slot, :], preferred_element_type=jnp.float32)
        for slot in range(taps - 1)
    ]
    result = weight[0][None, :] * inputs.astype(jnp.float32)
    for lag in range(1, taps):
        shifted = extended[taps - 1 - lag : taps - 1 - lag + length].astype(jnp.float32)
        slot_index = taps - 1 + position - lag
        fallback = jnp.zeros_like(shifted)
        for slot in range(taps - 1):
            fallback = jnp.where((slot_index == slot)[:, None], cached_rows[slot], fallback)
        shifted = jnp.where((position >= lag)[:, None], shifted, fallback)
        result = result + weight[lag][None, :] * shifted
    return jax.nn.silu(result).astype(jnp.bfloat16)


def per_device(
    residual,
    x_in,
    z_in,
    bc_in,
    dt_in,
    conv_x_weight,
    conv_bc_weight,
    conv_x_cache,
    conv_bc_cache,
    ssm_cache,
    dt_bias,
    a_log,
    d_skip,
    norm_gain,
    out_weight,
    attn_gain,
    q_weight,
    q_down,
    q_up,
    cache_keys,
    cache_values,
    new_keys,
    new_values,
    lengths,
):
    high_precision = lax.Precision.HIGH
    length = x_in.shape[0]
    taps = conv_x_weight.shape[0]
    seq_index = lax.axis_index("seq")
    seq_count = lax.axis_size("seq")
    reach = seq_count // 4 + 1
    first = seq_index * length
    long_hop = reach + 1
    tied_steps = 5
    behind_pieces = [jnp.stack([cache_keys, cache_values, new_keys, new_values])] * (reach + 1)
    forward_pieces = [jnp.stack([cache_keys, cache_values])] * (reach + 1)
    relay_steps = []
    for distance in range(1, long_hop):
        relay_steps.append([(distance, distance - 1, 1)])
    for distance in range(long_hop, reach + 1):
        relay_steps[distance - long_hop].append((distance, distance - long_hop, long_hop))

    def advance(values, tied=True):
        if not relay_steps or (tied and len(relay_steps) <= reach - tied_steps):
            return values
        moves = relay_steps.pop(0)
        sent = []
        for distance, source, steps in moves:
            sent.append(
                (
                    shifted_2(behind_pieces[source], "seq", steps),
                    shifted_2(forward_pieces[source], "seq", -steps),
                )
            )
        sent, values = lax.optimization_barrier((sent, values))
        for (distance, _, _), (behind, forward) in zip(moves, sent):
            behind_pieces[distance] = behind
            forward_pieces[distance] = forward
        return values

    local_index = first + jnp.arange(length, dtype=jnp.int32)
    segment, begin, valid, onehot = locate(lengths, local_index)
    position = local_index - begin
    x_border, bc_border = shifted_2(
        (x_in[length - taps + 1 :], bc_in[length - taps + 1 :]), "seq", 1
    )
    x_conv = convolve(x_in, x_border, conv_x_cache, conv_x_weight, position, onehot)
    bc_conv = convolve(bc_in, bc_border, conv_bc_cache, conv_bc_weight, position, onehot)
    prompts = lengths.shape[0]
    heads = dt_bias.shape[0]
    state_size = bc_in.shape[1] // 2
    head_size = x_in.shape[1] // heads
    table = jnp.transpose(ssm_cache, (0, 3, 1, 2)).reshape(prompts * state_size, heads * head_size)
    x_conv, bc_conv, table = advance((x_conv, bc_conv, table))
    heads = dt_bias.shape[0]
    state_size = bc_in.shape[1] // 2
    head_size = x_in.shape[1] // heads
    prompts = lengths.shape[0]
    values_bf = x_conv.reshape(length, heads, head_size)
    values = x_conv.astype(jnp.float32).reshape(length, heads, head_size)
    inputs_b = bc_conv[:, :state_size]
    inputs_c = bc_conv[:, state_size:]
    step = jax.nn.softplus(dt_in + dt_bias[None, :])
    log_decay = -step * jnp.exp(a_log)[None, :]
    cumulative = jnp.cumsum(log_decay, axis=0)
    local_begin = jnp.maximum(begin - first, 0)
    before = jnp.take(cumulative - log_decay, local_begin, axis=0)
    from_begin = jnp.exp(cumulative - before)
    block = min(length, 512)
    pair_scores = jnp.dot(inputs_c, inputs_b.T, preferred_element_type=jnp.float32)
    cumulative_t = cumulative.T
    step_t = step.T
    order = jnp.arange(length, dtype=jnp.int32)

    def intra(block_start):
        query_rows = block_start + jnp.arange(block, dtype=jnp.int32)
        same = (segment[:, None] == segment[None, :]) & (query_rows[:, None] >= order[None, :])
        gap = cumulative_t[:, :, None] - cumulative_t[:, None, :]
        factor = jnp.where(same[None], jnp.exp(jnp.where(same[None], gap, 0.0)), 0.0)
        weights = factor * step_t[:, None, :] * pair_scores[None, :, :]
        return jnp.einsum(
            "hqs,shd->qhd",
            weights,
            values_bf,
            precision=high_precision,
            preferred_element_type=jnp.float32,
        )

    intra_out = lax.map(intra, jnp.arange(length // block, dtype=jnp.int32) * block).reshape(
        length, heads, head_size
    )
    last_segment = segment[length - 1]
    in_last = segment == last_segment
    tail_weight = (
        jnp.where(in_last[:, None], jnp.exp(cumulative[length - 1][None, :] - cumulative), 0.0)
        * step
    )
    weighted = tail_weight[:, :, None] * values
    local_state = jnp.einsum(
        "thd,tn->hdn",
        weighted,
        inputs_b,
        precision=high_precision,
        preferred_element_type=jnp.float32,
    )
    whole_decay = jnp.exp(cumulative[length - 1] - before[length - 1])
    starts_here = begin[length - 1] >= first
    cached_last = lax.dynamic_index_in_dim(ssm_cache, last_segment, 0, keepdims=False)
    chain_state = local_state + jnp.where(
        starts_here, whole_decay[:, None, None] * cached_last, 0.0
    )
    chain_decay = jnp.where(starts_here, jnp.zeros_like(whole_decay), whole_decay)

    scan_decay, scan_state = advance((chain_decay, chain_state))
    distance = 1
    while distance <= reach and distance < seq_count:
        prior_decay, prior_state = shifted_2((scan_decay, scan_state), "seq", distance)
        scan_state = scan_decay[:, None, None] * prior_state + scan_state
        scan_decay = scan_decay * prior_decay
        scan_decay, scan_state = advance((scan_decay, scan_state))
        distance *= 2
    carried = advance(shifted_2(scan_state, "seq", 1))
    continuing = position[0] > 0
    first_rows = (segment == segment[0]) & continuing
    cached_rows = onehot & ~first_rows[:, None]
    selected = (cached_rows[:, :, None].astype(jnp.bfloat16) * inputs_c[:, None, :]).reshape(
        length, prompts * state_size
    )
    carried_table = jnp.transpose(carried, (2, 0, 1)).reshape(state_size, heads * head_size)
    from_cache = jnp.dot(selected, table, precision=high_precision, preferred_element_type=jnp.float32)
    from_carried = jnp.dot(
        inputs_c, carried_table, precision=high_precision, preferred_element_type=jnp.float32
    )
    init_out = (
        jnp.where(first_rows[:, None], from_carried, from_cache).reshape(length, heads, head_size)
        * from_begin[:, :, None]
    )
    mixed = intra_out + init_out + d_skip[None, :, None] * values
    gated = (
        mixed * jax.nn.silu(z_in.astype(jnp.float32).reshape(length, heads, head_size))
    ).reshape(length, heads * head_size)
    gated = advance(gated)
    squares = lax.psum(jnp.sum(gated * gated, axis=1), "tp")
    width = gated.shape[1] * lax.axis_size("tp")
    normed = (gated * lax.rsqrt(squares / width + EPS)[:, None] * norm_gain[None, :]).astype(
        jnp.bfloat16
    )
    normed = advance(normed)
    summed = lax.psum_scatter(
        jnp.dot(normed, out_weight, preferred_element_type=jnp.float32),
        "tp",
        scatter_dimension=0,
        tiled=True,
    )
    hidden = (residual.astype(jnp.float32) + summed).astype(jnp.bfloat16)
    level = hidden.astype(jnp.float32)
    attn_in = (
        level * lax.rsqrt(jnp.mean(level * level, axis=1, keepdims=True) + EPS) * attn_gain[None, :]
    ).astype(jnp.bfloat16)
    piece = lax.all_gather(attn_in, "tp", axis=0, tiled=True)
    low = jnp.dot(piece, q_down, preferred_element_type=jnp.float32).astype(jnp.bfloat16)
    query = (
        jnp.dot(piece, q_weight, preferred_element_type=jnp.float32)
        + jnp.dot(low, q_up, preferred_element_type=jnp.float32)
    ).astype(jnp.bfloat16)
    count_heads = query.shape[1] // HA

    def piece_mask(query_index, query_segment, offset, causal):
        key_index = (seq_index + offset) * length + jnp.arange(length, dtype=jnp.int32)
        key_segment, _, key_valid, _ = locate(lengths, key_index)
        allowed = key_valid[None, :] & (key_segment[None, :] == query_segment[:, None])
        if causal:
            allowed = allowed & (key_index[None, :] <= query_index[:, None])
        return allowed

    cache_pieces = [(cache_keys, cache_values, 0)]
    new_pieces = [(new_keys, new_values, 0)]
    while relay_steps:
        advance((), tied=False)
    for distance in range(1, reach + 1):
        behind = behind_pieces[distance]
        cache_pieces.append((behind[0], behind[1], -distance))
        new_pieces.append((behind[2], behind[3], -distance))
        forward = forward_pieces[distance]
        cache_pieces.append((forward[0], forward[1], distance))
    all_keys = jnp.concatenate(
        [entry[0] for entry in cache_pieces] + [entry[0] for entry in new_pieces], axis=0
    )
    all_values = jnp.concatenate(
        [entry[1] for entry in cache_pieces] + [entry[1] for entry in new_pieces], axis=0
    )
    mask = jnp.concatenate(
        [piece_mask(local_index, segment, entry[2], False) for entry in cache_pieces]
        + [piece_mask(local_index, segment, entry[2], True) for entry in new_pieces],
        axis=1,
    )
    scale = 1.0 / HA**0.5

    def attend(head):
        column = head * HA
        query_head = lax.dynamic_slice_in_dim(query, column, HA, 1)
        key_head = lax.dynamic_slice_in_dim(all_keys, column, HA, 1)
        value_head = lax.dynamic_slice_in_dim(all_values, column, HA, 1)
        scores = (
            lax.dot_general(
                query_head, key_head, (((1,), (1,)), ((), ())), preferred_element_type=jnp.float32
            )
            * scale
        )
        scores = jnp.where(mask, scores, NEG)
        top = jnp.max(scores, axis=1, keepdims=True)
        weights = jnp.exp(scores - top)
        probs = (weights / jnp.sum(weights, axis=1, keepdims=True)).astype(jnp.bfloat16)
        return jnp.dot(probs, value_head, preferred_element_type=jnp.float32).astype(jnp.bfloat16)

    per_head = lax.map(attend, jnp.arange(count_heads, dtype=jnp.int32))
    attended = jnp.transpose(per_head, (1, 0, 2)).reshape(length, count_heads * HA)
    return (hidden, attended)


def solution(mesh):
    in_specs = (
        P(("seq", "tp"), None),
        P("seq", "tp"),
        P("seq", "tp"),
        P("seq", None),
        P("seq", "tp"),
        P(None, "tp"),
        P(),
        P(None, None, "tp"),
        P(),
        P(None, "tp", None, None),
        P("tp"),
        P("tp"),
        P("tp"),
        P("tp"),
        P("tp", None),
        P(),
        P(None, "tp"),
        P(),
        P(None, "tp"),
        P("seq", "tp"),
        P("seq", "tp"),
        P("seq", "tp"),
        P("seq", "tp"),
        P(),
    )
    out_specs = (P(("seq", "tp"), None), P("seq", "tp"))
    return jax.shard_map(
        per_device, mesh=mesh, in_specs=in_specs, out_specs=out_specs, check_vma=False
    )
```

```python
import jax
import jax.numpy as jnp
from jax import lax
from jax.sharding import PartitionSpec as P

HA = 224


EPS = 1e-05
NEG = -1e30


def shifted_2(value, axis, steps):
    count = lax.axis_size(axis)
    initial, last = (max(0, -steps), min(count, count - steps))
    return lax.ppermute(value, axis, [(source, source + steps) for source in range(initial, last)])


def locate(lengths, index):
    ends = jnp.cumsum(lengths)
    starts = ends - lengths
    count = lengths.shape[0]
    segment = jnp.sum((index[:, None] >= ends[None, :]).astype(jnp.int32), axis=1)
    segment = jnp.minimum(segment, count - 1)
    onehot = segment[:, None] == jnp.arange(count, dtype=jnp.int32)[None, :]
    begin = jnp.sum(jnp.where(onehot, starts[None, :], 0), axis=1)
    valid = (index >= 0) & (index < ends[count - 1])
    return (segment, begin, valid, onehot)


def convolve(inputs, border, cache, weight, position, onehot):
    taps = weight.shape[0]
    length = inputs.shape[0]
    extended = jnp.concatenate([border, inputs], axis=0)
    picks = onehot.astype(jnp.bfloat16)
    cached_rows = [
        jnp.dot(picks, cache[:, slot, :], preferred_element_type=jnp.float32)
        for slot in range(taps - 1)
    ]
    result = weight[0][None, :] * inputs.astype(jnp.float32)
    for lag in range(1, taps):
        shifted = extended[taps - 1 - lag : taps - 1 - lag + length].astype(jnp.float32)
        slot_index = taps - 1 + position - lag
        fallback = jnp.zeros_like(shifted)
        for slot in range(taps - 1):
            fallback = jnp.where((slot_index == slot)[:, None], cached_rows[slot], fallback)
        shifted = jnp.where((position >= lag)[:, None], shifted, fallback)
        result = result + weight[lag][None, :] * shifted
    return jax.nn.silu(result).astype(jnp.bfloat16)


def per_device(
    residual,
    x_in,
    z_in,
    bc_in,
    dt_in,
    conv_x_weight,
    conv_bc_weight,
    conv_x_cache,
    conv_bc_cache,
    ssm_cache,
    dt_bias,
    a_log,
    d_skip,
    norm_gain,
    out_weight,
    attn_gain,
    q_weight,
    q_down,
    q_up,
    cache_keys,
    cache_values,
    new_keys,
    new_values,
    lengths,
):
    high_precision = lax.Precision.HIGH
    length = x_in.shape[0]
    taps = conv_x_weight.shape[0]
    seq_index = lax.axis_index("seq")
    seq_count = lax.axis_size("seq")
    reach = seq_count // 4 + 1
    first = seq_index * length
    long_hop = reach + 1
    tied_steps = 9
    behind_pieces = [jnp.stack([cache_keys, cache_values, new_keys, new_values])] * (reach + 1)
    forward_pieces = [jnp.stack([cache_keys, cache_values])] * (reach + 1)
    relay_steps = []
    for distance in range(1, long_hop):
        relay_steps.append([(distance, distance - 1, 1)])
    for distance in range(long_hop, reach + 1):
        relay_steps[distance - long_hop].append((distance, distance - long_hop, long_hop))

    def advance(values, tied=True):
        if not relay_steps or (tied and len(relay_steps) <= reach - tied_steps):
            return values
        moves = relay_steps.pop(0)
        sent = []
        for distance, source, steps in moves:
            sent.append(
                (
                    shifted_2(behind_pieces[source], "seq", steps),
                    shifted_2(forward_pieces[source], "seq", -steps),
                )
            )
        _, values = lax.optimization_barrier((sent, values))
        for (distance, _, _), (behind, forward) in zip(moves, sent):
            behind_pieces[distance] = behind
            forward_pieces[distance] = forward
        return values

    local_index = first + jnp.arange(length, dtype=jnp.int32)
    segment, begin, valid, onehot = locate(lengths, local_index)
    position = local_index - begin
    x_border, bc_border = shifted_2(
        (x_in[length - taps + 1 :], bc_in[length - taps + 1 :]), "seq", 1
    )
    x_conv = convolve(x_in, x_border, conv_x_cache, conv_x_weight, position, onehot)
    bc_conv = convolve(bc_in, bc_border, conv_bc_cache, conv_bc_weight, position, onehot)
    x_conv, bc_conv = advance((x_conv, bc_conv))
    heads = dt_bias.shape[0]
    state_size = bc_in.shape[1] // 2
    head_size = x_in.shape[1] // heads
    prompts = lengths.shape[0]
    values_bf = x_conv.reshape(length, heads, head_size)
    values = x_conv.astype(jnp.float32).reshape(length, heads, head_size)
    inputs_b = bc_conv[:, :state_size]
    inputs_c = bc_conv[:, state_size:]
    step = jax.nn.softplus(dt_in + dt_bias[None, :])
    log_decay = -step * jnp.exp(a_log)[None, :]
    cumulative = jnp.cumsum(log_decay, axis=0)
    local_begin = jnp.maximum(begin - first, 0)
    before = jnp.take(cumulative - log_decay, local_begin, axis=0)
    from_begin = jnp.exp(cumulative - before)
    block = min(length, 512)
    pair_scores = jnp.dot(inputs_c, inputs_b.T, preferred_element_type=jnp.float32)
    cumulative_t = cumulative.T
    step_t = step.T
    order = jnp.arange(length, dtype=jnp.int32)

    def intra(block_start):
        query_rows = block_start + jnp.arange(block, dtype=jnp.int32)
        same = (segment[:, None] == segment[None, :]) & (query_rows[:, None] >= order[None, :])
        gap = cumulative_t[:, :, None] - cumulative_t[:, None, :]
        factor = jnp.where(same[None], jnp.exp(jnp.where(same[None], gap, 0.0)), 0.0)
        weights = factor * step_t[:, None, :] * pair_scores[None, :, :]
        return jnp.einsum(
            "hqs,shd->qhd",
            weights,
            values_bf,
            precision=high_precision,
            preferred_element_type=jnp.float32,
        )

    intra_out = lax.map(intra, jnp.arange(length // block, dtype=jnp.int32) * block).reshape(
        length, heads, head_size
    )
    last_segment = segment[length - 1]
    in_last = segment == last_segment
    tail_weight = (
        jnp.where(in_last[:, None], jnp.exp(cumulative[length - 1][None, :] - cumulative), 0.0)
        * step
    )
    weighted = tail_weight[:, :, None] * values
    local_state = jnp.einsum(
        "thd,tn->hdn",
        weighted,
        inputs_b,
        precision=high_precision,
        preferred_element_type=jnp.float32,
    )
    whole_decay = jnp.exp(cumulative[length - 1] - before[length - 1])
    starts_here = begin[length - 1] >= first
    cached_last = lax.dynamic_index_in_dim(ssm_cache, last_segment, 0, keepdims=False)
    chain_state = local_state + jnp.where(
        starts_here, whole_decay[:, None, None] * cached_last, 0.0
    )
    chain_decay = jnp.where(starts_here, jnp.zeros_like(whole_decay), whole_decay)

    scan_decay, scan_state = advance((chain_decay, chain_state))
    distance = 1
    while distance <= reach and distance < seq_count:
        prior_decay, prior_state = shifted_2((scan_decay, scan_state), "seq", distance)
        scan_state = scan_decay[:, None, None] * prior_state + scan_state
        scan_decay = scan_decay * prior_decay
        scan_decay, scan_state = advance((scan_decay, scan_state))
        distance *= 2
    carried = advance(shifted_2(scan_state, "seq", 1))
    continuing = position[0] > 0
    replace = (jnp.arange(prompts, dtype=jnp.int32) == segment[0]) & continuing
    initial = jnp.where(replace[:, None, None, None], carried[None], ssm_cache)
    selected = (onehot[:, :, None].astype(jnp.bfloat16) * inputs_c[:, None, :]).reshape(
        length, prompts * state_size
    )
    table = jnp.transpose(initial, (0, 3, 1, 2)).reshape(prompts * state_size, heads * head_size)
    init_out = (
        jnp.dot(
            selected, table, precision=high_precision, preferred_element_type=jnp.float32
        ).reshape(length, heads, head_size)
        * from_begin[:, :, None]
    )
    mixed = intra_out + init_out + d_skip[None, :, None] * values
    gated = (
        mixed * jax.nn.silu(z_in.astype(jnp.float32).reshape(length, heads, head_size))
    ).reshape(length, heads * head_size)
    gated = advance(gated)
    squares = lax.psum(jnp.sum(gated * gated, axis=1), "tp")
    width = gated.shape[1] * lax.axis_size("tp")
    normed = (gated * lax.rsqrt(squares / width + EPS)[:, None] * norm_gain[None, :]).astype(
        jnp.bfloat16
    )
    normed = advance(normed)
    summed = lax.psum_scatter(
        jnp.dot(normed, out_weight, preferred_element_type=jnp.float32),
        "tp",
        scatter_dimension=0,
        tiled=True,
    )
    hidden = (residual.astype(jnp.float32) + summed).astype(jnp.bfloat16)
    level = hidden.astype(jnp.float32)
    attn_in = (
        level * lax.rsqrt(jnp.mean(level * level, axis=1, keepdims=True) + EPS) * attn_gain[None, :]
    ).astype(jnp.bfloat16)
    piece = lax.all_gather(attn_in, "tp", axis=0, tiled=True)
    low = jnp.dot(piece, q_down, preferred_element_type=jnp.float32).astype(jnp.bfloat16)
    query = (
        jnp.dot(piece, q_weight, preferred_element_type=jnp.float32)
        + jnp.dot(low, q_up, preferred_element_type=jnp.float32)
    ).astype(jnp.bfloat16)
    count_heads = query.shape[1] // HA

    def piece_mask(query_index, query_segment, offset, causal):
        key_index = (seq_index + offset) * length + jnp.arange(length, dtype=jnp.int32)
        key_segment, _, key_valid, _ = locate(lengths, key_index)
        allowed = key_valid[None, :] & (key_segment[None, :] == query_segment[:, None])
        if causal:
            allowed = allowed & (key_index[None, :] <= query_index[:, None])
        return allowed

    cache_pieces = [(cache_keys, cache_values, 0)]
    new_pieces = [(new_keys, new_values, 0)]
    while relay_steps:
        advance((), tied=False)
    for distance in range(1, reach + 1):
        behind = behind_pieces[distance]
        cache_pieces.append((behind[0], behind[1], -distance))
        new_pieces.append((behind[2], behind[3], -distance))
        forward = forward_pieces[distance]
        cache_pieces.append((forward[0], forward[1], distance))
    all_keys = jnp.concatenate(
        [entry[0] for entry in cache_pieces] + [entry[0] for entry in new_pieces], axis=0
    )
    all_values = jnp.concatenate(
        [entry[1] for entry in cache_pieces] + [entry[1] for entry in new_pieces], axis=0
    )
    mask = jnp.concatenate(
        [piece_mask(local_index, segment, entry[2], False) for entry in cache_pieces]
        + [piece_mask(local_index, segment, entry[2], True) for entry in new_pieces],
        axis=1,
    )
    scale = 1.0 / HA**0.5

    def attend(head):
        column = head * HA
        query_head = lax.dynamic_slice_in_dim(query, column, HA, 1)
        key_head = lax.dynamic_slice_in_dim(all_keys, column, HA, 1)
        value_head = lax.dynamic_slice_in_dim(all_values, column, HA, 1)
        scores = (
            lax.dot_general(
                query_head, key_head, (((1,), (1,)), ((), ())), preferred_element_type=jnp.float32
            )
            * scale
        )
        scores = jnp.where(mask, scores, NEG)
        top = jnp.max(scores, axis=1, keepdims=True)
        weights = jnp.exp(scores - top)
        probs = (weights / jnp.sum(weights, axis=1, keepdims=True)).astype(jnp.bfloat16)
        return jnp.dot(probs, value_head, preferred_element_type=jnp.float32).astype(jnp.bfloat16)

    per_head = lax.map(attend, jnp.arange(count_heads, dtype=jnp.int32))
    attended = jnp.transpose(per_head, (1, 0, 2)).reshape(length, count_heads * HA)
    return (hidden, attended)


def solution(mesh):
    in_specs = (
        P(("seq", "tp"), None),
        P("seq", "tp"),
        P("seq", "tp"),
        P("seq", None),
        P("seq", "tp"),
        P(None, "tp"),
        P(),
        P(None, None, "tp"),
        P(),
        P(None, "tp", None, None),
        P("tp"),
        P("tp"),
        P("tp"),
        P("tp"),
        P("tp", None),
        P(),
        P(None, "tp"),
        P(),
        P(None, "tp"),
        P("seq", "tp"),
        P("seq", "tp"),
        P("seq", "tp"),
        P("seq", "tp"),
        P(),
    )
    out_specs = (P(("seq", "tp"), None), P("seq", "tp"))
    return jax.shard_map(
        per_device, mesh=mesh, in_specs=in_specs, out_specs=out_specs, check_vma=False
    )
```

```python
import jax
import jax.numpy as jnp
from jax import lax
from jax.sharding import PartitionSpec as P

HA = 224


EPS = 1e-05
NEG = -1e30


def shifted_2(value, axis, steps):
    count = lax.axis_size(axis)
    initial, last = (max(0, -steps), min(count, count - steps))
    return lax.ppermute(value, axis, [(source, source + steps) for source in range(initial, last)])


def locate(lengths, index):
    ends = jnp.cumsum(lengths)
    starts = ends - lengths
    count = lengths.shape[0]
    segment = jnp.sum((index[:, None] >= ends[None, :]).astype(jnp.int32), axis=1)
    segment = jnp.minimum(segment, count - 1)
    onehot = segment[:, None] == jnp.arange(count, dtype=jnp.int32)[None, :]
    begin = jnp.sum(jnp.where(onehot, starts[None, :], 0), axis=1)
    valid = (index >= 0) & (index < ends[count - 1])
    return (segment, begin, valid, onehot)


def convolve(inputs, border, cache, weight, position, onehot):
    taps = weight.shape[0]
    length = inputs.shape[0]
    extended = jnp.concatenate([border, inputs], axis=0)
    picks = onehot.astype(jnp.bfloat16)
    cached_rows = [
        jnp.dot(picks, cache[:, slot, :], preferred_element_type=jnp.float32)
        for slot in range(taps - 1)
    ]
    result = weight[0][None, :] * inputs.astype(jnp.float32)
    for lag in range(1, taps):
        shifted = extended[taps - 1 - lag : taps - 1 - lag + length].astype(jnp.float32)
        slot_index = taps - 1 + position - lag
        fallback = jnp.zeros_like(shifted)
        for slot in range(taps - 1):
            fallback = jnp.where((slot_index == slot)[:, None], cached_rows[slot], fallback)
        shifted = jnp.where((position >= lag)[:, None], shifted, fallback)
        result = result + weight[lag][None, :] * shifted
    return jax.nn.silu(result).astype(jnp.bfloat16)


def per_device(
    residual,
    x_in,
    z_in,
    bc_in,
    dt_in,
    conv_x_weight,
    conv_bc_weight,
    conv_x_cache,
    conv_bc_cache,
    ssm_cache,
    dt_bias,
    a_log,
    d_skip,
    norm_gain,
    out_weight,
    attn_gain,
    q_weight,
    q_down,
    q_up,
    cache_keys,
    cache_values,
    new_keys,
    new_values,
    lengths,
):
    high_precision = lax.Precision.HIGH
    length = x_in.shape[0]
    taps = conv_x_weight.shape[0]
    seq_index = lax.axis_index("seq")
    seq_count = lax.axis_size("seq")
    reach = seq_count // 4 + 1
    first = seq_index * length
    long_hop = reach + 1
    tied_steps = 5
    behind_pieces = [jnp.stack([cache_keys, cache_values, new_keys, new_values])] * (reach + 1)
    forward_pieces = [jnp.stack([cache_keys, cache_values])] * (reach + 1)
    relay_steps = []
    for distance in range(1, long_hop):
        relay_steps.append([(distance, distance - 1, 1)])
    for distance in range(long_hop, reach + 1):
        relay_steps[distance - long_hop].append((distance, distance - long_hop, long_hop))

    def advance(values, tied=True, after=None):
        if not relay_steps or (tied and len(relay_steps) <= reach - tied_steps):
            return values
        moves = relay_steps.pop(0)
        sent = []
        for distance, source, steps in moves:
            behind, forward = behind_pieces[source], forward_pieces[source]
            if after is not None:
                behind, forward, _ = lax.optimization_barrier((behind, forward, after))
            sent.append((shifted_2(behind, "seq", steps), shifted_2(forward, "seq", -steps)))
        sent, values = lax.optimization_barrier((sent, values))
        for (distance, _, _), (behind, forward) in zip(moves, sent):
            behind_pieces[distance] = behind
            forward_pieces[distance] = forward
        return values

    local_index = first + jnp.arange(length, dtype=jnp.int32)
    segment, begin, valid, onehot = locate(lengths, local_index)
    position = local_index - begin
    x_border, bc_border = shifted_2(
        (x_in[length - taps + 1 :], bc_in[length - taps + 1 :]), "seq", 1
    )
    x_conv = convolve(x_in, x_border, conv_x_cache, conv_x_weight, position, onehot)
    bc_conv = convolve(bc_in, bc_border, conv_bc_cache, conv_bc_weight, position, onehot)
    x_conv, bc_conv = advance((x_conv, bc_conv))
    heads = dt_bias.shape[0]
    state_size = bc_in.shape[1] // 2
    head_size = x_in.shape[1] // heads
    prompts = lengths.shape[0]
    values_bf = x_conv.reshape(length, heads, head_size)
    values = x_conv.astype(jnp.float32).reshape(length, heads, head_size)
    inputs_b = bc_conv[:, :state_size]
    inputs_c = bc_conv[:, state_size:]
    step = jax.nn.softplus(dt_in + dt_bias[None, :])
    log_decay = -step * jnp.exp(a_log)[None, :]
    cumulative = jnp.cumsum(log_decay, axis=0)
    local_begin = jnp.maximum(begin - first, 0)
    before = jnp.take(cumulative - log_decay, local_begin, axis=0)
    from_begin = jnp.exp(cumulative - before)
    block = min(length, 512)
    pair_scores = jnp.dot(inputs_c, inputs_b.T, preferred_element_type=jnp.float32)
    cumulative_t = cumulative.T
    step_t = step.T
    order = jnp.arange(length, dtype=jnp.int32)

    def intra(block_start):
        query_rows = block_start + jnp.arange(block, dtype=jnp.int32)
        same = (segment[:, None] == segment[None, :]) & (query_rows[:, None] >= order[None, :])
        gap = cumulative_t[:, :, None] - cumulative_t[:, None, :]
        factor = jnp.where(same[None], jnp.exp(jnp.where(same[None], gap, 0.0)), 0.0)
        weights = factor * step_t[:, None, :] * pair_scores[None, :, :]
        return jnp.einsum(
            "hqs,shd->qhd",
            weights,
            values_bf,
            precision=high_precision,
            preferred_element_type=jnp.float32,
        )

    intra_out = lax.map(intra, jnp.arange(length // block, dtype=jnp.int32) * block).reshape(
        length, heads, head_size
    )
    last_segment = segment[length - 1]
    in_last = segment == last_segment
    tail_weight = (
        jnp.where(in_last[:, None], jnp.exp(cumulative[length - 1][None, :] - cumulative), 0.0)
        * step
    )
    weighted = tail_weight[:, :, None] * values
    local_state = jnp.einsum(
        "thd,tn->hdn",
        weighted,
        inputs_b,
        precision=high_precision,
        preferred_element_type=jnp.float32,
    )
    whole_decay = jnp.exp(cumulative[length - 1] - before[length - 1])
    starts_here = begin[length - 1] >= first
    cached_last = lax.dynamic_index_in_dim(ssm_cache, last_segment, 0, keepdims=False)
    chain_state = local_state + jnp.where(
        starts_here, whole_decay[:, None, None] * cached_last, 0.0
    )
    chain_decay = jnp.where(starts_here, jnp.zeros_like(whole_decay), whole_decay)

    scan_decay, scan_state = advance((chain_decay, chain_state))
    distance = 1
    while distance <= reach and distance < seq_count:
        prior_decay, prior_state = shifted_2((scan_decay, scan_state), "seq", distance)
        scan_state = scan_decay[:, None, None] * prior_state + scan_state
        scan_decay = scan_decay * prior_decay
        scan_decay, scan_state = advance((scan_decay, scan_state))
        distance *= 2
    carried = advance(shifted_2(scan_state, "seq", 1))
    continuing = position[0] > 0
    replace = (jnp.arange(prompts, dtype=jnp.int32) == segment[0]) & continuing
    initial = jnp.where(replace[:, None, None, None], carried[None], ssm_cache)
    selected = (onehot[:, :, None].astype(jnp.bfloat16) * inputs_c[:, None, :]).reshape(
        length, prompts * state_size
    )
    table = jnp.transpose(initial, (0, 3, 1, 2)).reshape(prompts * state_size, heads * head_size)
    init_out = (
        jnp.dot(
            selected, table, precision=high_precision, preferred_element_type=jnp.float32
        ).reshape(length, heads, head_size)
        * from_begin[:, :, None]
    )
    mixed = intra_out + init_out + d_skip[None, :, None] * values
    gated = (
        mixed * jax.nn.silu(z_in.astype(jnp.float32).reshape(length, heads, head_size))
    ).reshape(length, heads * head_size)
    gated = advance(gated)
    squares = lax.psum(jnp.sum(gated * gated, axis=1), "tp")
    width = gated.shape[1] * lax.axis_size("tp")
    normed = (gated * lax.rsqrt(squares / width + EPS)[:, None] * norm_gain[None, :]).astype(
        jnp.bfloat16
    )
    normed = advance(normed)
    summed = lax.psum_scatter(
        jnp.dot(normed, out_weight, preferred_element_type=jnp.float32),
        "tp",
        scatter_dimension=0,
        tiled=True,
    )
    hidden = (residual.astype(jnp.float32) + summed).astype(jnp.bfloat16)
    level = hidden.astype(jnp.float32)
    attn_in = (
        level * lax.rsqrt(jnp.mean(level * level, axis=1, keepdims=True) + EPS) * attn_gain[None, :]
    ).astype(jnp.bfloat16)
    piece = lax.all_gather(attn_in, "tp", axis=0, tiled=True)
    low = jnp.dot(piece, q_down, preferred_element_type=jnp.float32).astype(jnp.bfloat16)
    query = (
        jnp.dot(piece, q_weight, preferred_element_type=jnp.float32)
        + jnp.dot(low, q_up, preferred_element_type=jnp.float32)
    ).astype(jnp.bfloat16)
    count_heads = query.shape[1] // HA

    def piece_mask(query_index, query_segment, offset, causal):
        key_index = (seq_index + offset) * length + jnp.arange(length, dtype=jnp.int32)
        key_segment, _, key_valid, _ = locate(lengths, key_index)
        allowed = key_valid[None, :] & (key_segment[None, :] == query_segment[:, None])
        if causal:
            allowed = allowed & (key_index[None, :] <= query_index[:, None])
        return allowed

    cache_pieces = [(cache_keys, cache_values, 0)]
    new_pieces = [(new_keys, new_values, 0)]
    while relay_steps:
        advance((), tied=False, after=attn_in if len(relay_steps) <= 2 else None)
    for distance in range(1, reach + 1):
        behind = behind_pieces[distance]
        cache_pieces.append((behind[0], behind[1], -distance))
        new_pieces.append((behind[2], behind[3], -distance))
        forward = forward_pieces[distance]
        cache_pieces.append((forward[0], forward[1], distance))
    all_keys = jnp.concatenate(
        [entry[0] for entry in cache_pieces] + [entry[0] for entry in new_pieces], axis=0
    )
    all_values = jnp.concatenate(
        [entry[1] for entry in cache_pieces] + [entry[1] for entry in new_pieces], axis=0
    )
    mask = jnp.concatenate(
        [piece_mask(local_index, segment, entry[2], False) for entry in cache_pieces]
        + [piece_mask(local_index, segment, entry[2], True) for entry in new_pieces],
        axis=1,
    )
    scale = 1.0 / HA**0.5

    def attend(head):
        column = head * HA
        query_head = lax.dynamic_slice_in_dim(query, column, HA, 1)
        key_head = lax.dynamic_slice_in_dim(all_keys, column, HA, 1)
        value_head = lax.dynamic_slice_in_dim(all_values, column, HA, 1)
        scores = (
            lax.dot_general(
                query_head, key_head, (((1,), (1,)), ((), ())), preferred_element_type=jnp.float32
            )
            * scale
        )
        scores = jnp.where(mask, scores, NEG)
        top = jnp.max(scores, axis=1, keepdims=True)
        weights = jnp.exp(scores - top)
        probs = (weights / jnp.sum(weights, axis=1, keepdims=True)).astype(jnp.bfloat16)
        return jnp.dot(probs, value_head, preferred_element_type=jnp.float32).astype(jnp.bfloat16)

    per_head = lax.map(attend, jnp.arange(count_heads, dtype=jnp.int32))
    attended = jnp.transpose(per_head, (1, 0, 2)).reshape(length, count_heads * HA)
    return (hidden, attended)


def solution(mesh):
    in_specs = (
        P(("seq", "tp"), None),
        P("seq", "tp"),
        P("seq", "tp"),
        P("seq", None),
        P("seq", "tp"),
        P(None, "tp"),
        P(),
        P(None, None, "tp"),
        P(),
        P(None, "tp", None, None),
        P("tp"),
        P("tp"),
        P("tp"),
        P("tp"),
        P("tp", None),
        P(),
        P(None, "tp"),
        P(),
        P(None, "tp"),
        P("seq", "tp"),
        P("seq", "tp"),
        P("seq", "tp"),
        P("seq", "tp"),
        P(),
    )
    out_specs = (P(("seq", "tp"), None), P("seq", "tp"))
    return jax.shard_map(
        per_device, mesh=mesh, in_specs=in_specs, out_specs=out_specs, check_vma=False
    )
```

```python
import jax
import jax.numpy as jnp
from jax import lax
from jax.sharding import PartitionSpec as P

HA = 224


EPS = 1e-05
NEG = -1e30


def shifted_2(value, axis, steps):
    count = lax.axis_size(axis)
    initial, last = (max(0, -steps), min(count, count - steps))
    return lax.ppermute(value, axis, [(source, source + steps) for source in range(initial, last)])


def locate(lengths, index):
    ends = jnp.cumsum(lengths)
    starts = ends - lengths
    count = lengths.shape[0]
    segment = jnp.sum((index[:, None] >= ends[None, :]).astype(jnp.int32), axis=1)
    segment = jnp.minimum(segment, count - 1)
    onehot = segment[:, None] == jnp.arange(count, dtype=jnp.int32)[None, :]
    begin = jnp.sum(jnp.where(onehot, starts[None, :], 0), axis=1)
    valid = (index >= 0) & (index < ends[count - 1])
    return (segment, begin, valid, onehot)


def convolve(inputs, border, cache, weight, position, onehot):
    taps = weight.shape[0]
    length = inputs.shape[0]
    extended = jnp.concatenate([border, inputs], axis=0)
    picks = onehot.astype(jnp.bfloat16)
    cached_rows = [
        jnp.dot(picks, cache[:, slot, :], preferred_element_type=jnp.float32)
        for slot in range(taps - 1)
    ]
    result = weight[0][None, :] * inputs.astype(jnp.float32)
    for lag in range(1, taps):
        shifted = extended[taps - 1 - lag : taps - 1 - lag + length].astype(jnp.float32)
        slot_index = taps - 1 + position - lag
        fallback = jnp.zeros_like(shifted)
        for slot in range(taps - 1):
            fallback = jnp.where((slot_index == slot)[:, None], cached_rows[slot], fallback)
        shifted = jnp.where((position >= lag)[:, None], shifted, fallback)
        result = result + weight[lag][None, :] * shifted
    return jax.nn.silu(result).astype(jnp.bfloat16)


def per_device(
    residual,
    x_in,
    z_in,
    bc_in,
    dt_in,
    conv_x_weight,
    conv_bc_weight,
    conv_x_cache,
    conv_bc_cache,
    ssm_cache,
    dt_bias,
    a_log,
    d_skip,
    norm_gain,
    out_weight,
    attn_gain,
    q_weight,
    q_down,
    q_up,
    cache_keys,
    cache_values,
    new_keys,
    new_values,
    lengths,
):
    high_precision = lax.Precision.HIGH
    length = x_in.shape[0]
    taps = conv_x_weight.shape[0]
    seq_index = lax.axis_index("seq")
    seq_count = lax.axis_size("seq")
    reach = seq_count // 4 + 1
    first = seq_index * length
    long_hop = reach + 1
    tied_steps = 4
    behind_pieces = [jnp.stack([cache_keys, cache_values, new_keys, new_values])] * (reach + 1)
    forward_pieces = [jnp.stack([cache_keys, cache_values])] * (reach + 1)
    relay_steps = []
    for distance in range(1, long_hop):
        relay_steps.append([(distance, distance - 1, 1)])
    for distance in range(long_hop, reach + 1):
        relay_steps[distance - long_hop].append((distance, distance - long_hop, long_hop))

    def advance(values, tied=True, after=None):
        if not relay_steps or (tied and len(relay_steps) <= reach - tied_steps):
            return values
        moves = relay_steps.pop(0)
        sent = []
        for distance, source, steps in moves:
            behind, forward = behind_pieces[source], forward_pieces[source]
            if after is not None:
                behind, forward, _ = lax.optimization_barrier((behind, forward, after))
            sent.append((shifted_2(behind, "seq", steps), shifted_2(forward, "seq", -steps)))
        sent, values = lax.optimization_barrier((sent, values))
        for (distance, _, _), (behind, forward) in zip(moves, sent):
            behind_pieces[distance] = behind
            forward_pieces[distance] = forward
        return values

    local_index = first + jnp.arange(length, dtype=jnp.int32)
    segment, begin, valid, onehot = locate(lengths, local_index)
    position = local_index - begin
    x_border, bc_border = shifted_2(
        (x_in[length - taps + 1 :], bc_in[length - taps + 1 :]), "seq", 1
    )
    x_conv = convolve(x_in, x_border, conv_x_cache, conv_x_weight, position, onehot)
    bc_conv = convolve(bc_in, bc_border, conv_bc_cache, conv_bc_weight, position, onehot)
    x_conv, bc_conv = advance((x_conv, bc_conv))
    heads = dt_bias.shape[0]
    state_size = bc_in.shape[1] // 2
    head_size = x_in.shape[1] // heads
    prompts = lengths.shape[0]
    values_bf = x_conv.reshape(length, heads, head_size)
    values = x_conv.astype(jnp.float32).reshape(length, heads, head_size)
    inputs_b = bc_conv[:, :state_size]
    inputs_c = bc_conv[:, state_size:]
    step = jax.nn.softplus(dt_in + dt_bias[None, :])
    log_decay = -step * jnp.exp(a_log)[None, :]
    cumulative = jnp.cumsum(log_decay, axis=0)
    local_begin = jnp.maximum(begin - first, 0)
    before = jnp.take(cumulative - log_decay, local_begin, axis=0)
    from_begin = jnp.exp(cumulative - before)
    block = min(length, 512)
    pair_scores = jnp.dot(inputs_c, inputs_b.T, preferred_element_type=jnp.float32)
    cumulative_t = cumulative.T
    step_t = step.T
    order = jnp.arange(length, dtype=jnp.int32)

    def intra(block_start):
        query_rows = block_start + jnp.arange(block, dtype=jnp.int32)
        same = (segment[:, None] == segment[None, :]) & (query_rows[:, None] >= order[None, :])
        gap = cumulative_t[:, :, None] - cumulative_t[:, None, :]
        factor = jnp.where(same[None], jnp.exp(jnp.where(same[None], gap, 0.0)), 0.0)
        weights = factor * step_t[:, None, :] * pair_scores[None, :, :]
        return jnp.einsum(
            "hqs,shd->qhd",
            weights,
            values_bf,
            precision=high_precision,
            preferred_element_type=jnp.float32,
        )

    intra_out = lax.map(intra, jnp.arange(length // block, dtype=jnp.int32) * block).reshape(
        length, heads, head_size
    )
    last_segment = segment[length - 1]
    in_last = segment == last_segment
    tail_weight = (
        jnp.where(in_last[:, None], jnp.exp(cumulative[length - 1][None, :] - cumulative), 0.0)
        * step
    )
    weighted = tail_weight[:, :, None] * values
    local_state = jnp.einsum(
        "thd,tn->hdn",
        weighted,
        inputs_b,
        precision=high_precision,
        preferred_element_type=jnp.float32,
    )
    whole_decay = jnp.exp(cumulative[length - 1] - before[length - 1])
    starts_here = begin[length - 1] >= first
    cached_last = lax.dynamic_index_in_dim(ssm_cache, last_segment, 0, keepdims=False)
    chain_state = local_state + jnp.where(
        starts_here, whole_decay[:, None, None] * cached_last, 0.0
    )
    chain_decay = jnp.where(starts_here, jnp.zeros_like(whole_decay), whole_decay)

    scan_decay, scan_state = advance((chain_decay, chain_state))
    distance = 1
    while distance <= reach and distance < seq_count:
        prior_decay, prior_state = shifted_2((scan_decay, scan_state), "seq", distance)
        scan_state = scan_decay[:, None, None] * prior_state + scan_state
        scan_decay = scan_decay * prior_decay
        scan_decay, scan_state = advance((scan_decay, scan_state))
        distance *= 2
    carried = advance(shifted_2(scan_state, "seq", 1))
    continuing = position[0] > 0
    replace = (jnp.arange(prompts, dtype=jnp.int32) == segment[0]) & continuing
    initial = jnp.where(replace[:, None, None, None], carried[None], ssm_cache)
    selected = (onehot[:, :, None].astype(jnp.bfloat16) * inputs_c[:, None, :]).reshape(
        length, prompts * state_size
    )
    table = jnp.transpose(initial, (0, 3, 1, 2)).reshape(prompts * state_size, heads * head_size)
    init_out = (
        jnp.dot(
            selected, table, precision=high_precision, preferred_element_type=jnp.float32
        ).reshape(length, heads, head_size)
        * from_begin[:, :, None]
    )
    mixed = intra_out + init_out + d_skip[None, :, None] * values
    gated = (
        mixed * jax.nn.silu(z_in.astype(jnp.float32).reshape(length, heads, head_size))
    ).reshape(length, heads * head_size)
    gated = advance(gated)
    squares = lax.psum(jnp.sum(gated * gated, axis=1), "tp")
    width = gated.shape[1] * lax.axis_size("tp")
    normed = (gated * lax.rsqrt(squares / width + EPS)[:, None] * norm_gain[None, :]).astype(
        jnp.bfloat16
    )
    normed = advance(normed)
    summed = lax.psum_scatter(
        jnp.dot(normed, out_weight, preferred_element_type=jnp.float32),
        "tp",
        scatter_dimension=0,
        tiled=True,
    )
    hidden = (residual.astype(jnp.float32) + summed).astype(jnp.bfloat16)
    level = hidden.astype(jnp.float32)
    attn_in = (
        level * lax.rsqrt(jnp.mean(level * level, axis=1, keepdims=True) + EPS) * attn_gain[None, :]
    ).astype(jnp.bfloat16)
    piece = lax.all_gather(attn_in, "tp", axis=0, tiled=True)
    low = jnp.dot(piece, q_down, preferred_element_type=jnp.float32).astype(jnp.bfloat16)
    query = (
        jnp.dot(piece, q_weight, preferred_element_type=jnp.float32)
        + jnp.dot(low, q_up, preferred_element_type=jnp.float32)
    ).astype(jnp.bfloat16)
    count_heads = query.shape[1] // HA

    def piece_mask(query_index, query_segment, offset, causal):
        key_index = (seq_index + offset) * length + jnp.arange(length, dtype=jnp.int32)
        key_segment, _, key_valid, _ = locate(lengths, key_index)
        allowed = key_valid[None, :] & (key_segment[None, :] == query_segment[:, None])
        if causal:
            allowed = allowed & (key_index[None, :] <= query_index[:, None])
        return allowed

    cache_pieces = [(cache_keys, cache_values, 0)]
    new_pieces = [(new_keys, new_values, 0)]
    while relay_steps:
        advance((), tied=False, after=attn_in if len(relay_steps) <= 2 else None)
    for distance in range(1, reach + 1):
        behind = behind_pieces[distance]
        cache_pieces.append((behind[0], behind[1], -distance))
        new_pieces.append((behind[2], behind[3], -distance))
        forward = forward_pieces[distance]
        cache_pieces.append((forward[0], forward[1], distance))
    all_keys = jnp.concatenate(
        [entry[0] for entry in cache_pieces] + [entry[0] for entry in new_pieces], axis=0
    )
    all_values = jnp.concatenate(
        [entry[1] for entry in cache_pieces] + [entry[1] for entry in new_pieces], axis=0
    )
    mask = jnp.concatenate(
        [piece_mask(local_index, segment, entry[2], False) for entry in cache_pieces]
        + [piece_mask(local_index, segment, entry[2], True) for entry in new_pieces],
        axis=1,
    )
    scale = 1.0 / HA**0.5

    def attend(head):
        column = head * HA
        query_head = lax.dynamic_slice_in_dim(query, column, HA, 1)
        key_head = lax.dynamic_slice_in_dim(all_keys, column, HA, 1)
        value_head = lax.dynamic_slice_in_dim(all_values, column, HA, 1)
        scores = (
            lax.dot_general(
                query_head, key_head, (((1,), (1,)), ((), ())), preferred_element_type=jnp.float32
            )
            * scale
        )
        scores = jnp.where(mask, scores, NEG)
        top = jnp.max(scores, axis=1, keepdims=True)
        weights = jnp.exp(scores - top)
        probs = (weights / jnp.sum(weights, axis=1, keepdims=True)).astype(jnp.bfloat16)
        return jnp.dot(probs, value_head, preferred_element_type=jnp.float32).astype(jnp.bfloat16)

    per_head = lax.map(attend, jnp.arange(count_heads, dtype=jnp.int32))
    attended = jnp.transpose(per_head, (1, 0, 2)).reshape(length, count_heads * HA)
    return (hidden, attended)


def solution(mesh):
    in_specs = (
        P(("seq", "tp"), None),
        P("seq", "tp"),
        P("seq", "tp"),
        P("seq", None),
        P("seq", "tp"),
        P(None, "tp"),
        P(),
        P(None, None, "tp"),
        P(),
        P(None, "tp", None, None),
        P("tp"),
        P("tp"),
        P("tp"),
        P("tp"),
        P("tp", None),
        P(),
        P(None, "tp"),
        P(),
        P(None, "tp"),
        P("seq", "tp"),
        P("seq", "tp"),
        P("seq", "tp"),
        P("seq", "tp"),
        P(),
    )
    out_specs = (P(("seq", "tp"), None), P("seq", "tp"))
    return jax.shard_map(
        per_device, mesh=mesh, in_specs=in_specs, out_specs=out_specs, check_vma=False
    )
```

```python
import jax
import jax.numpy as jnp
from jax import lax
from jax.sharding import PartitionSpec as P

HA = 224


EPS = 1e-05
NEG = -1e30


def shifted_2(value, axis, steps):
    count = lax.axis_size(axis)
    initial, last = (max(0, -steps), min(count, count - steps))
    return lax.ppermute(value, axis, [(source, source + steps) for source in range(initial, last)])


def locate(lengths, index):
    ends = jnp.cumsum(lengths)
    starts = ends - lengths
    count = lengths.shape[0]
    segment = jnp.sum((index[:, None] >= ends[None, :]).astype(jnp.int32), axis=1)
    segment = jnp.minimum(segment, count - 1)
    onehot = segment[:, None] == jnp.arange(count, dtype=jnp.int32)[None, :]
    begin = jnp.sum(jnp.where(onehot, starts[None, :], 0), axis=1)
    valid = (index >= 0) & (index < ends[count - 1])
    return (segment, begin, valid, onehot)


def convolve(inputs, border, cache, weight, position, onehot):
    taps = weight.shape[0]
    length = inputs.shape[0]
    extended = jnp.concatenate([border, inputs], axis=0)
    picks = onehot.astype(jnp.bfloat16)
    cached_rows = [
        jnp.dot(picks, cache[:, slot, :], preferred_element_type=jnp.float32)
        for slot in range(taps - 1)
    ]
    result = weight[0][None, :] * inputs.astype(jnp.float32)
    for lag in range(1, taps):
        shifted = extended[taps - 1 - lag : taps - 1 - lag + length].astype(jnp.float32)
        slot_index = taps - 1 + position - lag
        fallback = jnp.zeros_like(shifted)
        for slot in range(taps - 1):
            fallback = jnp.where((slot_index == slot)[:, None], cached_rows[slot], fallback)
        shifted = jnp.where((position >= lag)[:, None], shifted, fallback)
        result = result + weight[lag][None, :] * shifted
    return jax.nn.silu(result).astype(jnp.bfloat16)


def per_device(
    residual,
    x_in,
    z_in,
    bc_in,
    dt_in,
    conv_x_weight,
    conv_bc_weight,
    conv_x_cache,
    conv_bc_cache,
    ssm_cache,
    dt_bias,
    a_log,
    d_skip,
    norm_gain,
    out_weight,
    attn_gain,
    q_weight,
    q_down,
    q_up,
    cache_keys,
    cache_values,
    new_keys,
    new_values,
    lengths,
):
    high_precision = lax.Precision.HIGH
    length = x_in.shape[0]
    taps = conv_x_weight.shape[0]
    seq_index = lax.axis_index("seq")
    seq_count = lax.axis_size("seq")
    reach = seq_count // 4 + 1
    first = seq_index * length
    long_hop = reach + 1
    tied_steps = 6
    behind_pieces = [jnp.stack([cache_keys, cache_values, new_keys, new_values])] * (reach + 1)
    forward_pieces = [jnp.stack([cache_keys, cache_values])] * (reach + 1)
    relay_steps = []
    for distance in range(1, long_hop):
        relay_steps.append([(distance, distance - 1, 1)])
    for distance in range(long_hop, reach + 1):
        relay_steps[distance - long_hop].append((distance, distance - long_hop, long_hop))

    def advance(values, tied=True):
        if not relay_steps or (tied and len(relay_steps) <= reach - tied_steps):
            return values
        moves = relay_steps.pop(0)
        sent = []
        for distance, source, steps in moves:
            sent.append(
                (
                    shifted_2(behind_pieces[source], "seq", steps),
                    shifted_2(forward_pieces[source], "seq", -steps),
                )
            )
        sent, values = lax.optimization_barrier((sent, values))
        for (distance, _, _), (behind, forward) in zip(moves, sent):
            behind_pieces[distance] = behind
            forward_pieces[distance] = forward
        return values

    local_index = first + jnp.arange(length, dtype=jnp.int32)
    segment, begin, valid, onehot = locate(lengths, local_index)
    position = local_index - begin
    x_border, bc_border = shifted_2(
        (x_in[length - taps + 1 :], bc_in[length - taps + 1 :]), "seq", 1
    )
    x_conv = convolve(x_in, x_border, conv_x_cache, conv_x_weight, position, onehot)
    bc_conv = convolve(bc_in, bc_border, conv_bc_cache, conv_bc_weight, position, onehot)
    x_conv, bc_conv = advance((x_conv, bc_conv))
    heads = dt_bias.shape[0]
    state_size = bc_in.shape[1] // 2
    head_size = x_in.shape[1] // heads
    prompts = lengths.shape[0]
    values_bf = x_conv.reshape(length, heads, head_size)
    values = x_conv.astype(jnp.float32).reshape(length, heads, head_size)
    inputs_b = bc_conv[:, :state_size]
    inputs_c = bc_conv[:, state_size:]
    step = jax.nn.softplus(dt_in + dt_bias[None, :])
    log_decay = -step * jnp.exp(a_log)[None, :]
    cumulative = jnp.cumsum(log_decay, axis=0)
    local_begin = jnp.maximum(begin - first, 0)
    before = jnp.take(cumulative - log_decay, local_begin, axis=0)
    from_begin = jnp.exp(cumulative - before)
    block = min(length, 512)
    pair_scores = jnp.dot(inputs_c, inputs_b.T, preferred_element_type=jnp.float32)
    cumulative_t = cumulative.T
    step_t = step.T
    order = jnp.arange(length, dtype=jnp.int32)

    def intra(block_start):
        query_rows = block_start + jnp.arange(block, dtype=jnp.int32)
        same = (segment[:, None] == segment[None, :]) & (query_rows[:, None] >= order[None, :])
        gap = cumulative_t[:, :, None] - cumulative_t[:, None, :]
        factor = jnp.where(same[None], jnp.exp(jnp.where(same[None], gap, 0.0)), 0.0)
        weights = factor * step_t[:, None, :] * pair_scores[None, :, :]
        return jnp.einsum(
            "hqs,shd->qhd",
            weights,
            values_bf,
            precision=high_precision,
            preferred_element_type=jnp.float32,
        )

    intra_out = lax.map(intra, jnp.arange(length // block, dtype=jnp.int32) * block).reshape(
        length, heads, head_size
    )
    last_segment = segment[length - 1]
    in_last = segment == last_segment
    tail_weight = (
        jnp.where(in_last[:, None], jnp.exp(cumulative[length - 1][None, :] - cumulative), 0.0)
        * step
    )
    weighted = tail_weight[:, :, None] * values
    local_state = jnp.einsum(
        "thd,tn->hdn",
        weighted,
        inputs_b,
        precision=high_precision,
        preferred_element_type=jnp.float32,
    )
    whole_decay = jnp.exp(cumulative[length - 1] - before[length - 1])
    starts_here = begin[length - 1] >= first
    cached_last = lax.dynamic_index_in_dim(ssm_cache, last_segment, 0, keepdims=False)
    chain_state = local_state + jnp.where(
        starts_here, whole_decay[:, None, None] * cached_last, 0.0
    )
    chain_decay = jnp.where(starts_here, jnp.zeros_like(whole_decay), whole_decay)

    scan_decay, scan_state = advance((chain_decay, chain_state))
    distance = 1
    while distance <= reach and distance < seq_count:
        prior_decay, prior_state = shifted_2((scan_decay, scan_state), "seq", distance)
        scan_state = scan_decay[:, None, None] * prior_state + scan_state
        scan_decay = scan_decay * prior_decay
        scan_decay, scan_state = advance((scan_decay, scan_state))
        distance *= 2
    carried = advance(shifted_2(scan_state, "seq", 1))
    continuing = position[0] > 0
    replace = (jnp.arange(prompts, dtype=jnp.int32) == segment[0]) & continuing
    initial = jnp.where(replace[:, None, None, None], carried[None], ssm_cache)
    selected = (onehot[:, :, None].astype(jnp.bfloat16) * inputs_c[:, None, :]).reshape(
        length, prompts * state_size
    )
    table = jnp.transpose(initial, (0, 3, 1, 2)).reshape(prompts * state_size, heads * head_size)
    init_out = (
        jnp.dot(
            selected, table, precision=high_precision, preferred_element_type=jnp.float32
        ).reshape(length, heads, head_size)
        * from_begin[:, :, None]
    )
    mixed = intra_out + init_out + d_skip[None, :, None] * values
    gated = (
        mixed * jax.nn.silu(z_in.astype(jnp.float32).reshape(length, heads, head_size))
    ).reshape(length, heads * head_size)
    gated = advance(gated)
    squares = lax.psum(jnp.sum(gated * gated, axis=1), "tp")
    width = gated.shape[1] * lax.axis_size("tp")
    normed = (gated * lax.rsqrt(squares / width + EPS)[:, None] * norm_gain[None, :]).astype(
        jnp.bfloat16
    )
    normed = advance(normed)
    summed = lax.psum_scatter(
        jnp.dot(normed, out_weight, preferred_element_type=jnp.float32),
        "tp",
        scatter_dimension=0,
        tiled=True,
    )
    hidden = (residual.astype(jnp.float32) + summed).astype(jnp.bfloat16)
    level = hidden.astype(jnp.float32)
    attn_in = (
        level * lax.rsqrt(jnp.mean(level * level, axis=1, keepdims=True) + EPS) * attn_gain[None, :]
    ).astype(jnp.bfloat16)
    piece = lax.all_gather(attn_in, "tp", axis=0, tiled=True)
    low = jnp.dot(piece, q_down, preferred_element_type=jnp.float32).astype(jnp.bfloat16)
    query = (
        jnp.dot(piece, q_weight, preferred_element_type=jnp.float32)
        + jnp.dot(low, q_up, preferred_element_type=jnp.float32)
    ).astype(jnp.bfloat16)
    count_heads = query.shape[1] // HA

    def piece_mask(query_index, query_segment, offset, causal):
        key_index = (seq_index + offset) * length + jnp.arange(length, dtype=jnp.int32)
        key_segment, _, key_valid, _ = locate(lengths, key_index)
        allowed = key_valid[None, :] & (key_segment[None, :] == query_segment[:, None])
        if causal:
            allowed = allowed & (key_index[None, :] <= query_index[:, None])
        return allowed

    cache_pieces = [(cache_keys, cache_values, 0)]
    new_pieces = [(new_keys, new_values, 0)]
    while relay_steps:
        advance((), tied=False)
    for distance in range(1, reach + 1):
        behind = behind_pieces[distance]
        cache_pieces.append((behind[0], behind[1], -distance))
        new_pieces.append((behind[2], behind[3], -distance))
        forward = forward_pieces[distance]
        cache_pieces.append((forward[0], forward[1], distance))
    all_keys = jnp.concatenate(
        [entry[0] for entry in cache_pieces] + [entry[0] for entry in new_pieces], axis=0
    )
    all_values = jnp.concatenate(
        [entry[1] for entry in cache_pieces] + [entry[1] for entry in new_pieces], axis=0
    )
    mask = jnp.concatenate(
        [piece_mask(local_index, segment, entry[2], False) for entry in cache_pieces]
        + [piece_mask(local_index, segment, entry[2], True) for entry in new_pieces],
        axis=1,
    )
    scale = 1.0 / HA**0.5

    def attend(head):
        column = head * HA
        query_head = lax.dynamic_slice_in_dim(query, column, HA, 1)
        key_head = lax.dynamic_slice_in_dim(all_keys, column, HA, 1)
        value_head = lax.dynamic_slice_in_dim(all_values, column, HA, 1)
        scores = (
            lax.dot_general(
                query_head, key_head, (((1,), (1,)), ((), ())), preferred_element_type=jnp.float32
            )
            * scale
        )
        scores = jnp.where(mask, scores, NEG)
        top = jnp.max(scores, axis=1, keepdims=True)
        weights = jnp.exp(scores - top)
        probs = (weights / jnp.sum(weights, axis=1, keepdims=True)).astype(jnp.bfloat16)
        return jnp.dot(probs, value_head, preferred_element_type=jnp.float32).astype(jnp.bfloat16)

    per_head = lax.map(attend, jnp.arange(count_heads, dtype=jnp.int32))
    attended = jnp.transpose(per_head, (1, 0, 2)).reshape(length, count_heads * HA)
    return (hidden, attended)


def solution(mesh):
    in_specs = (
        P(("seq", "tp"), None),
        P("seq", "tp"),
        P("seq", "tp"),
        P("seq", None),
        P("seq", "tp"),
        P(None, "tp"),
        P(),
        P(None, None, "tp"),
        P(),
        P(None, "tp", None, None),
        P("tp"),
        P("tp"),
        P("tp"),
        P("tp"),
        P("tp", None),
        P(),
        P(None, "tp"),
        P(),
        P(None, "tp"),
        P("seq", "tp"),
        P("seq", "tp"),
        P("seq", "tp"),
        P("seq", "tp"),
        P(),
    )
    out_specs = (P(("seq", "tp"), None), P("seq", "tp"))
    return jax.shard_map(
        per_device, mesh=mesh, in_specs=in_specs, out_specs=out_specs, check_vma=False
    )
```

```python
import jax
import jax.numpy as jnp
from jax import lax
from jax.sharding import PartitionSpec as P

HA = 224


EPS = 1e-05
NEG = -1e30


def shifted_2(value, axis, steps):
    count = lax.axis_size(axis)
    initial, last = (max(0, -steps), min(count, count - steps))
    return lax.ppermute(value, axis, [(source, source + steps) for source in range(initial, last)])


def locate(lengths, index):
    ends = jnp.cumsum(lengths)
    starts = ends - lengths
    count = lengths.shape[0]
    segment = jnp.sum((index[:, None] >= ends[None, :]).astype(jnp.int32), axis=1)
    segment = jnp.minimum(segment, count - 1)
    onehot = segment[:, None] == jnp.arange(count, dtype=jnp.int32)[None, :]
    begin = jnp.sum(jnp.where(onehot, starts[None, :], 0), axis=1)
    valid = (index >= 0) & (index < ends[count - 1])
    return (segment, begin, valid, onehot)


def convolve(inputs, border, cache, weight, position, onehot):
    taps = weight.shape[0]
    length = inputs.shape[0]
    extended = jnp.concatenate([border, inputs], axis=0)
    picks = onehot.astype(jnp.bfloat16)
    cached_rows = [
        jnp.dot(picks, cache[:, slot, :], preferred_element_type=jnp.float32)
        for slot in range(taps - 1)
    ]
    result = weight[0][None, :] * inputs.astype(jnp.float32)
    for lag in range(1, taps):
        shifted = extended[taps - 1 - lag : taps - 1 - lag + length].astype(jnp.float32)
        slot_index = taps - 1 + position - lag
        fallback = jnp.zeros_like(shifted)
        for slot in range(taps - 1):
            fallback = jnp.where((slot_index == slot)[:, None], cached_rows[slot], fallback)
        shifted = jnp.where((position >= lag)[:, None], shifted, fallback)
        result = result + weight[lag][None, :] * shifted
    return jax.nn.silu(result).astype(jnp.bfloat16)


def per_device(
    residual,
    x_in,
    z_in,
    bc_in,
    dt_in,
    conv_x_weight,
    conv_bc_weight,
    conv_x_cache,
    conv_bc_cache,
    ssm_cache,
    dt_bias,
    a_log,
    d_skip,
    norm_gain,
    out_weight,
    attn_gain,
    q_weight,
    q_down,
    q_up,
    cache_keys,
    cache_values,
    new_keys,
    new_values,
    lengths,
):
    high_precision = lax.Precision.HIGH
    length = x_in.shape[0]
    taps = conv_x_weight.shape[0]
    seq_index = lax.axis_index("seq")
    seq_count = lax.axis_size("seq")
    reach = seq_count // 4 + 1
    first = seq_index * length
    long_hop = reach + 1
    tied_steps = 5
    behind_pieces = [jnp.stack([cache_keys, cache_values, new_keys, new_values])] * (reach + 1)
    forward_pieces = [jnp.stack([cache_keys, cache_values])] * (reach + 1)
    relay_steps = []
    for distance in range(1, long_hop):
        relay_steps.append([(distance, distance - 1, 1)])
    for distance in range(long_hop, reach + 1):
        relay_steps[distance - long_hop].append((distance, distance - long_hop, long_hop))

    def advance(values, tied=True):
        if not relay_steps or (tied and len(relay_steps) <= reach - tied_steps):
            return values
        moves = relay_steps.pop(0)
        sent = []
        for distance, source, steps in moves:
            sent.append(
                (
                    shifted_2(behind_pieces[source], "seq", steps),
                    shifted_2(forward_pieces[source], "seq", -steps),
                )
            )
        sent, values = lax.optimization_barrier((sent, values))
        for (distance, _, _), (behind, forward) in zip(moves, sent):
            behind_pieces[distance] = behind
            forward_pieces[distance] = forward
        return values

    local_index = first + jnp.arange(length, dtype=jnp.int32)
    segment, begin, valid, onehot = locate(lengths, local_index)
    position = local_index - begin
    x_border, bc_border = shifted_2(
        (x_in[length - taps + 1 :], bc_in[length - taps + 1 :]), "seq", 1
    )
    x_conv = convolve(x_in, x_border, conv_x_cache, conv_x_weight, position, onehot)
    bc_conv = convolve(bc_in, bc_border, conv_bc_cache, conv_bc_weight, position, onehot)
    x_conv, bc_conv = advance((x_conv, bc_conv))
    heads = dt_bias.shape[0]
    state_size = bc_in.shape[1] // 2
    head_size = x_in.shape[1] // heads
    prompts = lengths.shape[0]
    values_bf = x_conv.reshape(length, heads, head_size)
    values = x_conv.astype(jnp.float32).reshape(length, heads, head_size)
    inputs_b = bc_conv[:, :state_size]
    inputs_c = bc_conv[:, state_size:]
    step = jax.nn.softplus(dt_in + dt_bias[None, :])
    log_decay = -step * jnp.exp(a_log)[None, :]
    cumulative = jnp.cumsum(log_decay, axis=0)
    local_begin = jnp.maximum(begin - first, 0)
    before = jnp.take(cumulative - log_decay, local_begin, axis=0)
    from_begin = jnp.exp(cumulative - before)
    block = min(length, 512)
    pair_scores = jnp.dot(inputs_c, inputs_b.T, preferred_element_type=jnp.float32)
    cumulative_t = cumulative.T
    step_t = step.T
    order = jnp.arange(length, dtype=jnp.int32)

    def intra(block_start):
        query_rows = block_start + jnp.arange(block, dtype=jnp.int32)
        same = (segment[:, None] == segment[None, :]) & (query_rows[:, None] >= order[None, :])
        gap = cumulative_t[:, :, None] - cumulative_t[:, None, :]
        factor = jnp.where(same[None], jnp.exp(jnp.where(same[None], gap, 0.0)), 0.0)
        weights = factor * step_t[:, None, :] * pair_scores[None, :, :]
        return jnp.einsum(
            "hqs,shd->qhd",
            weights,
            values_bf,
            precision=high_precision,
            preferred_element_type=jnp.float32,
        )

    intra_out = lax.map(intra, jnp.arange(length // block, dtype=jnp.int32) * block).reshape(
        length, heads, head_size
    )
    last_segment = segment[length - 1]
    in_last = segment == last_segment
    tail_weight = (
        jnp.where(in_last[:, None], jnp.exp(cumulative[length - 1][None, :] - cumulative), 0.0)
        * step
    )
    weighted = tail_weight[:, :, None] * values
    local_state = jnp.einsum(
        "thd,tn->hdn",
        weighted,
        inputs_b,
        precision=high_precision,
        preferred_element_type=jnp.float32,
    )
    whole_decay = jnp.exp(cumulative[length - 1] - before[length - 1])
    starts_here = begin[length - 1] >= first
    cached_last = lax.dynamic_index_in_dim(ssm_cache, last_segment, 0, keepdims=False)
    chain_state = local_state + jnp.where(
        starts_here, whole_decay[:, None, None] * cached_last, 0.0
    )
    chain_decay = jnp.where(starts_here, jnp.zeros_like(whole_decay), whole_decay)

    scan_decay, scan_state = advance((chain_decay, chain_state))
    distance = 1
    while distance <= reach and distance < seq_count:
        prior_decay, prior_state = shifted_2((scan_decay, scan_state), "seq", distance)
        scan_state = scan_decay[:, None, None] * prior_state + scan_state
        scan_decay = scan_decay * prior_decay
        scan_decay, scan_state = advance((scan_decay, scan_state))
        distance *= 2
    carried = advance(shifted_2(scan_state, "seq", 1))
    continuing = position[0] > 0
    replace = (jnp.arange(prompts, dtype=jnp.int32) == segment[0]) & continuing
    initial = jnp.where(replace[:, None, None, None], carried[None], ssm_cache)
    selected = (onehot[:, :, None].astype(jnp.bfloat16) * inputs_c[:, None, :]).reshape(
        length, prompts * state_size
    )
    table = jnp.transpose(initial, (0, 3, 1, 2)).reshape(prompts * state_size, heads * head_size)
    init_out = (
        jnp.dot(
            selected, table, precision=high_precision, preferred_element_type=jnp.float32
        ).reshape(length, heads, head_size)
        * from_begin[:, :, None]
    )
    mixed = intra_out + init_out + d_skip[None, :, None] * values
    gated = (
        mixed * jax.nn.silu(z_in.astype(jnp.float32).reshape(length, heads, head_size))
    ).reshape(length, heads * head_size)
    gated = advance(gated)
    squares = lax.psum(jnp.sum(gated * gated, axis=1), "tp")
    width = gated.shape[1] * lax.axis_size("tp")
    gained = (gated * norm_gain[None, :]).astype(jnp.bfloat16)
    gained = advance(gained)
    summed = lax.psum_scatter(
        jnp.dot(gained, out_weight, preferred_element_type=jnp.float32),
        "tp",
        scatter_dimension=0,
        tiled=True,
    )
    rows = residual.shape[0]
    row_scale = lax.dynamic_slice_in_dim(
        lax.rsqrt(squares / width + EPS), lax.axis_index("tp") * rows, rows, 0
    )
    hidden = (residual.astype(jnp.float32) + summed * row_scale[:, None]).astype(jnp.bfloat16)
    level = hidden.astype(jnp.float32)
    attn_in = (
        level * lax.rsqrt(jnp.mean(level * level, axis=1, keepdims=True) + EPS) * attn_gain[None, :]
    ).astype(jnp.bfloat16)
    piece = lax.all_gather(attn_in, "tp", axis=0, tiled=True)
    low = jnp.dot(piece, q_down, preferred_element_type=jnp.float32).astype(jnp.bfloat16)
    query = (
        jnp.dot(piece, q_weight, preferred_element_type=jnp.float32)
        + jnp.dot(low, q_up, preferred_element_type=jnp.float32)
    ).astype(jnp.bfloat16)
    count_heads = query.shape[1] // HA

    def piece_mask(query_index, query_segment, offset, causal):
        key_index = (seq_index + offset) * length + jnp.arange(length, dtype=jnp.int32)
        key_segment, _, key_valid, _ = locate(lengths, key_index)
        allowed = key_valid[None, :] & (key_segment[None, :] == query_segment[:, None])
        if causal:
            allowed = allowed & (key_index[None, :] <= query_index[:, None])
        return allowed

    cache_pieces = [(cache_keys, cache_values, 0)]
    new_pieces = [(new_keys, new_values, 0)]
    while relay_steps:
        advance((), tied=False)
    for distance in range(1, reach + 1):
        behind = behind_pieces[distance]
        cache_pieces.append((behind[0], behind[1], -distance))
        new_pieces.append((behind[2], behind[3], -distance))
        forward = forward_pieces[distance]
        cache_pieces.append((forward[0], forward[1], distance))
    all_keys = jnp.concatenate(
        [entry[0] for entry in cache_pieces] + [entry[0] for entry in new_pieces], axis=0
    )
    all_values = jnp.concatenate(
        [entry[1] for entry in cache_pieces] + [entry[1] for entry in new_pieces], axis=0
    )
    mask = jnp.concatenate(
        [piece_mask(local_index, segment, entry[2], False) for entry in cache_pieces]
        + [piece_mask(local_index, segment, entry[2], True) for entry in new_pieces],
        axis=1,
    )
    scale = 1.0 / HA**0.5

    def attend(head):
        column = head * HA
        query_head = lax.dynamic_slice_in_dim(query, column, HA, 1)
        key_head = lax.dynamic_slice_in_dim(all_keys, column, HA, 1)
        value_head = lax.dynamic_slice_in_dim(all_values, column, HA, 1)
        scores = (
            lax.dot_general(
                query_head, key_head, (((1,), (1,)), ((), ())), preferred_element_type=jnp.float32
            )
            * scale
        )
        scores = jnp.where(mask, scores, NEG)
        top = jnp.max(scores, axis=1, keepdims=True)
        weights = jnp.exp(scores - top)
        probs = (weights / jnp.sum(weights, axis=1, keepdims=True)).astype(jnp.bfloat16)
        return jnp.dot(probs, value_head, preferred_element_type=jnp.float32).astype(jnp.bfloat16)

    per_head = lax.map(attend, jnp.arange(count_heads, dtype=jnp.int32))
    attended = jnp.transpose(per_head, (1, 0, 2)).reshape(length, count_heads * HA)
    return (hidden, attended)


def solution(mesh):
    in_specs = (
        P(("seq", "tp"), None),
        P("seq", "tp"),
        P("seq", "tp"),
        P("seq", None),
        P("seq", "tp"),
        P(None, "tp"),
        P(),
        P(None, None, "tp"),
        P(),
        P(None, "tp", None, None),
        P("tp"),
        P("tp"),
        P("tp"),
        P("tp"),
        P("tp", None),
        P(),
        P(None, "tp"),
        P(),
        P(None, "tp"),
        P("seq", "tp"),
        P("seq", "tp"),
        P("seq", "tp"),
        P("seq", "tp"),
        P(),
    )
    out_specs = (P(("seq", "tp"), None), P("seq", "tp"))
    return jax.shard_map(
        per_device, mesh=mesh, in_specs=in_specs, out_specs=out_specs, check_vma=False
    )
```

```python
import jax
import jax.numpy as jnp
from jax import lax
from jax.sharding import PartitionSpec as P

HA = 224


EPS = 1e-05
NEG = -1e30


def shifted_2(value, axis, steps):
    count = lax.axis_size(axis)
    initial, last = (max(0, -steps), min(count, count - steps))
    return lax.ppermute(value, axis, [(source, source + steps) for source in range(initial, last)])


def locate(lengths, index):
    ends = jnp.cumsum(lengths)
    starts = ends - lengths
    count = lengths.shape[0]
    segment = jnp.sum((index[:, None] >= ends[None, :]).astype(jnp.int32), axis=1)
    segment = jnp.minimum(segment, count - 1)
    onehot = segment[:, None] == jnp.arange(count, dtype=jnp.int32)[None, :]
    begin = jnp.sum(jnp.where(onehot, starts[None, :], 0), axis=1)
    valid = (index >= 0) & (index < ends[count - 1])
    return (segment, begin, valid, onehot)


def convolve(inputs, border, cache, weight, position, onehot):
    taps = weight.shape[0]
    length = inputs.shape[0]
    extended = jnp.concatenate([border, inputs], axis=0)
    picks = onehot.astype(jnp.bfloat16)
    cached_rows = [
        jnp.dot(picks, cache[:, slot, :], preferred_element_type=jnp.float32)
        for slot in range(taps - 1)
    ]
    result = weight[0][None, :] * inputs.astype(jnp.float32)
    for lag in range(1, taps):
        shifted = extended[taps - 1 - lag : taps - 1 - lag + length].astype(jnp.float32)
        slot_index = taps - 1 + position - lag
        fallback = jnp.zeros_like(shifted)
        for slot in range(taps - 1):
            fallback = jnp.where((slot_index == slot)[:, None], cached_rows[slot], fallback)
        shifted = jnp.where((position >= lag)[:, None], shifted, fallback)
        result = result + weight[lag][None, :] * shifted
    return jax.nn.silu(result).astype(jnp.bfloat16)


def per_device(
    residual,
    x_in,
    z_in,
    bc_in,
    dt_in,
    conv_x_weight,
    conv_bc_weight,
    conv_x_cache,
    conv_bc_cache,
    ssm_cache,
    dt_bias,
    a_log,
    d_skip,
    norm_gain,
    out_weight,
    attn_gain,
    q_weight,
    q_down,
    q_up,
    cache_keys,
    cache_values,
    new_keys,
    new_values,
    lengths,
):
    high_precision = lax.Precision.HIGH
    length = x_in.shape[0]
    taps = conv_x_weight.shape[0]
    seq_index = lax.axis_index("seq")
    seq_count = lax.axis_size("seq")
    reach = seq_count // 4 + 1
    first = seq_index * length
    long_hop = reach + 1
    tied_steps = 5
    behind_pieces = [jnp.stack([cache_keys, cache_values, new_keys, new_values])] * (reach + 1)
    forward_pieces = [jnp.stack([cache_keys, cache_values])] * (reach + 1)
    relay_steps = []
    for distance in range(1, long_hop):
        relay_steps.append([(distance, distance - 1, 1)])
    for distance in range(long_hop, reach + 1):
        relay_steps[distance - long_hop].append((distance, distance - long_hop, long_hop))

    def advance(values, tied=True, after=None):
        if not relay_steps or (tied and len(relay_steps) <= reach - tied_steps):
            return values
        moves = relay_steps.pop(0)
        sent = []
        for distance, source, steps in moves:
            behind, forward = behind_pieces[source], forward_pieces[source]
            if after is not None:
                behind, forward, _ = lax.optimization_barrier((behind, forward, after))
            sent.append((shifted_2(behind, "seq", steps), shifted_2(forward, "seq", -steps)))
        sent, values = lax.optimization_barrier((sent, values))
        for (distance, _, _), (behind, forward) in zip(moves, sent):
            behind_pieces[distance] = behind
            forward_pieces[distance] = forward
        return values

    local_index = first + jnp.arange(length, dtype=jnp.int32)
    segment, begin, valid, onehot = locate(lengths, local_index)
    position = local_index - begin
    x_border, bc_border = shifted_2(
        (x_in[length - taps + 1 :], bc_in[length - taps + 1 :]), "seq", 1
    )
    x_conv = convolve(x_in, x_border, conv_x_cache, conv_x_weight, position, onehot)
    bc_conv = convolve(bc_in, bc_border, conv_bc_cache, conv_bc_weight, position, onehot)
    x_conv, bc_conv = advance((x_conv, bc_conv))
    heads = dt_bias.shape[0]
    state_size = bc_in.shape[1] // 2
    head_size = x_in.shape[1] // heads
    prompts = lengths.shape[0]
    values_bf = x_conv.reshape(length, heads, head_size)
    values = x_conv.astype(jnp.float32).reshape(length, heads, head_size)
    inputs_b = bc_conv[:, :state_size]
    inputs_c = bc_conv[:, state_size:]
    step = jax.nn.softplus(dt_in + dt_bias[None, :])
    log_decay = -step * jnp.exp(a_log)[None, :]
    cumulative = jnp.cumsum(log_decay, axis=0)
    local_begin = jnp.maximum(begin - first, 0)
    before = jnp.take(cumulative - log_decay, local_begin, axis=0)
    from_begin = jnp.exp(cumulative - before)
    block = min(length, 512)
    pair_scores = jnp.dot(inputs_c, inputs_b.T, preferred_element_type=jnp.float32)
    cumulative_t = cumulative.T
    step_t = step.T
    order = jnp.arange(length, dtype=jnp.int32)

    def intra(block_start):
        query_rows = block_start + jnp.arange(block, dtype=jnp.int32)
        same = (segment[:, None] == segment[None, :]) & (query_rows[:, None] >= order[None, :])
        gap = cumulative_t[:, :, None] - cumulative_t[:, None, :]
        factor = jnp.where(same[None], jnp.exp(jnp.where(same[None], gap, 0.0)), 0.0)
        weights = factor * step_t[:, None, :] * pair_scores[None, :, :]
        return jnp.einsum(
            "hqs,shd->qhd",
            weights,
            values_bf,
            precision=high_precision,
            preferred_element_type=jnp.float32,
        )

    intra_out = lax.map(intra, jnp.arange(length // block, dtype=jnp.int32) * block).reshape(
        length, heads, head_size
    )
    last_segment = segment[length - 1]
    in_last = segment == last_segment
    tail_weight = (
        jnp.where(in_last[:, None], jnp.exp(cumulative[length - 1][None, :] - cumulative), 0.0)
        * step
    )
    weighted = tail_weight[:, :, None] * values
    local_state = jnp.einsum(
        "thd,tn->hdn",
        weighted,
        inputs_b,
        precision=high_precision,
        preferred_element_type=jnp.float32,
    )
    whole_decay = jnp.exp(cumulative[length - 1] - before[length - 1])
    starts_here = begin[length - 1] >= first
    cached_last = lax.dynamic_index_in_dim(ssm_cache, last_segment, 0, keepdims=False)
    chain_state = local_state + jnp.where(
        starts_here, whole_decay[:, None, None] * cached_last, 0.0
    )
    chain_decay = jnp.where(starts_here, jnp.zeros_like(whole_decay), whole_decay)

    scan_decay, scan_state = advance((chain_decay, chain_state))
    distance = 1
    while distance <= reach and distance < seq_count:
        prior_decay, prior_state = shifted_2((scan_decay, scan_state), "seq", distance)
        scan_state = scan_decay[:, None, None] * prior_state + scan_state
        scan_decay = scan_decay * prior_decay
        scan_decay, scan_state = advance((scan_decay, scan_state))
        distance *= 2
    carried = advance(shifted_2(scan_state, "seq", 1))
    continuing = position[0] > 0
    replace = (jnp.arange(prompts, dtype=jnp.int32) == segment[0]) & continuing
    initial = jnp.where(replace[:, None, None, None], carried[None], ssm_cache)
    selected = (onehot[:, :, None].astype(jnp.bfloat16) * inputs_c[:, None, :]).reshape(
        length, prompts * state_size
    )
    table = jnp.transpose(initial, (0, 3, 1, 2)).reshape(prompts * state_size, heads * head_size)
    init_out = (
        jnp.dot(
            selected, table, precision=high_precision, preferred_element_type=jnp.float32
        ).reshape(length, heads, head_size)
        * from_begin[:, :, None]
    )
    mixed = intra_out + init_out + d_skip[None, :, None] * values
    gated = (
        mixed * jax.nn.silu(z_in.astype(jnp.float32).reshape(length, heads, head_size))
    ).reshape(length, heads * head_size)
    gated = advance(gated)
    squares = lax.psum(jnp.sum(gated * gated, axis=1), "tp")
    width = gated.shape[1] * lax.axis_size("tp")
    normed = (gated * lax.rsqrt(squares / width + EPS)[:, None] * norm_gain[None, :]).astype(
        jnp.bfloat16
    )
    normed = advance(normed)
    summed = lax.psum_scatter(
        jnp.dot(normed, out_weight, preferred_element_type=jnp.float32),
        "tp",
        scatter_dimension=0,
        tiled=True,
    )
    hidden = (residual.astype(jnp.float32) + summed).astype(jnp.bfloat16)
    level = hidden.astype(jnp.float32)
    attn_in = (
        level * lax.rsqrt(jnp.mean(level * level, axis=1, keepdims=True) + EPS) * attn_gain[None, :]
    ).astype(jnp.bfloat16)
    piece = lax.all_gather(attn_in, "tp", axis=0, tiled=True)
    low = jnp.dot(piece, q_down, preferred_element_type=jnp.float32).astype(jnp.bfloat16)
    query = (
        jnp.dot(piece, q_weight, preferred_element_type=jnp.float32)
        + jnp.dot(low, q_up, preferred_element_type=jnp.float32)
    ).astype(jnp.bfloat16)
    count_heads = query.shape[1] // HA

    def piece_mask(query_index, query_segment, offset, causal):
        key_index = (seq_index + offset) * length + jnp.arange(length, dtype=jnp.int32)
        key_segment, _, key_valid, _ = locate(lengths, key_index)
        allowed = key_valid[None, :] & (key_segment[None, :] == query_segment[:, None])
        if causal:
            allowed = allowed & (key_index[None, :] <= query_index[:, None])
        return allowed

    cache_pieces = [(cache_keys, cache_values, 0)]
    new_pieces = [(new_keys, new_values, 0)]
    while relay_steps:
        advance((), tied=False, after=attn_in if len(relay_steps) <= 1 else None)
    for distance in range(1, reach + 1):
        behind = behind_pieces[distance]
        cache_pieces.append((behind[0], behind[1], -distance))
        new_pieces.append((behind[2], behind[3], -distance))
        forward = forward_pieces[distance]
        cache_pieces.append((forward[0], forward[1], distance))
    all_keys = jnp.concatenate(
        [entry[0] for entry in cache_pieces] + [entry[0] for entry in new_pieces], axis=0
    )
    all_values = jnp.concatenate(
        [entry[1] for entry in cache_pieces] + [entry[1] for entry in new_pieces], axis=0
    )
    mask = jnp.concatenate(
        [piece_mask(local_index, segment, entry[2], False) for entry in cache_pieces]
        + [piece_mask(local_index, segment, entry[2], True) for entry in new_pieces],
        axis=1,
    )
    scale = 1.0 / HA**0.5

    def attend(head):
        column = head * HA
        query_head = lax.dynamic_slice_in_dim(query, column, HA, 1)
        key_head = lax.dynamic_slice_in_dim(all_keys, column, HA, 1)
        value_head = lax.dynamic_slice_in_dim(all_values, column, HA, 1)
        scores = (
            lax.dot_general(
                query_head, key_head, (((1,), (1,)), ((), ())), preferred_element_type=jnp.float32
            )
            * scale
        )
        scores = jnp.where(mask, scores, NEG)
        top = jnp.max(scores, axis=1, keepdims=True)
        weights = jnp.exp(scores - top)
        probs = (weights / jnp.sum(weights, axis=1, keepdims=True)).astype(jnp.bfloat16)
        return jnp.dot(probs, value_head, preferred_element_type=jnp.float32).astype(jnp.bfloat16)

    per_head = lax.map(attend, jnp.arange(count_heads, dtype=jnp.int32))
    attended = jnp.transpose(per_head, (1, 0, 2)).reshape(length, count_heads * HA)
    return (hidden, attended)


def solution(mesh):
    in_specs = (
        P(("seq", "tp"), None),
        P("seq", "tp"),
        P("seq", "tp"),
        P("seq", None),
        P("seq", "tp"),
        P(None, "tp"),
        P(),
        P(None, None, "tp"),
        P(),
        P(None, "tp", None, None),
        P("tp"),
        P("tp"),
        P("tp"),
        P("tp"),
        P("tp", None),
        P(),
        P(None, "tp"),
        P(),
        P(None, "tp"),
        P("seq", "tp"),
        P("seq", "tp"),
        P("seq", "tp"),
        P("seq", "tp"),
        P(),
    )
    out_specs = (P(("seq", "tp"), None), P("seq", "tp"))
    return jax.shard_map(
        per_device, mesh=mesh, in_specs=in_specs, out_specs=out_specs, check_vma=False
    )
```
